32 devices in a mesh: gx: 2 (over core), gy: 2 (over x), gz: 8 (over z, y).
Axes of the slice: x: 2, y: 2, z: 4, core: 2. Of those that a mesh axis runs over, the one named last changes fastest.
Arguments:
- phase_field: float32 [256, 128, 256], P('gz', 'gx', 'gy'), may hold values from -3 to 3
- centres: float32 [4], replicated, may hold values from -0.8 to 0.8
- widths: float32 [4], replicated, may hold values from 0.15 to 0.5
- densities: float32 [4], replicated, may hold values from 0.5 to 3
- colours: float32 [3, 4], replicated, may hold values from 0 to 1
Outputs:
- picture: float32 [4, 128, 256], P(None, ('gx', 'gz'), 'gy')
The draws below stay inside these ranges and needn't reach their ends.
All inputs are finite; a program needn't handle non-finite values.
Results may differ from the reference program's by a relative error of at most 0.0003.
Values sent between devices are 32-bit elements; how exact they have to be, the bound alone decides.
No kernel may reach another device: no remote copies, remote signals or barrier semaphores. Data moves between devices by JAX's collectives and lax.ppermute only.
A program may use at most 64 MiB of HBM per device.

```python
import math
import jax
import jax.numpy as jnp
from jax import lax

STEPS = 4
MATERIALS = 4
NX = 128
NY = 256
NZ = 256


def steps_of(stream_key, dims, split, least, largest):
    loudness = 1.0
    for dim, parts in split:
        steps = jax.random.uniform(jax.random.fold_in(jax.random.fold_in(stream_key, 6), dim), (parts,), jnp.float32, least / len(split), largest / len(split))
        loudness = loudness * jnp.repeat(jnp.exp(steps), dims[dim] // parts).reshape((-1,) + (1,) * (len(dims) - 1 - dim))
    return loudness


def bell_draw(own_key, extent, spread, most, pieces=(), kind=jnp.bfloat16):
    array = spread * jax.random.normal(own_key, extent, jnp.float32)
    if pieces:
        array = array * steps_of(own_key, extent, pieces, -0.22, 0.18)
    return jnp.clip(array, -most, most).astype(kind)


def setup_inputs(seed: int = 0) -> dict:
    key_list = jax.random.split(jax.random.key(seed), 6)
    phase_field = bell_draw(key_list[0], (NZ, NX, NY), 0.6, 3.0, ((0, 8), (1, 2), (2, 2)), jnp.float32)
    centres = jnp.clip(jax.random.uniform(key_list[1], (MATERIALS,), jnp.float32, -0.8, 0.8), -0.8, 0.8)
    widths = jnp.clip(jnp.exp(jax.random.uniform(key_list[2], (MATERIALS,), jnp.float32, math.log(0.15), math.log(0.5))), 0.15, 0.5)
    densities = jnp.clip(jnp.exp(jax.random.uniform(key_list[3], (MATERIALS,), jnp.float32, math.log(0.5), math.log(3.0))), 0.5, 3.0)
    colours = jnp.clip(jax.random.uniform(key_list[4], (3, MATERIALS), jnp.float32, 0.0, 1.0), 0.0, 1.0)
    return dict(phase_field=phase_field, centres=centres, widths=widths, densities=densities, colours=colours)


KAPPA = 0.5
RATE_DEPTH = 0.3
RATE_PLANE = 0.09


def neighbour_flux(padded, centre, dim_index, shift_by, weight):
    selector = [slice(1, -1), slice(1, -1), slice(1, -1)]
    selector[dim_index] = slice(shift_by, padded.shape[dim_index] - 2 + shift_by)
    differ = padded[tuple(selector)] - centre
    return weight * differ / (1.0 + (differ / KAPPA) ** 2)


def smooth_valid(padded):
    centre = padded[1:-1, 1:-1, 1:-1]
    updated = centre
    for dim_index, weight in ((0, RATE_DEPTH), (1, RATE_PLANE), (2, RATE_PLANE)):
        for shift_by in (0, 2):
            updated = updated + neighbour_flux(padded, centre, dim_index, shift_by, weight)
    return updated


def optics(values, centres, widths, densities, colours):
    bump_list = [densities[material] * jnp.exp(-((values - centres[material]) / widths[material]) ** 2) for material in range(MATERIALS)]
    extinct = sum(bump_list)
    emitted = jnp.stack([sum(colours[channel, material] * bump_list[material] for material in range(MATERIALS)) for channel in range(3)])
    return extinct, emitted


def render_column(column, centres, widths, densities, colours):
    extinct, emitted = optics(column, centres, widths, densities, colours)
    step_len = 1.0 / NZ
    running = jnp.cumsum(extinct, axis=0) - extinct
    through = jnp.exp(-step_len * running)
    radiance = step_len * jnp.sum(through[None] * emitted, axis=1)
    alpha_out = 1.0 - jnp.exp(-step_len * jnp.sum(extinct, axis=0))
    return jnp.concatenate([radiance, alpha_out[None]], axis=0)


def reference(phase_field, centres, widths, densities, colours):
    smoothed = phase_field
    for repeat in range(STEPS):
        smoothed = smooth_valid(jnp.pad(smoothed, 1))
    columns = jnp.moveaxis(smoothed, 1, 0)
    picture = lax.map(lambda column: render_column(column, centres, widths, densities, colours), columns)
    return jnp.moveaxis(picture, 1, 0)
```

```python
import functools

import jax
import jax.numpy as jnp
from jax import lax
from jax.experimental import pallas as pl
from jax.experimental.pallas import tpu as pltpu
from jax.sharding import PartitionSpec as P

STEPS = 4
MATERIALS = 4
CHANNELS = 3

KAPPA = 0.5
RATE_DEPTH = 0.3
RATE_PLANE = 0.09
LANES = 256


def with_halo(x, sides, width):
    for axis, dim in sides:
        size, length = (lax.axis_size(axis), x.shape[dim])
        up = [(i, (i + 1) % size) for i in range(size - 1)]
        down = [(j, i) for i, j in up]
        last = lax.slice_in_dim(x, length - width, length, axis=dim)
        first = lax.slice_in_dim(x, 0, width, axis=dim)
        before = lax.ppermute(last, axis, up)
        after = lax.ppermute(first, axis, down)
        pieces = [before, x, after]
        if dim == 2:
            fill = list(x.shape)
            fill[2] = LANES - length - 2 * width
            pieces.append(jnp.zeros(fill, x.dtype))
        x = jnp.concatenate(pieces, axis=dim)
    return x


def flux(d, rate):
    q = d * (1.0 / KAPPA)
    return rate * d / (1.0 + q * q)


def render_kernel(lim_ref, prm_ref, x_ref, out_ref, a_ref, b_ref, m_ref, *, interior, h):
    depth, rows, lanes = x_ref.shape
    d_in, r_in, l_in = interior
    halo = STEPS

    row = lax.broadcasted_iota(jnp.int32, (rows, lanes), 0)
    lane = lax.broadcasted_iota(jnp.int32, (rows, lanes), 1)
    ok = (row >= lim_ref[2]) & (row < lim_ref[3]) & (lane >= lim_ref[4]) & (lane < lim_ref[5])
    m_ref[...] = jnp.where(ok, 1.0, 0.0).astype(jnp.float32)

    def plane_update(src, z, g_prev):
        c = src[z]
        g = flux(src[z + 1] - c, RATE_DEPTH)
        fr = flux(pltpu.roll(c, rows - 1, 0) - c, RATE_PLANE)
        fc = flux(pltpu.roll(c, lanes - 1, 1) - c, RATE_PLANE)
        new = c + (g - g_prev) + (fr - pltpu.roll(fr, 1, 0)) + (fc - pltpu.roll(fc, 1, 1))
        return new, g

    def smooth(src, dst, s):
        z0, z1 = s + 1, depth - 1 - s
        g0 = flux(src[z0] - src[z0 - 1], RATE_DEPTH)

        def body(z, g_prev):
            new, g = plane_update(src, z, g_prev)
            inside = (z >= lim_ref[0]) & (z < lim_ref[1])
            zf = jnp.where(inside, 1.0, 0.0).astype(jnp.float32)
            dst[z] = new * (m_ref[...] * zf)
            return g

        lax.fori_loop(z0, z1, body, g0)

    smooth(x_ref, a_ref, 0)
    smooth(a_ref, b_ref, 1)
    smooth(b_ref, a_ref, 2)

    cen = [prm_ref[k] for k in range(MATERIALS)]
    wid = [prm_ref[MATERIALS + k] for k in range(MATERIALS)]
    den = [prm_ref[2 * MATERIALS + k] for k in range(MATERIALS)]
    col = [[prm_ref[3 * MATERIALS + ch * MATERIALS + k] for k in range(MATERIALS)] for ch in range(CHANNELS)]

    for ch in range(CHANNELS + 1):
        out_ref[ch] = jnp.zeros((r_in, l_in), jnp.float32)

    z0, z1 = halo, halo + d_in
    g0 = flux(a_ref[z0] - a_ref[z0 - 1], RATE_DEPTH)

    def final(z, g_prev):
        new, g = plane_update(a_ref, z, g_prev)
        v = pltpu.roll(pltpu.roll(new, rows - halo, 0), lanes - halo, 1)[:r_in, :l_in]
        bumps = [den[k] * jnp.exp(-(((v - cen[k]) / wid[k]) ** 2)) for k in range(MATERIALS)]
        ext = bumps[0] + bumps[1] + bumps[2] + bumps[3]
        run = out_ref[CHANNELS]
        through = jnp.exp(-h * run)
        for ch in range(CHANNELS):
            emit = col[ch][0] * bumps[0] + col[ch][1] * bumps[1] + col[ch][2] * bumps[2] + col[ch][3] * bumps[3]
            out_ref[ch] = out_ref[ch] + through * emit
        out_ref[CHANNELS] = run + ext
        return g

    lax.fori_loop(z0, z1, final, g0)
    for ch in range(CHANNELS):
        out_ref[ch] = h * out_ref[ch]


def render_block(padded, lim, prm, interior, h):
    depth, rows, lanes = padded.shape
    d_in, r_in, l_in = interior
    cells = depth * rows * lanes
    kernel = functools.partial(render_kernel, interior=interior, h=h)
    return pl.pallas_call(
        kernel,
        out_shape=jax.ShapeDtypeStruct((CHANNELS + 1, r_in, l_in), jnp.float32),
        in_specs=[
            pl.BlockSpec(memory_space=pltpu.SMEM),
            pl.BlockSpec(memory_space=pltpu.SMEM),
            pl.BlockSpec(memory_space=pltpu.VMEM),
        ],
        out_specs=pl.BlockSpec(memory_space=pltpu.VMEM),
        scratch_shapes=[
            pltpu.VMEM((depth, rows, lanes), jnp.float32),
            pltpu.VMEM((depth, rows, lanes), jnp.float32),
            pltpu.VMEM((rows, lanes), jnp.float32),
        ],
        compiler_params=pltpu.CompilerParams(vmem_limit_bytes=48 * 1024 * 1024),
        cost_estimate=pl.CostEstimate(
            flops=int(cells * STEPS * 40 + d_in * r_in * l_in * 60),
            transcendentals=int(d_in * r_in * l_in * (MATERIALS + 1)),
            bytes_accessed=int(cells * 4 + (CHANNELS + 1) * r_in * l_in * 4),
        ),
    )(lim, prm, padded)


def shards(phase_field, centres, widths, densities, colours):
    depth_cells, row_cells, col_cells = phase_field.shape
    groups = lax.axis_size("gz")
    h = 1.0 / (depth_cells * groups)
    padded = with_halo(phase_field, (("gx", 1), ("gy", 2), ("gz", 0)), STEPS)

    z_lo = STEPS - lax.axis_index("gz") * depth_cells
    r_lo = STEPS - lax.axis_index("gx") * row_cells
    c_lo = STEPS - lax.axis_index("gy") * col_cells
    lim = jnp.stack(
        [
            z_lo,
            z_lo + depth_cells * groups,
            r_lo,
            r_lo + row_cells * lax.axis_size("gx"),
            c_lo,
            c_lo + col_cells * lax.axis_size("gy"),
        ]
    ).astype(jnp.int32)
    prm = jnp.concatenate([centres, widths, densities, colours.reshape(-1)]).astype(jnp.float32)

    seg = render_block(padded, lim, prm, (depth_cells, row_cells, col_cells), h)

    rows_part = row_cells // groups
    parts = seg.reshape(CHANNELS + 1, groups, rows_part, col_cells)
    got = lax.all_to_all(parts, "gz", 1, 1, tiled=True)
    prefix = jnp.zeros((rows_part, col_cells), jnp.float32)
    rad = jnp.zeros((CHANNELS, rows_part, col_cells), jnp.float32)
    for g in range(groups):
        rad = rad + jnp.exp(-h * prefix)[None] * got[:CHANNELS, g]
        prefix = prefix + got[CHANNELS, g]
    alpha = 1.0 - jnp.exp(-h * prefix)
    return jnp.concatenate([rad, alpha[None]], axis=0)


def solution(mesh):
    placed = (P("gz", "gx", "gy"), P(), P(), P(), P())
    return jax.shard_map(
        shards, mesh=mesh, in_specs=placed, out_specs=P(None, ("gx", "gz"), "gy"), check_vma=False
    )
```

```python
import functools
import itertools

import jax
import jax.numpy as jnp
from jax import lax
from jax.experimental import pallas as pl
from jax.experimental.pallas import tpu as pltpu
from jax.sharding import PartitionSpec as P

STEPS = 4
MATERIALS = 4
CHANNELS = 3

KAPPA = 0.5
RATE_DEPTH = 0.3
RATE_PLANE = 0.09
LANES = 256


def pick(cond, a, b):
    if isinstance(cond, bool):
        return a if cond else b
    return jnp.where(cond, a, b)


def axis_moves(axis):
    n = lax.axis_size(axis)
    if n == 1:
        return []
    if n == 2:
        me = lax.axis_index(axis)
        return [([(0, 1), (1, 0)], me == 0, me == 1)]
    up = [(i, i + 1) for i in range(n - 1)]
    down = [(i + 1, i) for i in range(n - 1)]
    return [(up, True, True), (down, False, False)]


def halo_stage(x, dim_axes, width):
    dims = [d for d, _ in dim_axes]
    axes = [a for _, a in dim_axes]
    sizes = [lax.axis_size(a) for a in axes]
    options = [[None] + axis_moves(a) for a in axes]
    blocks = {}
    for combo in itertools.product(*options):
        if all(m is None for m in combo):
            continue
        piece = x
        for d, m in zip(dims, combo):
            if m is not None:
                n_d = piece.shape[d]
                lo = lax.slice_in_dim(piece, 0, width, axis=d)
                hi = lax.slice_in_dim(piece, n_d - width, n_d, axis=d)
                piece = pick(m[1], hi, lo)
        used = [(a, s, m) for a, s, m in zip(axes, sizes, combo) if m is not None]
        pairs = []
        for parts in itertools.product(*[m[0] for _, _, m in used]):
            src = dst = 0
            for (_, s, _), (p, q) in zip(used, parts):
                src, dst = src * s + p, dst * s + q
            pairs.append((src, dst))
        got = lax.ppermute(piece, tuple(a for a, _, _ in used), pairs)
        landing = [(d, m[2]) for d, m in zip(dims, combo) if m is not None]
        for sides in itertools.product(("lo", "hi"), repeat=len(landing)):
            cond = True
            for (d, land_lo), side in zip(landing, sides):
                this = land_lo if side == "lo" else (not land_lo if isinstance(land_lo, bool) else ~land_lo)
                if isinstance(cond, bool) and isinstance(this, bool):
                    cond = cond and this
                elif isinstance(cond, bool):
                    cond = this if cond else False
                elif isinstance(this, bool):
                    cond = cond if this else False
                else:
                    cond = cond & this
            if cond is False:
                continue
            key = [None] * len(dims)
            for (d, _), side in zip(landing, sides):
                key[dims.index(d)] = side
            key = tuple(k or "mid" for k in key)
            val = got if cond is True else jnp.where(cond, got, 0.0)
            blocks[key] = val if key not in blocks else blocks[key] + val
    blocks[tuple("mid" for _ in dims)] = x

    def block_shape(key):
        shape = list(x.shape)
        for d, k in zip(dims, key):
            if k != "mid":
                shape[d] = width
        return shape

    def assemble(prefix):
        level = len(prefix)
        if level == len(dims):
            key = tuple(prefix)
            if key in blocks:
                return blocks[key]
            return jnp.zeros(block_shape(key), x.dtype)
        parts = [assemble(prefix + [k]) for k in ("lo", "mid", "hi")]
        return jnp.concatenate(parts, axis=dims[level])

    return assemble([])


def flux(d, rate):
    q = d * (1.0 / KAPPA)
    return rate * d / (1.0 + q * q)


def render_kernel(lim_ref, prm_ref, x_ref, out_ref, a_ref, b_ref, m_ref, *, interior, h):
    depth, rows, lanes = x_ref.shape
    d_in, r_in, l_in = interior
    halo = STEPS

    row = lax.broadcasted_iota(jnp.int32, (rows, lanes), 0)
    lane = lax.broadcasted_iota(jnp.int32, (rows, lanes), 1)
    ok = (row >= lim_ref[2]) & (row < lim_ref[3]) & (lane >= lim_ref[4]) & (lane < lim_ref[5])
    m_ref[...] = jnp.where(ok, 1.0, 0.0).astype(jnp.float32)

    def plane_update(src, z, g_prev):
        c = src[z]
        g = flux(src[z + 1] - c, RATE_DEPTH)
        fr = flux(pltpu.roll(c, rows - 1, 0) - c, RATE_PLANE)
        fc = flux(pltpu.roll(c, lanes - 1, 1) - c, RATE_PLANE)
        new = c + (g - g_prev) + (fr - pltpu.roll(fr, 1, 0)) + (fc - pltpu.roll(fc, 1, 1))
        return new, g

    def smooth(src, dst, s):
        z0, z1 = s + 1, depth - 1 - s
        g0 = flux(src[z0] - src[z0 - 1], RATE_DEPTH)

        def body(z, g_prev):
            new, g = plane_update(src, z, g_prev)
            inside = (z >= lim_ref[0]) & (z < lim_ref[1])
            zf = jnp.where(inside, 1.0, 0.0).astype(jnp.float32)
            dst[z] = new * (m_ref[...] * zf)
            return g

        lax.fori_loop(z0, z1, body, g0)

    smooth(x_ref, a_ref, 0)
    smooth(a_ref, b_ref, 1)
    smooth(b_ref, a_ref, 2)

    cen = [prm_ref[k] for k in range(MATERIALS)]
    wid = [prm_ref[MATERIALS + k] for k in range(MATERIALS)]
    den = [prm_ref[2 * MATERIALS + k] for k in range(MATERIALS)]
    col = [[prm_ref[3 * MATERIALS + ch * MATERIALS + k] for k in range(MATERIALS)] for ch in range(CHANNELS)]

    for ch in range(CHANNELS + 1):
        out_ref[ch] = jnp.zeros((r_in, l_in), jnp.float32)

    z0, z1 = halo, halo + d_in
    g0 = flux(a_ref[z0] - a_ref[z0 - 1], RATE_DEPTH)

    def final(z, g_prev):
        new, g = plane_update(a_ref, z, g_prev)
        v = pltpu.roll(pltpu.roll(new, rows - halo, 0), lanes - halo, 1)[:r_in, :l_in]
        bumps = [den[k] * jnp.exp(-(((v - cen[k]) / wid[k]) ** 2)) for k in range(MATERIALS)]
        ext = bumps[0] + bumps[1] + bumps[2] + bumps[3]
        run = out_ref[CHANNELS]
        through = jnp.exp(-h * run)
        for ch in range(CHANNELS):
            emit = col[ch][0] * bumps[0] + col[ch][1] * bumps[1] + col[ch][2] * bumps[2] + col[ch][3] * bumps[3]
            out_ref[ch] = out_ref[ch] + through * emit
        out_ref[CHANNELS] = run + ext
        return g

    lax.fori_loop(z0, z1, final, g0)
    for ch in range(CHANNELS):
        out_ref[ch] = h * out_ref[ch]


def render_block(padded, lim, prm, interior, h):
    depth, rows, lanes = padded.shape
    d_in, r_in, l_in = interior
    cells = depth * rows * lanes
    kernel = functools.partial(render_kernel, interior=interior, h=h)
    return pl.pallas_call(
        kernel,
        out_shape=jax.ShapeDtypeStruct((CHANNELS + 1, r_in, l_in), jnp.float32),
        in_specs=[
            pl.BlockSpec(memory_space=pltpu.SMEM),
            pl.BlockSpec(memory_space=pltpu.SMEM),
            pl.BlockSpec(memory_space=pltpu.VMEM),
        ],
        out_specs=pl.BlockSpec(memory_space=pltpu.VMEM),
        scratch_shapes=[
            pltpu.VMEM((depth, rows, lanes), jnp.float32),
            pltpu.VMEM((depth, rows, lanes), jnp.float32),
            pltpu.VMEM((rows, lanes), jnp.float32),
        ],
        compiler_params=pltpu.CompilerParams(vmem_limit_bytes=48 * 1024 * 1024),
        cost_estimate=pl.CostEstimate(
            flops=int(cells * STEPS * 40 + d_in * r_in * l_in * 60),
            transcendentals=int(d_in * r_in * l_in * (MATERIALS + 1)),
            bytes_accessed=int(cells * 4 + (CHANNELS + 1) * r_in * l_in * 4),
        ),
    )(lim, prm, padded)


def shards(phase_field, centres, widths, densities, colours):
    depth_cells, row_cells, col_cells = phase_field.shape
    groups = lax.axis_size("gz")
    h = 1.0 / (depth_cells * groups)
    padded = halo_stage(phase_field, ((0, "gz"),), STEPS)
    padded = halo_stage(padded, ((1, "gx"), (2, "gy")), STEPS)
    fill = (padded.shape[0], padded.shape[1], LANES - padded.shape[2])
    padded = jnp.concatenate([padded, jnp.zeros(fill, padded.dtype)], axis=2)

    z_lo = STEPS - lax.axis_index("gz") * depth_cells
    r_lo = STEPS - lax.axis_index("gx") * row_cells
    c_lo = STEPS - lax.axis_index("gy") * col_cells
    lim = jnp.stack(
        [
            z_lo,
            z_lo + depth_cells * groups,
            r_lo,
            r_lo + row_cells * lax.axis_size("gx"),
            c_lo,
            c_lo + col_cells * lax.axis_size("gy"),
        ]
    ).astype(jnp.int32)
    prm = jnp.concatenate([centres, widths, densities, colours.reshape(-1)]).astype(jnp.float32)

    seg = render_block(padded, lim, prm, (depth_cells, row_cells, col_cells), h)

    rows_part = row_cells // groups
    parts = seg.reshape(CHANNELS + 1, groups, rows_part, col_cells)
    got = lax.all_to_all(parts, "gz", 1, 1, tiled=True)
    prefix = jnp.zeros((rows_part, col_cells), jnp.float32)
    rad = jnp.zeros((CHANNELS, rows_part, col_cells), jnp.float32)
    for g in range(groups):
        rad = rad + jnp.exp(-h * prefix)[None] * got[:CHANNELS, g]
        prefix = prefix + got[CHANNELS, g]
    alpha = 1.0 - jnp.exp(-h * prefix)
    return jnp.concatenate([rad, alpha[None]], axis=0)


def solution(mesh):
    placed = (P("gz", "gx", "gy"), P(), P(), P(), P())
    return jax.shard_map(
        shards, mesh=mesh, in_specs=placed, out_specs=P(None, ("gx", "gz"), "gy"), check_vma=False
    )
```

```python
import functools
import itertools

import jax
import jax.numpy as jnp
from jax import lax
from jax.experimental import pallas as pl
from jax.experimental.pallas import tpu as pltpu
from jax.sharding import PartitionSpec as P

STEPS = 4
MATERIALS = 4
CHANNELS = 3

KAPPA = 0.5
RATE_DEPTH = 0.3
RATE_PLANE = 0.09
LANES = 256


def pick(cond, a, b):
    if isinstance(cond, bool):
        return a if cond else b
    return jnp.where(cond, a, b)


def axis_moves(axis):
    n = lax.axis_size(axis)
    if n == 1:
        return []
    if n == 2:
        me = lax.axis_index(axis)
        return [([(0, 1), (1, 0)], me == 0, me == 1)]
    up = [(i, i + 1) for i in range(n - 1)]
    down = [(i + 1, i) for i in range(n - 1)]
    return [(up, True, True), (down, False, False)]


def halo_stage(x, dim_axes, width):
    dims = [d for d, _ in dim_axes]
    axes = [a for _, a in dim_axes]
    sizes = [lax.axis_size(a) for a in axes]
    options = [[None] + axis_moves(a) for a in axes]
    blocks = {}
    for combo in itertools.product(*options):
        if all(m is None for m in combo):
            continue
        piece = x
        for d, m in zip(dims, combo):
            if m is not None:
                n_d = piece.shape[d]
                lo = lax.slice_in_dim(piece, 0, width, axis=d)
                hi = lax.slice_in_dim(piece, n_d - width, n_d, axis=d)
                piece = pick(m[1], hi, lo)
        used = [(a, s, m) for a, s, m in zip(axes, sizes, combo) if m is not None]
        pairs = []
        for parts in itertools.product(*[m[0] for _, _, m in used]):
            src = dst = 0
            for (_, s, _), (p, q) in zip(used, parts):
                src, dst = src * s + p, dst * s + q
            pairs.append((src, dst))
        got = lax.ppermute(piece, tuple(a for a, _, _ in used), pairs)
        landing = [(d, m[2]) for d, m in zip(dims, combo) if m is not None]
        for sides in itertools.product(("lo", "hi"), repeat=len(landing)):
            cond = True
            for (d, land_lo), side in zip(landing, sides):
                this = land_lo if side == "lo" else (not land_lo if isinstance(land_lo, bool) else ~land_lo)
                if isinstance(cond, bool) and isinstance(this, bool):
                    cond = cond and this
                elif isinstance(cond, bool):
                    cond = this if cond else False
                elif isinstance(this, bool):
                    cond = cond if this else False
                else:
                    cond = cond & this
            if cond is False:
                continue
            key = [None] * len(dims)
            for (d, _), side in zip(landing, sides):
                key[dims.index(d)] = side
            key = tuple(k or "mid" for k in key)
            val = got if cond is True else jnp.where(cond, got, 0.0)
            blocks[key] = val if key not in blocks else blocks[key] + val
    blocks[tuple("mid" for _ in dims)] = x

    def block(*key):
        if key in blocks:
            return blocks[key]
        shape = list(x.shape)
        for d, k in zip(dims, key):
            if k != "mid":
                shape[d] = width
        return jnp.zeros(shape, x.dtype)

    return block


def flux(d, rate):
    q = d * (1.0 / KAPPA)
    return rate * d / (1.0 + q * q)


def render_kernel(lim_ref, prm_ref, x_hbm, zlo_hbm, zhi_hbm, rband_hbm, cband_hbm, out_ref, a_ref, b_ref, m_ref, sem,
                  *, interior, h):
    depth, rows, lanes = a_ref.shape
    d_in, r_in, l_in = interior
    halo = STEPS
    copies = [
        pltpu.make_async_copy(x_hbm, b_ref.at[halo:halo + d_in, 0:r_in, 0:l_in], sem.at[0]),
        pltpu.make_async_copy(zlo_hbm, b_ref.at[0:halo, 0:r_in, 0:l_in], sem.at[1]),
        pltpu.make_async_copy(zhi_hbm, b_ref.at[halo + d_in:depth, 0:r_in, 0:l_in], sem.at[2]),
        pltpu.make_async_copy(rband_hbm, b_ref.at[:, r_in:rows, 0:l_in], sem.at[3]),
        pltpu.make_async_copy(cband_hbm, b_ref.at[:, :, l_in:lanes], sem.at[4]),
    ]
    for cp in copies:
        cp.start()

    row = lax.broadcasted_iota(jnp.int32, (rows, lanes), 0)
    lane = lax.broadcasted_iota(jnp.int32, (rows, lanes), 1)
    row_at = jnp.where(row < r_in + halo, row, row - rows)
    lane_at = jnp.where(lane < (l_in + lanes) // 2, lane, lane - lanes)
    ok = (row_at >= lim_ref[2]) & (row_at < lim_ref[3]) & (lane_at >= lim_ref[4]) & (lane_at < lim_ref[5])
    m_ref[...] = jnp.where(ok, 1.0, 0.0).astype(jnp.float32)

    cen = [prm_ref[k] for k in range(MATERIALS)]
    wid = [prm_ref[MATERIALS + k] for k in range(MATERIALS)]
    den = [prm_ref[2 * MATERIALS + k] for k in range(MATERIALS)]
    col = [[prm_ref[3 * MATERIALS + ch * MATERIALS + k] for k in range(MATERIALS)] for ch in range(CHANNELS)]
    for ch in range(CHANNELS + 1):
        out_ref[ch] = jnp.zeros((r_in, l_in), jnp.float32)

    for cp in copies:
        cp.wait()

    def smooth(src, dst, s):
        z0, z1 = s + 1, depth - 1 - s
        g0 = flux(src[z0] - src[z0 - 1], RATE_DEPTH)

        def body(z, g_prev):
            c = src[z]
            g = flux(src[z + 1] - c, RATE_DEPTH)
            fr = flux(pltpu.roll(c, rows - 1, 0) - c, RATE_PLANE)
            fc = flux(pltpu.roll(c, lanes - 1, 1) - c, RATE_PLANE)
            new = c + (g - g_prev) + (fr - pltpu.roll(fr, 1, 0)) + (fc - pltpu.roll(fc, 1, 1))
            inside = (z >= lim_ref[0]) & (z < lim_ref[1])
            zf = jnp.where(inside, 1.0, 0.0).astype(jnp.float32)
            dst[z] = new * (m_ref[...] * zf)
            return g

        lax.fori_loop(z0, z1, body, g0)

    smooth(b_ref, a_ref, 0)
    smooth(a_ref, b_ref, 1)
    smooth(b_ref, a_ref, 2)

    z0, z1 = halo, halo + d_in
    g0 = flux(a_ref[z0, 0:r_in, 0:l_in] - a_ref[z0 - 1, 0:r_in, 0:l_in], RATE_DEPTH)

    def final(z, g_prev):
        ci = a_ref[z, 0:r_in, 0:l_in]
        g = flux(a_ref[z + 1, 0:r_in, 0:l_in] - ci, RATE_DEPTH)
        c0 = a_ref[z, :, 0:l_in]
        fr = flux(pltpu.roll(c0, rows - 1, 0) - c0, RATE_PLANE)
        cr = a_ref[z, 0:r_in, :]
        fc = flux(pltpu.roll(cr, lanes - 1, 1) - cr, RATE_PLANE)
        v = ci + (g - g_prev) + (fr - pltpu.roll(fr, 1, 0))[0:r_in] + (fc - pltpu.roll(fc, 1, 1))[:, 0:l_in]
        bumps = [den[k] * jnp.exp(-(((v - cen[k]) / wid[k]) ** 2)) for k in range(MATERIALS)]
        ext = bumps[0] + bumps[1] + bumps[2] + bumps[3]
        run = out_ref[CHANNELS]
        through = jnp.exp(-h * run)
        for ch in range(CHANNELS):
            emit = col[ch][0] * bumps[0] + col[ch][1] * bumps[1] + col[ch][2] * bumps[2] + col[ch][3] * bumps[3]
            out_ref[ch] = out_ref[ch] + through * emit
        out_ref[CHANNELS] = run + ext
        return g

    lax.fori_loop(z0, z1, final, g0)
    for ch in range(CHANNELS):
        out_ref[ch] = h * out_ref[ch]


def render_block(pieces, lim, prm, interior, h):
    d_in, r_in, l_in = interior
    depth, rows, lanes = d_in + 2 * STEPS, r_in + 2 * STEPS, LANES
    cells = depth * rows * lanes
    kernel = functools.partial(render_kernel, interior=interior, h=h)
    return pl.pallas_call(
        kernel,
        out_shape=jax.ShapeDtypeStruct((CHANNELS + 1, r_in, l_in), jnp.float32),
        in_specs=[pl.BlockSpec(memory_space=pltpu.SMEM)] * 2 + [pl.BlockSpec(memory_space=pl.ANY)] * 5,
        out_specs=pl.BlockSpec(memory_space=pltpu.VMEM),
        scratch_shapes=[
            pltpu.VMEM((depth, rows, lanes), jnp.float32),
            pltpu.VMEM((depth, rows, lanes), jnp.float32),
            pltpu.VMEM((rows, lanes), jnp.float32),
            pltpu.SemaphoreType.DMA((5,)),
        ],
        compiler_params=pltpu.CompilerParams(vmem_limit_bytes=48 * 1024 * 1024),
        cost_estimate=pl.CostEstimate(
            flops=int(cells * STEPS * 40 + d_in * r_in * l_in * 60),
            transcendentals=int(d_in * r_in * l_in * (MATERIALS + 1)),
            bytes_accessed=int(cells * 4 + (CHANNELS + 1) * r_in * l_in * 4),
        ),
    )(lim, prm, *pieces)


def shards(phase_field, centres, widths, densities, colours):
    depth_cells, row_cells, col_cells = phase_field.shape
    groups = lax.axis_size("gz")
    h = 1.0 / (depth_cells * groups)
    zblock = halo_stage(phase_field, ((0, "gz"),), STEPS)
    zlo, zhi = zblock("lo"), zblock("hi")
    deep = jnp.concatenate([zlo, phase_field, zhi], axis=0)
    plane = halo_stage(deep, ((1, "gx"), (2, "gy")), STEPS)
    rband = jnp.concatenate([plane("hi", "mid"), plane("lo", "mid")], axis=1)
    right = jnp.concatenate([plane("mid", "hi"), plane("hi", "hi"), plane("lo", "hi")], axis=1)
    left = jnp.concatenate([plane("mid", "lo"), plane("hi", "lo"), plane("lo", "lo")], axis=1)
    fill = jnp.zeros(right.shape[:2] + (LANES - col_cells - 2 * STEPS,), jnp.float32)
    cband = jnp.concatenate([right, fill, left], axis=2)

    z_lo = STEPS - lax.axis_index("gz") * depth_cells
    r_lo = -lax.axis_index("gx") * row_cells
    c_lo = -lax.axis_index("gy") * col_cells
    lim = jnp.stack(
        [
            z_lo,
            z_lo + depth_cells * groups,
            r_lo,
            r_lo + row_cells * lax.axis_size("gx"),
            c_lo,
            c_lo + col_cells * lax.axis_size("gy"),
        ]
    ).astype(jnp.int32)
    prm = jnp.concatenate([centres, widths, densities, colours.reshape(-1)]).astype(jnp.float32)

    seg = render_block((phase_field, zlo, zhi, rband, cband), lim, prm, (depth_cells, row_cells, col_cells), h)

    rows_part = row_cells // groups
    parts = seg.reshape(CHANNELS + 1, groups, rows_part, col_cells)
    got = lax.all_to_all(parts, "gz", 1, 1, tiled=True)
    prefix = jnp.zeros((rows_part, col_cells), jnp.float32)
    rad = jnp.zeros((CHANNELS, rows_part, col_cells), jnp.float32)
    for g in range(groups):
        rad = rad + jnp.exp(-h * prefix)[None] * got[:CHANNELS, g]
        prefix = prefix + got[CHANNELS, g]
    alpha = 1.0 - jnp.exp(-h * prefix)
    return jnp.concatenate([rad, alpha[None]], axis=0)


def solution(mesh):
    placed = (P("gz", "gx", "gy"), P(), P(), P(), P())
    return jax.shard_map(
        shards, mesh=mesh, in_specs=placed, out_specs=P(None, ("gx", "gz"), "gy"), check_vma=False
    )
```

```python
import functools
import itertools

import jax
import jax.numpy as jnp
from jax import lax
from jax.experimental import pallas as pl
from jax.experimental.pallas import tpu as pltpu
from jax.sharding import PartitionSpec as P

STEPS = 4
MATERIALS = 4
CHANNELS = 3

KAPPA = 0.5
RATE_DEPTH = 0.3
RATE_PLANE = 0.09
LANES = 256


def pick(cond, a, b):
    if isinstance(cond, bool):
        return a if cond else b
    return jnp.where(cond, a, b)


def axis_moves(axis):
    n = lax.axis_size(axis)
    if n == 1:
        return []
    if n == 2:
        me = lax.axis_index(axis)
        return [([(0, 1), (1, 0)], me == 0, me == 1)]
    up = [(i, i + 1) for i in range(n - 1)]
    down = [(i + 1, i) for i in range(n - 1)]
    return [(up, True, True), (down, False, False)]


def halo_stage(x, dim_axes, width, order):
    dims = [d for d, _ in dim_axes]
    axes = [a for _, a in dim_axes]
    sizes = [lax.axis_size(a) for a in axes]
    options = [[None] + axis_moves(a) for a in axes]
    blocks = {}
    for combo in itertools.product(*options):
        if all(m is None for m in combo):
            continue
        piece = x
        for d, m in zip(dims, combo):
            if m is not None:
                n_d = piece.shape[d]
                lo = lax.slice_in_dim(piece, 0, width, axis=d)
                hi = lax.slice_in_dim(piece, n_d - width, n_d, axis=d)
                piece = pick(m[1], hi, lo)
        used = [(a, s, m) for a, s, m in zip(axes, sizes, combo) if m is not None]
        used.sort(key=lambda u: order.index(u[0]))
        pairs = []
        for parts in itertools.product(*[m[0] for _, _, m in used]):
            src = dst = 0
            for (_, s, _), (p, q) in zip(used, parts):
                src, dst = src * s + p, dst * s + q
            pairs.append((src, dst))
        got = lax.ppermute(piece, tuple(a for a, _, _ in used), pairs)
        landing = [(d, m[2]) for d, m in zip(dims, combo) if m is not None]
        for sides in itertools.product(("lo", "hi"), repeat=len(landing)):
            cond = True
            for (d, land_lo), side in zip(landing, sides):
                this = land_lo if side == "lo" else (not land_lo if isinstance(land_lo, bool) else ~land_lo)
                if isinstance(cond, bool) and isinstance(this, bool):
                    cond = cond and this
                elif isinstance(cond, bool):
                    cond = this if cond else False
                elif isinstance(this, bool):
                    cond = cond if this else False
                else:
                    cond = cond & this
            if cond is False:
                continue
            key = [None] * len(dims)
            for (d, _), side in zip(landing, sides):
                key[dims.index(d)] = side
            key = tuple(k or "mid" for k in key)
            val = got if cond is True else jnp.where(cond, got, 0.0)
            blocks[key] = val if key not in blocks else blocks[key] + val
    blocks[tuple("mid" for _ in dims)] = x

    def block(*key):
        if key in blocks:
            return blocks[key]
        shape = list(x.shape)
        for d, k in zip(dims, key):
            if k != "mid":
                shape[d] = width
        return jnp.zeros(shape, x.dtype)

    return block


def flux(d, rate):
    q = d * (1.0 / KAPPA)
    return rate * d / (1.0 + q * q)


def render_kernel(lim_ref, prm_ref, x_hbm, zlo_hbm, zhi_hbm, rband_hbm, cband_hbm, out_ref, a_ref, b_ref, m_ref, sem,
                  *, interior, h):
    depth, rows, lanes = a_ref.shape
    d_in, r_in, l_in = interior
    halo = STEPS
    copies = [
        pltpu.make_async_copy(x_hbm, b_ref.at[halo:halo + d_in, 0:r_in, 0:l_in], sem.at[0]),
        pltpu.make_async_copy(zlo_hbm, b_ref.at[0:halo, 0:r_in, 0:l_in], sem.at[1]),
        pltpu.make_async_copy(zhi_hbm, b_ref.at[halo + d_in:depth, 0:r_in, 0:l_in], sem.at[2]),
        pltpu.make_async_copy(rband_hbm, b_ref.at[:, r_in:rows, 0:l_in], sem.at[3]),
        pltpu.make_async_copy(cband_hbm, b_ref.at[:, :, l_in:lanes], sem.at[4]),
    ]
    for cp in copies:
        cp.start()

    row = lax.broadcasted_iota(jnp.int32, (rows, lanes), 0)
    lane = lax.broadcasted_iota(jnp.int32, (rows, lanes), 1)
    row_at = jnp.where(row < r_in + halo, row, row - rows)
    lane_at = jnp.where(lane < (l_in + lanes) // 2, lane, lane - lanes)
    ok = (row_at >= lim_ref[2]) & (row_at < lim_ref[3]) & (lane_at >= lim_ref[4]) & (lane_at < lim_ref[5])
    m_ref[...] = jnp.where(ok, 1.0, 0.0).astype(jnp.float32)

    cen = [prm_ref[k] for k in range(MATERIALS)]
    wid = [prm_ref[MATERIALS + k] for k in range(MATERIALS)]
    den = [prm_ref[2 * MATERIALS + k] for k in range(MATERIALS)]
    col = [[prm_ref[3 * MATERIALS + ch * MATERIALS + k] for k in range(MATERIALS)] for ch in range(CHANNELS)]
    for ch in range(CHANNELS + 1):
        out_ref[ch] = jnp.zeros((r_in, l_in), jnp.float32)

    for cp in copies:
        cp.wait()

    def smooth(src, dst, s):
        z0, z1 = s + 1, depth - 1 - s
        g0 = flux(src[z0] - src[z0 - 1], RATE_DEPTH)

        def body(z, g_prev):
            c = src[z]
            g = flux(src[z + 1] - c, RATE_DEPTH)
            fr = flux(pltpu.roll(c, rows - 1, 0) - c, RATE_PLANE)
            fc = flux(pltpu.roll(c, lanes - 1, 1) - c, RATE_PLANE)
            new = c + (g - g_prev) + (fr - pltpu.roll(fr, 1, 0)) + (fc - pltpu.roll(fc, 1, 1))
            inside = (z >= lim_ref[0]) & (z < lim_ref[1])
            zf = jnp.where(inside, 1.0, 0.0).astype(jnp.float32)
            dst[z] = new * (m_ref[...] * zf)
            return g

        lax.fori_loop(z0, z1, body, g0)

    smooth(b_ref, a_ref, 0)
    smooth(a_ref, b_ref, 1)
    smooth(b_ref, a_ref, 2)

    z0, z1 = halo, halo + d_in
    g0 = flux(a_ref[z0, 0:r_in, 0:l_in] - a_ref[z0 - 1, 0:r_in, 0:l_in], RATE_DEPTH)

    def final(z, g_prev):
        ci = a_ref[z, 0:r_in, 0:l_in]
        g = flux(a_ref[z + 1, 0:r_in, 0:l_in] - ci, RATE_DEPTH)
        c0 = a_ref[z, :, 0:l_in]
        fr = flux(pltpu.roll(c0, rows - 1, 0) - c0, RATE_PLANE)
        cr = a_ref[z, 0:r_in, :]
        fc = flux(pltpu.roll(cr, lanes - 1, 1) - cr, RATE_PLANE)
        v = ci + (g - g_prev) + (fr - pltpu.roll(fr, 1, 0))[0:r_in] + (fc - pltpu.roll(fc, 1, 1))[:, 0:l_in]
        bumps = [den[k] * jnp.exp(-(((v - cen[k]) / wid[k]) ** 2)) for k in range(MATERIALS)]
        ext = bumps[0] + bumps[1] + bumps[2] + bumps[3]
        run = out_ref[CHANNELS]
        through = jnp.exp(-h * run)
        for ch in range(CHANNELS):
            emit = col[ch][0] * bumps[0] + col[ch][1] * bumps[1] + col[ch][2] * bumps[2] + col[ch][3] * bumps[3]
            out_ref[ch] = out_ref[ch] + through * emit
        out_ref[CHANNELS] = run + ext
        return g

    lax.fori_loop(z0, z1, final, g0)
    for ch in range(CHANNELS):
        out_ref[ch] = h * out_ref[ch]


def render_block(pieces, lim, prm, interior, h):
    d_in, r_in, l_in = interior
    depth, rows, lanes = d_in + 2 * STEPS, r_in + 2 * STEPS, LANES
    cells = depth * rows * lanes
    kernel = functools.partial(render_kernel, interior=interior, h=h)
    return pl.pallas_call(
        kernel,
        out_shape=jax.ShapeDtypeStruct((CHANNELS + 1, r_in, l_in), jnp.float32),
        in_specs=[pl.BlockSpec(memory_space=pltpu.SMEM)] * 2 + [pl.BlockSpec(memory_space=pl.ANY)] * 5,
        out_specs=pl.BlockSpec(memory_space=pltpu.VMEM),
        scratch_shapes=[
            pltpu.VMEM((depth, rows, lanes), jnp.float32),
            pltpu.VMEM((depth, rows, lanes), jnp.float32),
            pltpu.VMEM((rows, lanes), jnp.float32),
            pltpu.SemaphoreType.DMA((5,)),
        ],
        compiler_params=pltpu.CompilerParams(vmem_limit_bytes=48 * 1024 * 1024),
        cost_estimate=pl.CostEstimate(
            flops=int(cells * STEPS * 40 + d_in * r_in * l_in * 60),
            transcendentals=int(d_in * r_in * l_in * (MATERIALS + 1)),
            bytes_accessed=int(cells * 4 + (CHANNELS + 1) * r_in * l_in * 4),
        ),
    )(lim, prm, *pieces)


def shards(phase_field, centres, widths, densities, colours, order):
    depth_cells, row_cells, col_cells = phase_field.shape
    groups = lax.axis_size("gz")
    h = 1.0 / (depth_cells * groups)
    block = halo_stage(phase_field, ((0, "gz"), (1, "gx"), (2, "gy")), STEPS, order)
    zlo, zhi = block("lo", "mid", "mid"), block("hi", "mid", "mid")
    sides = ("lo", "mid", "hi")

    def band(parts):
        return jnp.concatenate([jnp.concatenate([block(zs, r, c) for r, c in parts], axis=1) for zs in sides], axis=0)

    rband = band((("hi", "mid"), ("lo", "mid")))
    right = band((("mid", "hi"), ("hi", "hi"), ("lo", "hi")))
    left = band((("mid", "lo"), ("hi", "lo"), ("lo", "lo")))
    fill = jnp.zeros(right.shape[:2] + (LANES - col_cells - 2 * STEPS,), jnp.float32)
    cband = jnp.concatenate([right, fill, left], axis=2)

    z_lo = STEPS - lax.axis_index("gz") * depth_cells
    r_lo = -lax.axis_index("gx") * row_cells
    c_lo = -lax.axis_index("gy") * col_cells
    lim = jnp.stack(
        [
            z_lo,
            z_lo + depth_cells * groups,
            r_lo,
            r_lo + row_cells * lax.axis_size("gx"),
            c_lo,
            c_lo + col_cells * lax.axis_size("gy"),
        ]
    ).astype(jnp.int32)
    prm = jnp.concatenate([centres, widths, densities, colours.reshape(-1)]).astype(jnp.float32)

    seg = render_block((phase_field, zlo, zhi, rband, cband), lim, prm, (depth_cells, row_cells, col_cells), h)

    rows_part = row_cells // groups
    parts = seg.reshape(CHANNELS + 1, groups, rows_part, col_cells)
    got = lax.all_to_all(parts, "gz", 1, 1, tiled=True)
    prefix = jnp.zeros((rows_part, col_cells), jnp.float32)
    rad = jnp.zeros((CHANNELS, rows_part, col_cells), jnp.float32)
    for g in range(groups):
        rad = rad + jnp.exp(-h * prefix)[None] * got[:CHANNELS, g]
        prefix = prefix + got[CHANNELS, g]
    alpha = 1.0 - jnp.exp(-h * prefix)
    return jnp.concatenate([rad, alpha[None]], axis=0)


def solution(mesh):
    placed = (P("gz", "gx", "gy"), P(), P(), P(), P())
    return jax.shard_map(
        functools.partial(shards, order=tuple(mesh.axis_names)), mesh=mesh, in_specs=placed, out_specs=P(None, ("gx", "gz"), "gy"), check_vma=False
    )
```

```python
import functools
import itertools

import jax
import jax.numpy as jnp
from jax import lax
from jax.experimental import pallas as pl
from jax.experimental.pallas import tpu as pltpu
from jax.sharding import PartitionSpec as P

STEPS = 4
MATERIALS = 4
CHANNELS = 3

KAPPA = 0.5
RATE_DEPTH = 0.3
RATE_PLANE = 0.09
LANES = 256
CHUNK = 8


def pick(cond, a, b):
    if isinstance(cond, bool):
        return a if cond else b
    return jnp.where(cond, a, b)


def axis_moves(axis):
    n = lax.axis_size(axis)
    if n == 1:
        return []
    if n == 2:
        me = lax.axis_index(axis)
        return [([(0, 1), (1, 0)], me == 0, me == 1)]
    up = [(i, i + 1) for i in range(n - 1)]
    down = [(i + 1, i) for i in range(n - 1)]
    return [(up, True, True), (down, False, False)]


def halo_stage(x_parts, dim_axes, width):
    x_parts = x_parts if isinstance(x_parts, tuple) else (x_parts,)
    x = x_parts[0] if len(x_parts) == 1 else jnp.concatenate(x_parts, axis=0)
    dims = [d for d, _ in dim_axes]
    axes = [a for _, a in dim_axes]
    sizes = [lax.axis_size(a) for a in axes]
    options = [[None] + axis_moves(a) for a in axes]
    blocks = {}
    for combo in itertools.product(*options):
        if all(m is None for m in combo):
            continue
        cut = []
        for part in x_parts:
            for d, m in zip(dims, combo):
                if m is not None:
                    n_d = part.shape[d]
                    lo = lax.slice_in_dim(part, 0, width, axis=d)
                    hi = lax.slice_in_dim(part, n_d - width, n_d, axis=d)
                    part = pick(m[1], hi, lo)
            cut.append(part)
        piece = cut[0] if len(cut) == 1 else jnp.concatenate(cut, axis=0)
        used = [(a, s, m) for a, s, m in zip(axes, sizes, combo) if m is not None]
        pairs = []
        for parts in itertools.product(*[m[0] for _, _, m in used]):
            src = dst = 0
            for (_, s, _), (p, q) in zip(used, parts):
                src, dst = src * s + p, dst * s + q
            pairs.append((src, dst))
        got = lax.ppermute(piece, tuple(a for a, _, _ in used), pairs)
        landing = [(d, m[2]) for d, m in zip(dims, combo) if m is not None]
        for sides in itertools.product(("lo", "hi"), repeat=len(landing)):
            cond = True
            for (d, land_lo), side in zip(landing, sides):
                this = land_lo if side == "lo" else (not land_lo if isinstance(land_lo, bool) else ~land_lo)
                if isinstance(cond, bool) and isinstance(this, bool):
                    cond = cond and this
                elif isinstance(cond, bool):
                    cond = this if cond else False
                elif isinstance(this, bool):
                    cond = cond if this else False
                else:
                    cond = cond & this
            if cond is False:
                continue
            key = [None] * len(dims)
            for (d, _), side in zip(landing, sides):
                key[dims.index(d)] = side
            key = tuple(k or "mid" for k in key)
            val = got if cond is True else jnp.where(cond, got, 0.0)
            blocks[key] = val if key not in blocks else blocks[key] + val
    blocks[tuple("mid" for _ in dims)] = x

    def block(*key):
        if key in blocks:
            return blocks[key]
        shape = list(x.shape)
        for d, k in zip(dims, key):
            if k != "mid":
                shape[d] = width
        return jnp.zeros(shape, x.dtype)

    return block


def flux(d, rate):
    q = d * (1.0 / KAPPA)
    return rate * d / (1.0 + q * q)


def render_kernel(lim_ref, prm_ref, x_hbm, zlo_hbm, zhi_hbm, rband_hbm, cband_hbm, out_ref, a_ref, b_ref, m_ref, sem,
                  *, interior, h):
    depth, rows, lanes = a_ref.shape
    d_in, r_in, l_in = interior
    halo = STEPS
    chunk = CHUNK
    n_chunks = -(-depth // chunk)
    chunk_copies = []
    for k in range(n_chunks):
        lo, hi = k * chunk, min(depth, (k + 1) * chunk)
        jobs = [
            (rband_hbm.at[lo:hi], b_ref.at[lo:hi, r_in:rows, 0:l_in]),
            (cband_hbm.at[lo:hi], b_ref.at[lo:hi, :, l_in:lanes]),
        ]
        spans = ((0, halo, zlo_hbm, 0), (halo, halo + d_in, x_hbm, halo), (halo + d_in, depth, zhi_hbm, halo + d_in))
        for s_lo, s_hi, ref, base in spans:
            a, b = max(lo, s_lo), min(hi, s_hi)
            if a < b:
                jobs.append((ref.at[a - base:b - base], b_ref.at[a:b, 0:r_in, 0:l_in]))
        chunk_copies.append(jobs)
    sem_at = 0
    for k, jobs in enumerate(chunk_copies):
        made = []
        for src_ref, dst_ref in jobs:
            made.append(pltpu.make_async_copy(src_ref, dst_ref, sem.at[sem_at]))
            sem_at += 1
        chunk_copies[k] = made
        for cp in made:
            cp.start()

    row = lax.broadcasted_iota(jnp.int32, (rows, lanes), 0)
    lane = lax.broadcasted_iota(jnp.int32, (rows, lanes), 1)
    row_at = jnp.where(row < r_in + halo, row, row - rows)
    lane_at = jnp.where(lane < (l_in + lanes) // 2, lane, lane - lanes)
    ok = (row_at >= lim_ref[2]) & (row_at < lim_ref[3]) & (lane_at >= lim_ref[4]) & (lane_at < lim_ref[5])
    m_ref[...] = jnp.where(ok, 1.0, 0.0).astype(jnp.float32)

    cen = [prm_ref[k] for k in range(MATERIALS)]
    wid = [prm_ref[MATERIALS + k] for k in range(MATERIALS)]
    den = [prm_ref[2 * MATERIALS + k] for k in range(MATERIALS)]
    col = [[prm_ref[3 * MATERIALS + ch * MATERIALS + k] for k in range(MATERIALS)] for ch in range(CHANNELS)]
    for ch in range(CHANNELS + 1):
        out_ref[ch] = jnp.zeros((r_in, l_in), jnp.float32)

    def smooth(src, dst, s, arrived=None):
        z0, z1 = s + 1, depth - 1 - s
        if arrived is not None:
            arrived(0)
            arrived(1)
        g0 = flux(src[z0] - src[z0 - 1], RATE_DEPTH)

        def body(z, g_prev):
            c = src[z]
            g = flux(src[z + 1] - c, RATE_DEPTH)
            fr = flux(pltpu.roll(c, rows - 1, 0) - c, RATE_PLANE)
            fc = flux(pltpu.roll(c, lanes - 1, 1) - c, RATE_PLANE)
            new = c + (g - g_prev) + (fr - pltpu.roll(fr, 1, 0)) + (fc - pltpu.roll(fc, 1, 1))
            inside = (z >= lim_ref[0]) & (z < lim_ref[1])
            zf = jnp.where(inside, 1.0, 0.0).astype(jnp.float32)
            dst[z] = new * (m_ref[...] * zf)
            return g

        if arrived is None:
            lax.fori_loop(z0, z1, body, g0)
            return
        g = g0
        for k in range(n_chunks):
            lo, hi = max(z0, k * chunk), min(z1, (k + 1) * chunk)
            if 1 <= k and k + 1 < n_chunks:
                arrived(k + 1)
            if lo < hi:
                g = lax.fori_loop(lo, hi, body, g)

    def arrived(k):
        for cp in chunk_copies[k]:
            cp.wait()

    smooth(b_ref, a_ref, 0, arrived)
    smooth(a_ref, b_ref, 1)
    smooth(b_ref, a_ref, 2)

    z0, z1 = halo, halo + d_in
    g0 = flux(a_ref[z0, 0:r_in, 0:l_in] - a_ref[z0 - 1, 0:r_in, 0:l_in], RATE_DEPTH)

    def final(z, g_prev):
        ci = a_ref[z, 0:r_in, 0:l_in]
        g = flux(a_ref[z + 1, 0:r_in, 0:l_in] - ci, RATE_DEPTH)
        c0 = a_ref[z, :, 0:l_in]
        fr = flux(pltpu.roll(c0, rows - 1, 0) - c0, RATE_PLANE)
        cr = a_ref[z, 0:r_in, :]
        fc = flux(pltpu.roll(cr, lanes - 1, 1) - cr, RATE_PLANE)
        v = ci + (g - g_prev) + (fr - pltpu.roll(fr, 1, 0))[0:r_in] + (fc - pltpu.roll(fc, 1, 1))[:, 0:l_in]
        bumps = [den[k] * jnp.exp(-(((v - cen[k]) / wid[k]) ** 2)) for k in range(MATERIALS)]
        ext = bumps[0] + bumps[1] + bumps[2] + bumps[3]
        run = out_ref[CHANNELS]
        through = jnp.exp(-h * run)
        for ch in range(CHANNELS):
            emit = col[ch][0] * bumps[0] + col[ch][1] * bumps[1] + col[ch][2] * bumps[2] + col[ch][3] * bumps[3]
            out_ref[ch] = out_ref[ch] + through * emit
        out_ref[CHANNELS] = run + ext
        return g

    lax.fori_loop(z0, z1, final, g0)
    for ch in range(CHANNELS):
        out_ref[ch] = h * out_ref[ch]


def render_block(pieces, lim, prm, interior, h):
    d_in, r_in, l_in = interior
    depth, rows, lanes = d_in + 2 * STEPS, r_in + 2 * STEPS, LANES
    cells = depth * rows * lanes
    kernel = functools.partial(render_kernel, interior=interior, h=h)
    n_dma = 0
    for k in range(-(-depth // CHUNK)):
        lo, hi = k * CHUNK, min(depth, (k + 1) * CHUNK)
        n_dma += 2 + sum(1 for s_lo, s_hi in ((0, STEPS), (STEPS, STEPS + d_in), (STEPS + d_in, depth)) if max(lo, s_lo) < min(hi, s_hi))
    return pl.pallas_call(
        kernel,
        out_shape=jax.ShapeDtypeStruct((CHANNELS + 1, r_in, l_in), jnp.float32),
        in_specs=[pl.BlockSpec(memory_space=pltpu.SMEM)] * 2 + [pl.BlockSpec(memory_space=pl.ANY)] * 5,
        out_specs=pl.BlockSpec(memory_space=pltpu.VMEM),
        scratch_shapes=[
            pltpu.VMEM((depth, rows, lanes), jnp.float32),
            pltpu.VMEM((depth, rows, lanes), jnp.float32),
            pltpu.VMEM((rows, lanes), jnp.float32),
            pltpu.SemaphoreType.DMA((n_dma,)),
        ],
        compiler_params=pltpu.CompilerParams(vmem_limit_bytes=48 * 1024 * 1024),
        cost_estimate=pl.CostEstimate(
            flops=int(cells * STEPS * 40 + d_in * r_in * l_in * 60),
            transcendentals=int(d_in * r_in * l_in * (MATERIALS + 1)),
            bytes_accessed=int(cells * 4 + (CHANNELS + 1) * r_in * l_in * 4),
        ),
    )(lim, prm, *pieces)


def shards(phase_field, centres, widths, densities, colours):
    depth_cells, row_cells, col_cells = phase_field.shape
    groups = lax.axis_size("gz")
    h = 1.0 / (depth_cells * groups)
    zblock = halo_stage(phase_field, ((0, "gz"),), STEPS)
    zlo, zhi = zblock("lo"), zblock("hi")
    plane = halo_stage((zlo, phase_field, zhi), ((1, "gx"), (2, "gy")), STEPS)
    rband = jnp.concatenate([plane("hi", "mid"), plane("lo", "mid")], axis=1)
    right = jnp.concatenate([plane("mid", "hi"), plane("hi", "hi"), plane("lo", "hi")], axis=1)
    left = jnp.concatenate([plane("mid", "lo"), plane("hi", "lo"), plane("lo", "lo")], axis=1)
    fill = jnp.zeros(right.shape[:2] + (LANES - col_cells - 2 * STEPS,), jnp.float32)
    cband = jnp.concatenate([right, fill, left], axis=2)

    z_lo = STEPS - lax.axis_index("gz") * depth_cells
    r_lo = -lax.axis_index("gx") * row_cells
    c_lo = -lax.axis_index("gy") * col_cells
    lim = jnp.stack(
        [
            z_lo,
            z_lo + depth_cells * groups,
            r_lo,
            r_lo + row_cells * lax.axis_size("gx"),
            c_lo,
            c_lo + col_cells * lax.axis_size("gy"),
        ]
    ).astype(jnp.int32)
    prm = jnp.concatenate([centres, widths, densities, colours.reshape(-1)]).astype(jnp.float32)

    seg = render_block((phase_field, zlo, zhi, rband, cband), lim, prm, (depth_cells, row_cells, col_cells), h)

    rows_part = row_cells // groups
    parts = seg.reshape(CHANNELS + 1, groups, rows_part, col_cells)
    got = lax.all_to_all(parts, "gz", 1, 1, tiled=True)
    prefix = jnp.zeros((rows_part, col_cells), jnp.float32)
    rad = jnp.zeros((CHANNELS, rows_part, col_cells), jnp.float32)
    for g in range(groups):
        rad = rad + jnp.exp(-h * prefix)[None] * got[:CHANNELS, g]
        prefix = prefix + got[CHANNELS, g]
    alpha = 1.0 - jnp.exp(-h * prefix)
    return jnp.concatenate([rad, alpha[None]], axis=0)


def solution(mesh):
    placed = (P("gz", "gx", "gy"), P(), P(), P(), P())
    return jax.shard_map(
        shards, mesh=mesh, in_specs=placed, out_specs=P(None, ("gx", "gz"), "gy"), check_vma=False
    )
```

```python
import functools
import itertools

import jax
import jax.numpy as jnp
from jax import lax
from jax.experimental import pallas as pl
from jax.experimental.pallas import tpu as pltpu
from jax.sharding import PartitionSpec as P

STEPS = 4
MATERIALS = 4
CHANNELS = 3

KAPPA = 0.5
RATE_DEPTH = 0.3
RATE_PLANE = 0.09
LANES = 256


def pick(cond, a, b):
    if isinstance(cond, bool):
        return a if cond else b
    return jnp.where(cond, a, b)


def axis_moves(axis):
    n = lax.axis_size(axis)
    if n == 1:
        return []
    if n == 2:
        me = lax.axis_index(axis)
        return [([(0, 1), (1, 0)], me == 0, me == 1)]
    up = [(i, i + 1) for i in range(n - 1)]
    down = [(i + 1, i) for i in range(n - 1)]
    return [(up, True, True), (down, False, False)]


def halo_stage(x, dim_axes, width):
    dims = [d for d, _ in dim_axes]
    axes = [a for _, a in dim_axes]
    sizes = [lax.axis_size(a) for a in axes]
    options = [[None] + axis_moves(a) for a in axes]
    blocks = {}
    for combo in itertools.product(*options):
        if all(m is None for m in combo):
            continue
        piece = x
        for d, m in zip(dims, combo):
            if m is not None:
                n_d = piece.shape[d]
                lo = lax.slice_in_dim(piece, 0, width, axis=d)
                hi = lax.slice_in_dim(piece, n_d - width, n_d, axis=d)
                piece = pick(m[1], hi, lo)
        used = [(a, s, m) for a, s, m in zip(axes, sizes, combo) if m is not None]
        pairs = []
        for parts in itertools.product(*[m[0] for _, _, m in used]):
            src = dst = 0
            for (_, s, _), (p, q) in zip(used, parts):
                src, dst = src * s + p, dst * s + q
            pairs.append((src, dst))
        got = lax.ppermute(piece, tuple(a for a, _, _ in used), pairs)
        landing = [(d, m[2]) for d, m in zip(dims, combo) if m is not None]
        for sides in itertools.product(("lo", "hi"), repeat=len(landing)):
            cond = True
            for (d, land_lo), side in zip(landing, sides):
                this = land_lo if side == "lo" else (not land_lo if isinstance(land_lo, bool) else ~land_lo)
                if isinstance(cond, bool) and isinstance(this, bool):
                    cond = cond and this
                elif isinstance(cond, bool):
                    cond = this if cond else False
                elif isinstance(this, bool):
                    cond = cond if this else False
                else:
                    cond = cond & this
            if cond is False:
                continue
            key = [None] * len(dims)
            for (d, _), side in zip(landing, sides):
                key[dims.index(d)] = side
            key = tuple(k or "mid" for k in key)
            val = got if cond is True else jnp.where(cond, got, 0.0)
            blocks[key] = val if key not in blocks else blocks[key] + val
    blocks[tuple("mid" for _ in dims)] = x

    def block(*key):
        if key in blocks:
            return blocks[key]
        shape = list(x.shape)
        for d, k in zip(dims, key):
            if k != "mid":
                shape[d] = width
        return jnp.zeros(shape, x.dtype)

    return block


def flux(d):
    q = d * (1.0 / KAPPA)
    return d / (1.0 + q * q)


def render_kernel(lim_ref, prm_ref, x_hbm, zlo_hbm, zhi_hbm, rband_hbm, cband_hbm, out_ref, a_ref, b_ref, m_ref, acc_ref, sem,
                  *, interior, h):
    depth, rows, lanes = a_ref.shape
    d_in, r_in, l_in = interior
    halo = STEPS
    copies = [
        pltpu.make_async_copy(x_hbm, b_ref.at[halo:halo + d_in, 0:r_in, 0:l_in], sem.at[0]),
        pltpu.make_async_copy(zlo_hbm, b_ref.at[0:halo, 0:r_in, 0:l_in], sem.at[1]),
        pltpu.make_async_copy(zhi_hbm, b_ref.at[halo + d_in:depth, 0:r_in, 0:l_in], sem.at[2]),
        pltpu.make_async_copy(rband_hbm, b_ref.at[:, r_in:rows, 0:l_in], sem.at[3]),
        pltpu.make_async_copy(cband_hbm, b_ref.at[:, :, l_in:lanes], sem.at[4]),
    ]
    for cp in copies:
        cp.start()

    row = lax.broadcasted_iota(jnp.int32, (rows, lanes), 0)
    lane = lax.broadcasted_iota(jnp.int32, (rows, lanes), 1)
    row_at = jnp.where(row < r_in + halo, row, row - rows)
    lane_at = jnp.where(lane < (l_in + lanes) // 2, lane, lane - lanes)
    ok = (row_at >= lim_ref[2]) & (row_at < lim_ref[3]) & (lane_at >= lim_ref[4]) & (lane_at < lim_ref[5])
    m_ref[0] = jnp.zeros((rows, lanes), jnp.float32)
    m_ref[1] = jnp.where(ok, 1.0, 0.0).astype(jnp.float32)

    cen = [prm_ref[k] for k in range(MATERIALS)]
    wid = [prm_ref[MATERIALS + k] for k in range(MATERIALS)]
    den = [prm_ref[2 * MATERIALS + k] for k in range(MATERIALS)]
    col = [[prm_ref[3 * MATERIALS + ch * MATERIALS + k] for k in range(MATERIALS)] for ch in range(CHANNELS)]
    out_ref[CHANNELS] = jnp.zeros((r_in, l_in), jnp.float32)
    for k in range(MATERIALS):
        acc_ref[k] = jnp.zeros((r_in, l_in), jnp.float32)

    for cp in copies:
        cp.wait()

    def smooth(src, dst, s):
        z0, z1 = s + 1, depth - 1 - s
        g0 = flux(src[z0] - src[z0 - 1])

        def body(z, g_prev):
            c = src[z]
            g = flux(src[z + 1] - c)
            fr = flux(pltpu.roll(c, rows - 1, 0) - c)
            fc = flux(pltpu.roll(c, lanes - 1, 1) - c)
            plane = (fr - pltpu.roll(fr, 1, 0)) + (fc - pltpu.roll(fc, 1, 1))
            new = c + RATE_DEPTH * (g - g_prev) + RATE_PLANE * plane
            inside = ((z >= lim_ref[0]) & (z < lim_ref[1])).astype(jnp.int32)
            dst[z] = new * m_ref[inside]
            return g

        lax.fori_loop(z0, z1, body, g0)

    smooth(b_ref, a_ref, 0)
    smooth(a_ref, b_ref, 1)
    smooth(b_ref, a_ref, 2)

    z0, z1 = halo, halo + d_in
    g0 = flux(a_ref[z0, 0:r_in, 0:l_in] - a_ref[z0 - 1, 0:r_in, 0:l_in])

    def final(z, g_prev):
        ci = a_ref[z, 0:r_in, 0:l_in]
        g = flux(a_ref[z + 1, 0:r_in, 0:l_in] - ci)
        c0 = a_ref[z, :, 0:l_in]
        fr = flux(pltpu.roll(c0, rows - 1, 0) - c0)
        cr = a_ref[z, 0:r_in, :]
        fc = flux(pltpu.roll(cr, lanes - 1, 1) - cr)
        plane = (fr - pltpu.roll(fr, 1, 0))[0:r_in] + (fc - pltpu.roll(fc, 1, 1))[:, 0:l_in]
        v = ci + RATE_DEPTH * (g - g_prev) + RATE_PLANE * plane
        bumps = [den[k] * jnp.exp(-(((v - cen[k]) / wid[k]) ** 2)) for k in range(MATERIALS)]
        ext = bumps[0] + bumps[1] + bumps[2] + bumps[3]
        run = out_ref[CHANNELS]
        through = jnp.exp(-h * run)
        for k in range(MATERIALS):
            acc_ref[k] = acc_ref[k] + through * bumps[k]
        out_ref[CHANNELS] = run + ext
        return g

    lax.fori_loop(z0, z1, final, g0)
    for ch in range(CHANNELS):
        emit = col[ch][0] * acc_ref[0] + col[ch][1] * acc_ref[1] + col[ch][2] * acc_ref[2] + col[ch][3] * acc_ref[3]
        out_ref[ch] = h * emit


def render_block(pieces, lim, prm, interior, h):
    d_in, r_in, l_in = interior
    depth, rows, lanes = d_in + 2 * STEPS, r_in + 2 * STEPS, LANES
    cells = depth * rows * lanes
    kernel = functools.partial(render_kernel, interior=interior, h=h)
    return pl.pallas_call(
        kernel,
        out_shape=jax.ShapeDtypeStruct((CHANNELS + 1, r_in, l_in), jnp.float32),
        in_specs=[pl.BlockSpec(memory_space=pltpu.SMEM)] * 2 + [pl.BlockSpec(memory_space=pl.ANY)] * 5,
        out_specs=pl.BlockSpec(memory_space=pltpu.VMEM),
        scratch_shapes=[
            pltpu.VMEM((depth, rows, lanes), jnp.float32),
            pltpu.VMEM((depth, rows, lanes), jnp.float32),
            pltpu.VMEM((2, rows, lanes), jnp.float32),
            pltpu.VMEM((MATERIALS, r_in, l_in), jnp.float32),
            pltpu.SemaphoreType.DMA((5,)),
        ],
        compiler_params=pltpu.CompilerParams(vmem_limit_bytes=48 * 1024 * 1024),
        cost_estimate=pl.CostEstimate(
            flops=int(cells * STEPS * 40 + d_in * r_in * l_in * 60),
            transcendentals=int(d_in * r_in * l_in * (MATERIALS + 1)),
            bytes_accessed=int(cells * 4 + (CHANNELS + 1) * r_in * l_in * 4),
        ),
    )(lim, prm, *pieces)


def shards(phase_field, centres, widths, densities, colours):
    depth_cells, row_cells, col_cells = phase_field.shape
    groups = lax.axis_size("gz")
    h = 1.0 / (depth_cells * groups)
    zblock = halo_stage(phase_field, ((0, "gz"),), STEPS)
    zlo, zhi = zblock("lo"), zblock("hi")
    deep = jnp.concatenate([zlo, phase_field, zhi], axis=0)
    plane = halo_stage(deep, ((1, "gx"), (2, "gy")), STEPS)
    rband = jnp.concatenate([plane("hi", "mid"), plane("lo", "mid")], axis=1)
    right = jnp.concatenate([plane("mid", "hi"), plane("hi", "hi"), plane("lo", "hi")], axis=1)
    left = jnp.concatenate([plane("mid", "lo"), plane("hi", "lo"), plane("lo", "lo")], axis=1)
    fill = jnp.zeros(right.shape[:2] + (LANES - col_cells - 2 * STEPS,), jnp.float32)
    cband = jnp.concatenate([right, fill, left], axis=2)

    z_lo = STEPS - lax.axis_index("gz") * depth_cells
    r_lo = -lax.axis_index("gx") * row_cells
    c_lo = -lax.axis_index("gy") * col_cells
    lim = jnp.stack(
        [
            z_lo,
            z_lo + depth_cells * groups,
            r_lo,
            r_lo + row_cells * lax.axis_size("gx"),
            c_lo,
            c_lo + col_cells * lax.axis_size("gy"),
        ]
    ).astype(jnp.int32)
    prm = jnp.concatenate([centres, widths, densities, colours.reshape(-1)]).astype(jnp.float32)

    seg = render_block((phase_field, zlo, zhi, rband, cband), lim, prm, (depth_cells, row_cells, col_cells), h)

    rows_part = row_cells // groups
    parts = seg.reshape(CHANNELS + 1, groups, rows_part, col_cells)
    got = lax.all_to_all(parts, "gz", 1, 1, tiled=True)
    prefix = jnp.zeros((rows_part, col_cells), jnp.float32)
    rad = jnp.zeros((CHANNELS, rows_part, col_cells), jnp.float32)
    for g in range(groups):
        rad = rad + jnp.exp(-h * prefix)[None] * got[:CHANNELS, g]
        prefix = prefix + got[CHANNELS, g]
    alpha = 1.0 - jnp.exp(-h * prefix)
    return jnp.concatenate([rad, alpha[None]], axis=0)


def solution(mesh):
    placed = (P("gz", "gx", "gy"), P(), P(), P(), P())
    return jax.shard_map(
        shards, mesh=mesh, in_specs=placed, out_specs=P(None, ("gx", "gz"), "gy"), check_vma=False
    )
```

```python
import functools
import itertools

import jax
import jax.numpy as jnp
from jax import lax
from jax.experimental import pallas as pl
from jax.experimental.pallas import tpu as pltpu
from jax.sharding import PartitionSpec as P

STEPS = 4
MATERIALS = 4
CHANNELS = 3

KAPPA = 0.5
RATE_DEPTH = 0.3
RATE_PLANE = 0.09
LANES = 256


def pick(cond, a, b):
    if isinstance(cond, bool):
        return a if cond else b
    return jnp.where(cond, a, b)


def axis_moves(axis):
    n = lax.axis_size(axis)
    if n == 1:
        return []
    if n == 2:
        me = lax.axis_index(axis)
        return [([(0, 1), (1, 0)], me == 0, me == 1)]
    up = [(i, i + 1) for i in range(n - 1)]
    down = [(i + 1, i) for i in range(n - 1)]
    return [(up, True, True), (down, False, False)]


def halo_stage(x, dim_axes, width):
    dims = [d for d, _ in dim_axes]
    axes = [a for _, a in dim_axes]
    sizes = [lax.axis_size(a) for a in axes]
    options = [[None] + axis_moves(a) for a in axes]
    blocks = {}
    for combo in itertools.product(*options):
        if all(m is None for m in combo):
            continue
        piece = x
        for d, m in zip(dims, combo):
            if m is not None:
                n_d = piece.shape[d]
                lo = lax.slice_in_dim(piece, 0, width, axis=d)
                hi = lax.slice_in_dim(piece, n_d - width, n_d, axis=d)
                piece = pick(m[1], hi, lo)
        used = [(a, s, m) for a, s, m in zip(axes, sizes, combo) if m is not None]
        pairs = []
        for parts in itertools.product(*[m[0] for _, _, m in used]):
            src = dst = 0
            for (_, s, _), (p, q) in zip(used, parts):
                src, dst = src * s + p, dst * s + q
            pairs.append((src, dst))
        got = lax.ppermute(piece, tuple(a for a, _, _ in used), pairs)
        landing = [(d, m[2]) for d, m in zip(dims, combo) if m is not None]
        for sides in itertools.product(("lo", "hi"), repeat=len(landing)):
            cond = True
            for (d, land_lo), side in zip(landing, sides):
                this = land_lo if side == "lo" else (not land_lo if isinstance(land_lo, bool) else ~land_lo)
                if isinstance(cond, bool) and isinstance(this, bool):
                    cond = cond and this
                elif isinstance(cond, bool):
                    cond = this if cond else False
                elif isinstance(this, bool):
                    cond = cond if this else False
                else:
                    cond = cond & this
            if cond is False:
                continue
            key = [None] * len(dims)
            for (d, _), side in zip(landing, sides):
                key[dims.index(d)] = side
            key = tuple(k or "mid" for k in key)
            val = got if cond is True else jnp.where(cond, got, 0.0)
            blocks[key] = val if key not in blocks else blocks[key] + val
    blocks[tuple("mid" for _ in dims)] = x

    def block(*key):
        if key in blocks:
            return blocks[key]
        shape = list(x.shape)
        for d, k in zip(dims, key):
            if k != "mid":
                shape[d] = width
        return jnp.zeros(shape, x.dtype)

    return block


def flux(d, rate):
    q = d * (1.0 / KAPPA)
    return rate * d / (1.0 + q * q)


def render_kernel(lim_ref, prm_ref, x_hbm, zlo_hbm, zhi_hbm, rband_hbm, cband_hbm, out_ref, a_ref, b_ref, m_ref, acc_ref, sem,
                  *, interior, h):
    depth, rows, lanes = a_ref.shape
    d_in, r_in, l_in = interior
    halo = STEPS
    copies = [
        pltpu.make_async_copy(x_hbm, b_ref.at[halo:halo + d_in, 0:r_in, 0:l_in], sem.at[0]),
        pltpu.make_async_copy(zlo_hbm, b_ref.at[0:halo, 0:r_in, 0:l_in], sem.at[1]),
        pltpu.make_async_copy(zhi_hbm, b_ref.at[halo + d_in:depth, 0:r_in, 0:l_in], sem.at[2]),
        pltpu.make_async_copy(rband_hbm, b_ref.at[:, r_in:rows, 0:l_in], sem.at[3]),
        pltpu.make_async_copy(cband_hbm, b_ref.at[:, :, l_in:lanes], sem.at[4]),
    ]
    for cp in copies:
        cp.start()

    row = lax.broadcasted_iota(jnp.int32, (rows, lanes), 0)
    lane = lax.broadcasted_iota(jnp.int32, (rows, lanes), 1)
    row_at = jnp.where(row < r_in + halo, row, row - rows)
    lane_at = jnp.where(lane < (l_in + lanes) // 2, lane, lane - lanes)
    ok = (row_at >= lim_ref[2]) & (row_at < lim_ref[3]) & (lane_at >= lim_ref[4]) & (lane_at < lim_ref[5])
    m_ref[...] = jnp.where(ok, 1.0, 0.0).astype(jnp.float32)

    cen = [prm_ref[k] for k in range(MATERIALS)]
    wid = [prm_ref[MATERIALS + k] for k in range(MATERIALS)]
    den = [prm_ref[2 * MATERIALS + k] for k in range(MATERIALS)]
    col = [[prm_ref[3 * MATERIALS + ch * MATERIALS + k] for k in range(MATERIALS)] for ch in range(CHANNELS)]
    out_ref[CHANNELS] = jnp.zeros((r_in, l_in), jnp.float32)
    for k in range(MATERIALS):
        acc_ref[k] = jnp.zeros((r_in, l_in), jnp.float32)

    for cp in copies:
        cp.wait()

    def smooth(src, dst, s):
        z0, z1 = s + 1, depth - 1 - s
        g0 = flux(src[z0] - src[z0 - 1], RATE_DEPTH)

        def body(z, g_prev):
            c = src[z]
            g = flux(src[z + 1] - c, RATE_DEPTH)
            fr = flux(pltpu.roll(c, rows - 1, 0) - c, RATE_PLANE)
            fc = flux(pltpu.roll(c, lanes - 1, 1) - c, RATE_PLANE)
            new = c + (g - g_prev) + (fr - pltpu.roll(fr, 1, 0)) + (fc - pltpu.roll(fc, 1, 1))
            inside = (z >= lim_ref[0]) & (z < lim_ref[1])
            zf = jnp.where(inside, 1.0, 0.0).astype(jnp.float32)
            dst[z] = new * (m_ref[...] * zf)
            return g

        lax.fori_loop(z0, z1, body, g0)

    smooth(b_ref, a_ref, 0)
    smooth(a_ref, b_ref, 1)
    smooth(b_ref, a_ref, 2)

    z0, z1 = halo, halo + d_in
    g0 = flux(a_ref[z0, 0:r_in, 0:l_in] - a_ref[z0 - 1, 0:r_in, 0:l_in], RATE_DEPTH)

    def final(z, g_prev):
        ci = a_ref[z, 0:r_in, 0:l_in]
        g = flux(a_ref[z + 1, 0:r_in, 0:l_in] - ci, RATE_DEPTH)
        c0 = a_ref[z, :, 0:l_in]
        fr = flux(pltpu.roll(c0, rows - 1, 0) - c0, RATE_PLANE)
        cr = a_ref[z, 0:r_in, :]
        fc = flux(pltpu.roll(cr, lanes - 1, 1) - cr, RATE_PLANE)
        v = ci + (g - g_prev) + (fr - pltpu.roll(fr, 1, 0))[0:r_in] + (fc - pltpu.roll(fc, 1, 1))[:, 0:l_in]
        bumps = [den[k] * jnp.exp(-(((v - cen[k]) / wid[k]) ** 2)) for k in range(MATERIALS)]
        ext = bumps[0] + bumps[1] + bumps[2] + bumps[3]
        run = out_ref[CHANNELS]
        through = jnp.exp(-h * run)
        for k in range(MATERIALS):
            acc_ref[k] = acc_ref[k] + through * bumps[k]
        out_ref[CHANNELS] = run + ext
        return g

    lax.fori_loop(z0, z1, final, g0)
    for ch in range(CHANNELS):
        emit = col[ch][0] * acc_ref[0] + col[ch][1] * acc_ref[1] + col[ch][2] * acc_ref[2] + col[ch][3] * acc_ref[3]
        out_ref[ch] = h * emit


def render_block(pieces, lim, prm, interior, h):
    d_in, r_in, l_in = interior
    depth, rows, lanes = d_in + 2 * STEPS, r_in + 2 * STEPS, LANES
    cells = depth * rows * lanes
    kernel = functools.partial(render_kernel, interior=interior, h=h)
    return pl.pallas_call(
        kernel,
        out_shape=jax.ShapeDtypeStruct((CHANNELS + 1, r_in, l_in), jnp.float32),
        in_specs=[pl.BlockSpec(memory_space=pltpu.SMEM)] * 2 + [pl.BlockSpec(memory_space=pl.ANY)] * 5,
        out_specs=pl.BlockSpec(memory_space=pltpu.VMEM),
        scratch_shapes=[
            pltpu.VMEM((depth, rows, lanes), jnp.float32),
            pltpu.VMEM((depth, rows, lanes), jnp.float32),
            pltpu.VMEM((rows, lanes), jnp.float32),
            pltpu.VMEM((MATERIALS, r_in, l_in), jnp.float32),
            pltpu.SemaphoreType.DMA((5,)),
        ],
        compiler_params=pltpu.CompilerParams(vmem_limit_bytes=48 * 1024 * 1024),
        cost_estimate=pl.CostEstimate(
            flops=int(cells * STEPS * 40 + d_in * r_in * l_in * 60),
            transcendentals=int(d_in * r_in * l_in * (MATERIALS + 1)),
            bytes_accessed=int(cells * 4 + (CHANNELS + 1) * r_in * l_in * 4),
        ),
    )(lim, prm, *pieces)


def shards(phase_field, centres, widths, densities, colours):
    depth_cells, row_cells, col_cells = phase_field.shape
    groups = lax.axis_size("gz")
    h = 1.0 / (depth_cells * groups)
    zblock = halo_stage(phase_field, ((0, "gz"),), STEPS)
    zlo, zhi = zblock("lo"), zblock("hi")
    deep = jnp.concatenate([zlo, phase_field, zhi], axis=0)
    plane = halo_stage(deep, ((1, "gx"), (2, "gy")), STEPS)
    rband = jnp.concatenate([plane("hi", "mid"), plane("lo", "mid")], axis=1)
    right = jnp.concatenate([plane("mid", "hi"), plane("hi", "hi"), plane("lo", "hi")], axis=1)
    left = jnp.concatenate([plane("mid", "lo"), plane("hi", "lo"), plane("lo", "lo")], axis=1)
    fill = jnp.zeros(right.shape[:2] + (LANES - col_cells - 2 * STEPS,), jnp.float32)
    cband = jnp.concatenate([right, fill, left], axis=2)

    z_lo = STEPS - lax.axis_index("gz") * depth_cells
    r_lo = -lax.axis_index("gx") * row_cells
    c_lo = -lax.axis_index("gy") * col_cells
    lim = jnp.stack(
        [
            z_lo,
            z_lo + depth_cells * groups,
            r_lo,
            r_lo + row_cells * lax.axis_size("gx"),
            c_lo,
            c_lo + col_cells * lax.axis_size("gy"),
        ]
    ).astype(jnp.int32)
    prm = jnp.concatenate([centres, widths, densities, colours.reshape(-1)]).astype(jnp.float32)

    seg = render_block((phase_field, zlo, zhi, rband, cband), lim, prm, (depth_cells, row_cells, col_cells), h)

    rows_part = row_cells // groups
    parts = seg.reshape(CHANNELS + 1, groups, rows_part, col_cells)
    got = lax.all_to_all(parts, "gz", 1, 1, tiled=True)
    prefix = jnp.zeros((rows_part, col_cells), jnp.float32)
    rad = jnp.zeros((CHANNELS, rows_part, col_cells), jnp.float32)
    for g in range(groups):
        rad = rad + jnp.exp(-h * prefix)[None] * got[:CHANNELS, g]
        prefix = prefix + got[CHANNELS, g]
    alpha = 1.0 - jnp.exp(-h * prefix)
    return jnp.concatenate([rad, alpha[None]], axis=0)


def solution(mesh):
    placed = (P("gz", "gx", "gy"), P(), P(), P(), P())
    return jax.shard_map(
        shards, mesh=mesh, in_specs=placed, out_specs=P(None, ("gx", "gz"), "gy"), check_vma=False
    )
```

```python
import functools
import itertools

import jax
import jax.numpy as jnp
from jax import lax
from jax.experimental import pallas as pl
from jax.experimental.pallas import tpu as pltpu
from jax.sharding import PartitionSpec as P

STEPS = 4
MATERIALS = 4
CHANNELS = 3

KAPPA = 0.5
RATE_DEPTH = 0.3
RATE_PLANE = 0.09
LANES = 256


def pick(cond, a, b):
    if isinstance(cond, bool):
        return a if cond else b
    return jnp.where(cond, a, b)


def axis_moves(axis):
    n = lax.axis_size(axis)
    if n == 1:
        return []
    if n == 2:
        me = lax.axis_index(axis)
        return [([(0, 1), (1, 0)], me == 0, me == 1)]
    up = [(i, i + 1) for i in range(n - 1)]
    down = [(i + 1, i) for i in range(n - 1)]
    return [(up, True, True), (down, False, False)]


def halo_stage(x, dim_axes, width):
    dims = [d for d, _ in dim_axes]
    axes = [a for _, a in dim_axes]
    sizes = [lax.axis_size(a) for a in axes]
    options = [[None] + axis_moves(a) for a in axes]
    blocks = {}
    for combo in itertools.product(*options):
        if all(m is None for m in combo):
            continue
        piece = x
        for d, m in zip(dims, combo):
            if m is not None:
                n_d = piece.shape[d]
                lo = lax.slice_in_dim(piece, 0, width, axis=d)
                hi = lax.slice_in_dim(piece, n_d - width, n_d, axis=d)
                piece = pick(m[1], hi, lo)
        used = [(a, s, m) for a, s, m in zip(axes, sizes, combo) if m is not None]
        pairs = []
        for parts in itertools.product(*[m[0] for _, _, m in used]):
            src = dst = 0
            for (_, s, _), (p, q) in zip(used, parts):
                src, dst = src * s + p, dst * s + q
            pairs.append((src, dst))
        got = lax.ppermute(piece, tuple(a for a, _, _ in used), pairs)
        landing = [(d, m[2]) for d, m in zip(dims, combo) if m is not None]
        for sides in itertools.product(("lo", "hi"), repeat=len(landing)):
            cond = True
            for (d, land_lo), side in zip(landing, sides):
                this = land_lo if side == "lo" else (not land_lo if isinstance(land_lo, bool) else ~land_lo)
                if isinstance(cond, bool) and isinstance(this, bool):
                    cond = cond and this
                elif isinstance(cond, bool):
                    cond = this if cond else False
                elif isinstance(this, bool):
                    cond = cond if this else False
                else:
                    cond = cond & this
            if cond is False:
                continue
            key = [None] * len(dims)
            for (d, _), side in zip(landing, sides):
                key[dims.index(d)] = side
            key = tuple(k or "mid" for k in key)
            val = got if cond is True else jnp.where(cond, got, 0.0)
            blocks[key] = val if key not in blocks else blocks[key] + val
    blocks[tuple("mid" for _ in dims)] = x

    def block(*key):
        if key in blocks:
            return blocks[key]
        shape = list(x.shape)
        for d, k in zip(dims, key):
            if k != "mid":
                shape[d] = width
        return jnp.zeros(shape, x.dtype)

    return block


def flux(d, rate):
    q = d * (1.0 / KAPPA)
    return rate * d / (1.0 + q * q)


def make_mask(lim_ref, m_ref, rows, lanes, r_in, l_in):
    row = lax.broadcasted_iota(jnp.int32, (rows, lanes), 0)
    lane = lax.broadcasted_iota(jnp.int32, (rows, lanes), 1)
    row_at = jnp.where(row < r_in + STEPS, row, row - rows)
    lane_at = jnp.where(lane < (l_in + lanes) // 2, lane, lane - lanes)
    ok = (row_at >= lim_ref[2]) & (row_at < lim_ref[3]) & (lane_at >= lim_ref[4]) & (lane_at < lim_ref[5])
    m_ref[...] = jnp.where(ok, 1.0, 0.0).astype(jnp.float32)


def smooth_planes(lim_ref, m_ref, src, dst, z0, z1):
    rows, lanes = m_ref.shape
    g0 = flux(src[z0] - src[z0 - 1], RATE_DEPTH)

    def body(z, g_prev):
        c = src[z]
        g = flux(src[z + 1] - c, RATE_DEPTH)
        fr = flux(pltpu.roll(c, rows - 1, 0) - c, RATE_PLANE)
        fc = flux(pltpu.roll(c, lanes - 1, 1) - c, RATE_PLANE)
        new = c + (g - g_prev) + (fr - pltpu.roll(fr, 1, 0)) + (fc - pltpu.roll(fc, 1, 1))
        inside = (z >= lim_ref[0]) & (z < lim_ref[1])
        zf = jnp.where(inside, 1.0, 0.0).astype(jnp.float32)
        dst[z] = new * (m_ref[...] * zf)
        return g

    lax.fori_loop(z0, z1, body, g0)


def scan_planes(prm_ref, src, acc_ref, run_ref, z0, z1, h):
    rows, lanes = src.shape[1:]
    r_in, l_in = run_ref.shape
    cen = [prm_ref[k] for k in range(MATERIALS)]
    wid = [prm_ref[MATERIALS + k] for k in range(MATERIALS)]
    den = [prm_ref[2 * MATERIALS + k] for k in range(MATERIALS)]
    run_ref[...] = jnp.zeros((r_in, l_in), jnp.float32)
    for k in range(MATERIALS):
        acc_ref[k] = jnp.zeros((r_in, l_in), jnp.float32)
    g0 = flux(src[z0, 0:r_in, 0:l_in] - src[z0 - 1, 0:r_in, 0:l_in], RATE_DEPTH)

    def final(z, g_prev):
        ci = src[z, 0:r_in, 0:l_in]
        g = flux(src[z + 1, 0:r_in, 0:l_in] - ci, RATE_DEPTH)
        c0 = src[z, :, 0:l_in]
        fr = flux(pltpu.roll(c0, rows - 1, 0) - c0, RATE_PLANE)
        cr = src[z, 0:r_in, :]
        fc = flux(pltpu.roll(cr, lanes - 1, 1) - cr, RATE_PLANE)
        v = ci + (g - g_prev) + (fr - pltpu.roll(fr, 1, 0))[0:r_in] + (fc - pltpu.roll(fc, 1, 1))[:, 0:l_in]
        bumps = [den[k] * jnp.exp(-(((v - cen[k]) / wid[k]) ** 2)) for k in range(MATERIALS)]
        ext = bumps[0] + bumps[1] + bumps[2] + bumps[3]
        run = run_ref[...]
        through = jnp.exp(-h * run)
        for k in range(MATERIALS):
            acc_ref[k] = acc_ref[k] + through * bumps[k]
        run_ref[...] = run + ext
        return g

    lax.fori_loop(z0, z1, final, g0)


def core_copies(x_hbm, rband_hbm, cband_hbm, b_ref, sem, lo, hi, at):
    r_in, l_in = x_hbm.shape[1:]
    rows, lanes = b_ref.shape[1:]
    p0, p1 = lo + STEPS, hi + STEPS
    return [
        pltpu.make_async_copy(x_hbm.at[lo:hi], b_ref.at[p0:p1, 0:r_in, 0:l_in], sem.at[at]),
        pltpu.make_async_copy(rband_hbm.at[lo:hi], b_ref.at[p0:p1, r_in:rows, 0:l_in], sem.at[at + 1]),
        pltpu.make_async_copy(cband_hbm.at[lo:hi], b_ref.at[p0:p1, :, l_in:lanes], sem.at[at + 2]),
    ]


def inner_kernel(lim_ref, prm_ref, x_hbm, rband_hbm, cband_hbm, ex_ref, part_ref, a_ref, b_ref, m_ref, sem, *, h):
    depth, rows, lanes = a_ref.shape
    d_in, r_in, l_in = x_hbm.shape
    copies = core_copies(x_hbm, rband_hbm, cband_hbm, b_ref, sem, 0, d_in, 0)
    for cp in copies:
        cp.start()
    make_mask(lim_ref, m_ref, rows, lanes, r_in, l_in)
    for cp in copies:
        cp.wait()
    e = STEPS
    smooth_planes(lim_ref, m_ref, b_ref, a_ref, e + 1, depth - e - 1)
    smooth_planes(lim_ref, m_ref, a_ref, b_ref, e + 2, depth - e - 2)
    smooth_planes(lim_ref, m_ref, b_ref, a_ref, e + 3, depth - e - 3)
    scan_planes(prm_ref, a_ref, part_ref.at[0:MATERIALS], part_ref.at[MATERIALS], e + 4, depth - e - 4, h)
    for s, src in ((0, a_ref), (1, b_ref), (2, a_ref)):
        for j, z in enumerate((e + 1 + s, e + 2 + s, depth - e - 3 - s, depth - e - 2 - s)):
            ex_ref[s, j] = src[z]


def outer_kernel(lim_ref, prm_ref, x_hbm, rband_hbm, cband_hbm, zlo_hbm, zhi_hbm, ex_hbm, part_ref,
                 out_ref, a_ref, b_ref, m_ref, acc_ref, run_ref, sem, *, h):
    depth, rows, lanes = a_ref.shape
    d_in, r_in, l_in = x_hbm.shape
    copies = core_copies(x_hbm, rband_hbm, cband_hbm, b_ref, sem, 0, 2, 0)
    copies += core_copies(x_hbm, rband_hbm, cband_hbm, b_ref, sem, d_in - 2, d_in, 3)
    copies.append(pltpu.make_async_copy(zlo_hbm, b_ref.at[0:STEPS], sem.at[6]))
    copies.append(pltpu.make_async_copy(zhi_hbm, b_ref.at[depth - STEPS:depth], sem.at[7]))
    for cp in copies:
        cp.start()
    make_mask(lim_ref, m_ref, rows, lanes, r_in, l_in)
    for cp in copies:
        cp.wait()
    e = STEPS
    bufs = (a_ref, b_ref, a_ref)
    srcs = (b_ref, a_ref, b_ref)
    for s in range(STEPS - 1):
        smooth_planes(lim_ref, m_ref, srcs[s], bufs[s], s + 1, s + 1 + STEPS)
        smooth_planes(lim_ref, m_ref, srcs[s], bufs[s], depth - STEPS - 1 - s, depth - 1 - s)
        for j, z in enumerate((e + 1 + s, e + 2 + s, depth - e - 3 - s, depth - e - 2 - s)):
            cp = pltpu.make_async_copy(ex_hbm.at[s, j], bufs[s].at[z], sem.at[8])
            cp.start()
            cp.wait()
    top = STEPS
    scan_planes(prm_ref, a_ref, acc_ref.at[0], run_ref.at[0], top, top + STEPS, h)
    scan_planes(prm_ref, a_ref, acc_ref.at[1], run_ref.at[1], depth - 2 * STEPS, depth - STEPS, h)
    s_lo, s_mid, s_hi = run_ref[0], part_ref[MATERIALS], run_ref[1]
    t_lo = jnp.exp(-h * s_lo)
    t_mid = jnp.exp(-h * (s_lo + s_mid))
    acc = [acc_ref[0, k] + t_lo * part_ref[k] + t_mid * acc_ref[1, k] for k in range(MATERIALS)]
    col = [[prm_ref[3 * MATERIALS + ch * MATERIALS + k] for k in range(MATERIALS)] for ch in range(CHANNELS)]
    for ch in range(CHANNELS):
        out_ref[ch] = h * (col[ch][0] * acc[0] + col[ch][1] * acc[1] + col[ch][2] * acc[2] + col[ch][3] * acc[3])
    out_ref[CHANNELS] = (s_lo + s_mid) + s_hi


def render_block(x, rband, cband, zlo, zhi, lim, prm, h):
    d_in, r_in, l_in = x.shape
    depth, rows, lanes = d_in + 2 * STEPS, r_in + 2 * STEPS, LANES
    cells = depth * rows * lanes
    smem = pl.BlockSpec(memory_space=pltpu.SMEM)
    anyspace = pl.BlockSpec(memory_space=pl.ANY)
    vmem = pl.BlockSpec(memory_space=pltpu.VMEM)
    params = pltpu.CompilerParams(vmem_limit_bytes=48 * 1024 * 1024)
    planes = [pltpu.VMEM((depth, rows, lanes), jnp.float32)] * 2 + [pltpu.VMEM((rows, lanes), jnp.float32)]
    inner_frac = (d_in - 2 * STEPS) / d_in
    ex, part = pl.pallas_call(
        functools.partial(inner_kernel, h=h),
        out_shape=(
            jax.ShapeDtypeStruct((STEPS - 1, 4, rows, lanes), jnp.float32),
            jax.ShapeDtypeStruct((MATERIALS + 1, r_in, l_in), jnp.float32),
        ),
        in_specs=[smem, smem, anyspace, anyspace, anyspace],
        out_specs=(vmem, vmem),
        scratch_shapes=planes + [pltpu.SemaphoreType.DMA((3,))],
        compiler_params=params,
        cost_estimate=pl.CostEstimate(
            flops=int(inner_frac * (cells * STEPS * 40 + d_in * r_in * l_in * 60)),
            transcendentals=int(inner_frac * d_in * r_in * l_in * (MATERIALS + 1)),
            bytes_accessed=int(cells * 4),
        ),
    )(lim, prm, x, rband, cband)
    return pl.pallas_call(
        functools.partial(outer_kernel, h=h),
        out_shape=jax.ShapeDtypeStruct((CHANNELS + 1, r_in, l_in), jnp.float32),
        in_specs=[smem, smem] + [anyspace] * 6 + [vmem],
        out_specs=vmem,
        scratch_shapes=planes + [
            pltpu.VMEM((2, MATERIALS, r_in, l_in), jnp.float32),
            pltpu.VMEM((2, r_in, l_in), jnp.float32),
            pltpu.SemaphoreType.DMA((9,)),
        ],
        compiler_params=params,
        cost_estimate=pl.CostEstimate(
            flops=int((1 - inner_frac) * (cells * STEPS * 40 + d_in * r_in * l_in * 60)),
            transcendentals=int((1 - inner_frac) * d_in * r_in * l_in * (MATERIALS + 1)),
            bytes_accessed=int(cells * 4 // 4),
        ),
    )(lim, prm, x, rband, cband, zlo, zhi, ex, part)


def shards(phase_field, centres, widths, densities, colours):
    depth_cells, row_cells, col_cells = phase_field.shape
    groups = lax.axis_size("gz")
    h = 1.0 / (depth_cells * groups)
    plane = halo_stage(phase_field, ((1, "gx"), (2, "gy")), STEPS)
    rband = jnp.concatenate([plane("hi", "mid"), plane("lo", "mid")], axis=1)
    right = jnp.concatenate([plane("mid", "hi"), plane("hi", "hi"), plane("lo", "hi")], axis=1)
    left = jnp.concatenate([plane("mid", "lo"), plane("hi", "lo"), plane("lo", "lo")], axis=1)
    fill = jnp.zeros(right.shape[:2] + (LANES - col_cells - 2 * STEPS,), jnp.float32)
    cband = jnp.concatenate([right, fill, left], axis=2)
    def face(lo, hi):
        core = jnp.concatenate([phase_field[lo:hi], rband[lo:hi]], axis=1)
        return jnp.concatenate([core, cband[lo:hi]], axis=2)

    lo_face, hi_face = face(0, STEPS), face(depth_cells - STEPS, depth_cells)
    zlo = jnp.zeros_like(lo_face)
    zhi = jnp.zeros_like(hi_face)
    for pairs, send_hi, land_lo in axis_moves("gz"):
        got = lax.ppermute(pick(send_hi, hi_face, lo_face), "gz", pairs)
        zlo = zlo + pick(land_lo, got, jnp.zeros_like(got))
        zhi = zhi + pick(land_lo, jnp.zeros_like(got), got)

    z_lo = STEPS - lax.axis_index("gz") * depth_cells
    r_lo = -lax.axis_index("gx") * row_cells
    c_lo = -lax.axis_index("gy") * col_cells
    lim = jnp.stack(
        [
            z_lo,
            z_lo + depth_cells * groups,
            r_lo,
            r_lo + row_cells * lax.axis_size("gx"),
            c_lo,
            c_lo + col_cells * lax.axis_size("gy"),
        ]
    ).astype(jnp.int32)
    prm = jnp.concatenate([centres, widths, densities, colours.reshape(-1)]).astype(jnp.float32)

    seg = render_block(phase_field, rband, cband, zlo, zhi, lim, prm, h)

    rows_part = row_cells // groups
    parts = seg.reshape(CHANNELS + 1, groups, rows_part, col_cells)
    got = lax.all_to_all(parts, "gz", 1, 1, tiled=True)
    prefix = jnp.zeros((rows_part, col_cells), jnp.float32)
    rad = jnp.zeros((CHANNELS, rows_part, col_cells), jnp.float32)
    for g in range(groups):
        rad = rad + jnp.exp(-h * prefix)[None] * got[:CHANNELS, g]
        prefix = prefix + got[CHANNELS, g]
    alpha = 1.0 - jnp.exp(-h * prefix)
    return jnp.concatenate([rad, alpha[None]], axis=0)


def solution(mesh):
    placed = (P("gz", "gx", "gy"), P(), P(), P(), P())
    return jax.shard_map(
        shards, mesh=mesh, in_specs=placed, out_specs=P(None, ("gx", "gz"), "gy"), check_vma=False
    )
```

```python
import functools
import itertools

import jax
import jax.numpy as jnp
from jax import lax
from jax.experimental import pallas as pl
from jax.experimental.pallas import tpu as pltpu
from jax.sharding import PartitionSpec as P


STEPS = 4
MATERIALS = 4
CHANNELS = 3

KAPPA = 0.5
RATE_DEPTH = 0.3
RATE_PLANE = 0.09
LANES = 256


def pick(cond, a, b):
    if isinstance(cond, bool):
        return a if cond else b
    return jnp.where(cond, a, b)


def axis_moves(axis):
    n = lax.axis_size(axis)
    if n == 1:
        return []
    if n == 2:
        me = lax.axis_index(axis)
        return [([(0, 1), (1, 0)], me == 0, me == 1)]
    up = [(i, i + 1) for i in range(n - 1)]
    down = [(i + 1, i) for i in range(n - 1)]
    return [(up, True, True), (down, False, False)]


def halo_stage(x, dim_axes, width):
    dims = [d for d, _ in dim_axes]
    axes = [a for _, a in dim_axes]
    sizes = [lax.axis_size(a) for a in axes]
    options = [[None] + axis_moves(a) for a in axes]
    blocks = {}
    for combo in itertools.product(*options):
        if all(m is None for m in combo):
            continue
        piece = x
        for d, m in zip(dims, combo):
            if m is not None:
                n_d = piece.shape[d]
                lo = lax.slice_in_dim(piece, 0, width, axis=d)
                hi = lax.slice_in_dim(piece, n_d - width, n_d, axis=d)
                piece = pick(m[1], hi, lo)
        used = [(a, s, m) for a, s, m in zip(axes, sizes, combo) if m is not None]
        pairs = []
        for parts in itertools.product(*[m[0] for _, _, m in used]):
            src = dst = 0
            for (_, s, _), (p, q) in zip(used, parts):
                src, dst = src * s + p, dst * s + q
            pairs.append((src, dst))
        got = lax.ppermute(piece, tuple(a for a, _, _ in used), pairs)
        landing = [(d, m[2]) for d, m in zip(dims, combo) if m is not None]
        for sides in itertools.product(("lo", "hi"), repeat=len(landing)):
            cond = True
            for (d, land_lo), side in zip(landing, sides):
                this = land_lo if side == "lo" else (not land_lo if isinstance(land_lo, bool) else ~land_lo)
                if isinstance(cond, bool) and isinstance(this, bool):
                    cond = cond and this
                elif isinstance(cond, bool):
                    cond = this if cond else False
                elif isinstance(this, bool):
                    cond = cond if this else False
                else:
                    cond = cond & this
            if cond is False:
                continue
            key = [None] * len(dims)
            for (d, _), side in zip(landing, sides):
                key[dims.index(d)] = side
            key = tuple(k or "mid" for k in key)
            val = got if cond is True else jnp.where(cond, got, 0.0)
            blocks[key] = val if key not in blocks else blocks[key] + val
    blocks[tuple("mid" for _ in dims)] = x

    def block(*key):
        if key in blocks:
            return blocks[key]
        shape = list(x.shape)
        for d, k in zip(dims, key):
            if k != "mid":
                shape[d] = width
        return jnp.zeros(shape, x.dtype)

    return block


def flux(d, rate):
    q = d * (1.0 / KAPPA)
    return rate * d / (1.0 + q * q)


def make_mask(lim_ref, m_ref, rows, lanes, r_in, l_in):
    row = lax.broadcasted_iota(jnp.int32, (rows, lanes), 0)
    lane = lax.broadcasted_iota(jnp.int32, (rows, lanes), 1)
    row_at = jnp.where(row < r_in + STEPS, row, row - rows)
    lane_at = jnp.where(lane < (l_in + lanes) // 2, lane, lane - lanes)
    ok = (row_at >= lim_ref[2]) & (row_at < lim_ref[3]) & (lane_at >= lim_ref[4]) & (lane_at < lim_ref[5])
    m_ref[...] = jnp.where(ok, 1.0, 0.0).astype(jnp.float32)


def smooth_planes(lim_ref, m_ref, src, dst, z0, z1):
    rows, lanes = m_ref.shape
    g0 = flux(src[z0] - src[z0 - 1], RATE_DEPTH)

    def body(z, g_prev):
        c = src[z]
        g = flux(src[z + 1] - c, RATE_DEPTH)
        fr = flux(pltpu.roll(c, rows - 1, 0) - c, RATE_PLANE)
        fc = flux(pltpu.roll(c, lanes - 1, 1) - c, RATE_PLANE)
        new = c + (g - g_prev) + (fr - pltpu.roll(fr, 1, 0)) + (fc - pltpu.roll(fc, 1, 1))
        inside = (z >= lim_ref[0]) & (z < lim_ref[1])
        zf = jnp.where(inside, 1.0, 0.0).astype(jnp.float32)
        dst[z] = new * (m_ref[...] * zf)
        return g

    lax.fori_loop(z0, z1, body, g0)


def scan_planes(prm_ref, src, acc_ref, run_ref, z0, z1, h):
    rows, lanes = src.shape[1:]
    r_in, l_in = run_ref.shape
    cen = [prm_ref[k] for k in range(MATERIALS)]
    wid = [prm_ref[MATERIALS + k] for k in range(MATERIALS)]
    den = [prm_ref[2 * MATERIALS + k] for k in range(MATERIALS)]
    run_ref[...] = jnp.zeros((r_in, l_in), jnp.float32)
    for k in range(MATERIALS):
        acc_ref[k] = jnp.zeros((r_in, l_in), jnp.float32)
    g0 = flux(src[z0, 0:r_in, 0:l_in] - src[z0 - 1, 0:r_in, 0:l_in], RATE_DEPTH)

    def final(z, g_prev):
        ci = src[z, 0:r_in, 0:l_in]
        g = flux(src[z + 1, 0:r_in, 0:l_in] - ci, RATE_DEPTH)
        c0 = src[z, :, 0:l_in]
        fr = flux(pltpu.roll(c0, rows - 1, 0) - c0, RATE_PLANE)
        cr = src[z, 0:r_in, :]
        fc = flux(pltpu.roll(cr, lanes - 1, 1) - cr, RATE_PLANE)
        v = ci + (g - g_prev) + (fr - pltpu.roll(fr, 1, 0))[0:r_in] + (fc - pltpu.roll(fc, 1, 1))[:, 0:l_in]
        bumps = [den[k] * jnp.exp(-(((v - cen[k]) / wid[k]) ** 2)) for k in range(MATERIALS)]
        ext = bumps[0] + bumps[1] + bumps[2] + bumps[3]
        run = run_ref[...]
        through = jnp.exp(-h * run)
        for k in range(MATERIALS):
            acc_ref[k] = acc_ref[k] + through * bumps[k]
        run_ref[...] = run + ext
        return g

    lax.fori_loop(z0, z1, final, g0)


def core_copies(x_hbm, rband_hbm, cband_hbm, b_ref, sem, lo, hi, at):
    r_in, l_in = x_hbm.shape[1:]
    rows, lanes = b_ref.shape[1:]
    p0, p1 = lo + STEPS, hi + STEPS
    return [
        pltpu.make_async_copy(x_hbm.at[lo:hi], b_ref.at[p0:p1, 0:r_in, 0:l_in], sem.at[at]),
        pltpu.make_async_copy(rband_hbm.at[lo:hi], b_ref.at[p0:p1, r_in:rows, 0:l_in], sem.at[at + 1]),
        pltpu.make_async_copy(cband_hbm.at[lo:hi], b_ref.at[p0:p1, :, l_in:lanes], sem.at[at + 2]),
    ]


def inner_kernel(lim_ref, prm_ref, x_hbm, rband_hbm, cband_hbm, ex_ref, part_ref, a_ref, b_ref, m_ref, sem, *, h):
    depth, rows, lanes = a_ref.shape
    d_in, r_in, l_in = x_hbm.shape
    copies = core_copies(x_hbm, rband_hbm, cband_hbm, b_ref, sem, 0, d_in, 0)
    for cp in copies:
        cp.start()
    make_mask(lim_ref, m_ref, rows, lanes, r_in, l_in)
    for cp in copies:
        cp.wait()
    e = STEPS
    smooth_planes(lim_ref, m_ref, b_ref, a_ref, e + 1, depth - e - 1)
    smooth_planes(lim_ref, m_ref, a_ref, b_ref, e + 2, depth - e - 2)
    smooth_planes(lim_ref, m_ref, b_ref, a_ref, e + 3, depth - e - 3)
    scan_planes(prm_ref, a_ref, part_ref.at[0:MATERIALS], part_ref.at[MATERIALS], e + 4, depth - e - 4, h)
    for s, src in ((0, a_ref), (1, b_ref), (2, a_ref)):
        for j, z in enumerate((e + 1 + s, e + 2 + s, depth - e - 3 - s, depth - e - 2 - s)):
            ex_ref[s, j] = src[z]


def outer_kernel(lim_ref, prm_ref, x_hbm, rband_hbm, cband_hbm, zlo_hbm, zhi_hbm, ex_hbm, part_ref,
                 out_ref, a_ref, b_ref, m_ref, acc_ref, run_ref, sem, *, h):
    depth, rows, lanes = a_ref.shape
    d_in, r_in, l_in = x_hbm.shape
    copies = core_copies(x_hbm, rband_hbm, cband_hbm, b_ref, sem, 0, 2, 0)
    copies += core_copies(x_hbm, rband_hbm, cband_hbm, b_ref, sem, d_in - 2, d_in, 3)
    copies.append(pltpu.make_async_copy(zlo_hbm, b_ref.at[0:STEPS], sem.at[6]))
    copies.append(pltpu.make_async_copy(zhi_hbm, b_ref.at[depth - STEPS:depth], sem.at[7]))
    for cp in copies:
        cp.start()
    make_mask(lim_ref, m_ref, rows, lanes, r_in, l_in)
    for cp in copies:
        cp.wait()
    e = STEPS
    bufs = (a_ref, b_ref, a_ref)
    srcs = (b_ref, a_ref, b_ref)
    for s in range(STEPS - 1):
        smooth_planes(lim_ref, m_ref, srcs[s], bufs[s], s + 1, s + 1 + STEPS)
        smooth_planes(lim_ref, m_ref, srcs[s], bufs[s], depth - STEPS - 1 - s, depth - 1 - s)
        for j, z in enumerate((e + 1 + s, e + 2 + s, depth - e - 3 - s, depth - e - 2 - s)):
            cp = pltpu.make_async_copy(ex_hbm.at[s, j], bufs[s].at[z], sem.at[8])
            cp.start()
            cp.wait()
    top = STEPS
    scan_planes(prm_ref, a_ref, acc_ref.at[0], run_ref.at[0], top, top + STEPS, h)
    scan_planes(prm_ref, a_ref, acc_ref.at[1], run_ref.at[1], depth - 2 * STEPS, depth - STEPS, h)
    s_lo, s_mid, s_hi = run_ref[0], part_ref[MATERIALS], run_ref[1]
    t_lo = jnp.exp(-h * s_lo)
    t_mid = jnp.exp(-h * (s_lo + s_mid))
    acc = [acc_ref[0, k] + t_lo * part_ref[k] + t_mid * acc_ref[1, k] for k in range(MATERIALS)]
    col = [[prm_ref[3 * MATERIALS + ch * MATERIALS + k] for k in range(MATERIALS)] for ch in range(CHANNELS)]
    for ch in range(CHANNELS):
        out_ref[ch] = h * (col[ch][0] * acc[0] + col[ch][1] * acc[1] + col[ch][2] * acc[2] + col[ch][3] * acc[3])
    out_ref[CHANNELS] = (s_lo + s_mid) + s_hi


def render_block(x, rband, cband, zlo, zhi, lim, prm, h):
    d_in, r_in, l_in = x.shape
    depth, rows, lanes = d_in + 2 * STEPS, r_in + 2 * STEPS, LANES
    cells = depth * rows * lanes
    smem = pl.BlockSpec(memory_space=pltpu.SMEM)
    anyspace = pl.BlockSpec(memory_space=pl.ANY)
    vmem = pl.BlockSpec(memory_space=pltpu.VMEM)
    params = pltpu.CompilerParams(vmem_limit_bytes=48 * 1024 * 1024)
    planes = [pltpu.VMEM((depth, rows, lanes), jnp.float32)] * 2 + [pltpu.VMEM((rows, lanes), jnp.float32)]
    inner_frac = (d_in - 2 * STEPS) / d_in
    inner_call = pl.pallas_call(
        functools.partial(inner_kernel, h=h),
        out_shape=(
            jax.ShapeDtypeStruct((STEPS - 1, 4, rows, lanes), jnp.float32),
            jax.ShapeDtypeStruct((MATERIALS + 1, r_in, l_in), jnp.float32),
        ),
        in_specs=[smem, smem, anyspace, anyspace, anyspace],
        out_specs=(vmem, vmem),
        scratch_shapes=planes + [pltpu.SemaphoreType.DMA((3,))],
        compiler_params=params,
        cost_estimate=pl.CostEstimate(
            flops=int(inner_frac * (cells * STEPS * 40 + d_in * r_in * l_in * 60)),
            transcendentals=int(inner_frac * d_in * r_in * l_in * (MATERIALS + 1)),
            bytes_accessed=int(cells * 4),
        ),
    )
    outer_call = pl.pallas_call(
        functools.partial(outer_kernel, h=h),
        out_shape=jax.ShapeDtypeStruct((CHANNELS + 1, r_in, l_in), jnp.float32),
        in_specs=[smem, smem] + [anyspace] * 6 + [vmem],
        out_specs=vmem,
        scratch_shapes=planes + [
            pltpu.VMEM((2, MATERIALS, r_in, l_in), jnp.float32),
            pltpu.VMEM((2, r_in, l_in), jnp.float32),
            pltpu.SemaphoreType.DMA((9,)),
        ],
        compiler_params=params,
        cost_estimate=pl.CostEstimate(
            flops=int((1 - inner_frac) * (cells * STEPS * 40 + d_in * r_in * l_in * 60)),
            transcendentals=int((1 - inner_frac) * d_in * r_in * l_in * (MATERIALS + 1)),
            bytes_accessed=int(cells * 4 // 4),
        ),
    )
    ex, part = inner_call(lim, prm, x, rband, cband)
    return outer_call(lim, prm, x, rband, cband, zlo, zhi, ex, part)


def shards_body(phase_field, centres, widths, densities, colours):
    depth_cells, row_cells, col_cells = phase_field.shape
    groups = lax.axis_size("gz")
    h = 1.0 / (depth_cells * groups)

    def bands(x):
        plane = halo_stage(x, ((1, "gx"), (2, "gy")), STEPS)
        rb = jnp.concatenate([plane("hi", "mid"), plane("lo", "mid")], axis=1)
        right = jnp.concatenate([plane("mid", "hi"), plane("hi", "hi"), plane("lo", "hi")], axis=1)
        left = jnp.concatenate([plane("mid", "lo"), plane("hi", "lo"), plane("lo", "lo")], axis=1)
        fill = jnp.zeros(right.shape[:2] + (LANES - col_cells - 2 * STEPS,), jnp.float32)
        return rb, jnp.concatenate([right, fill, left], axis=2)

    rband, cband = bands(phase_field)
    zcore = halo_stage(phase_field, ((0, "gz"),), STEPS)
    zlo_c, zhi_c = zcore("lo"), zcore("hi")
    rband_z, cband_z = bands(jnp.concatenate([zlo_c, zhi_c], axis=0))

    def face(core, rb, cb):
        return jnp.concatenate([jnp.concatenate([core, rb], axis=1), cb], axis=2)

    zlo = face(zlo_c, rband_z[:STEPS], cband_z[:STEPS])
    zhi = face(zhi_c, rband_z[STEPS:], cband_z[STEPS:])

    z_lo = STEPS - lax.axis_index("gz") * depth_cells
    r_lo = -lax.axis_index("gx") * row_cells
    c_lo = -lax.axis_index("gy") * col_cells
    lim = jnp.stack(
        [
            z_lo,
            z_lo + depth_cells * groups,
            r_lo,
            r_lo + row_cells * lax.axis_size("gx"),
            c_lo,
            c_lo + col_cells * lax.axis_size("gy"),
        ]
    ).astype(jnp.int32)
    prm = jnp.concatenate([centres, widths, densities, colours.reshape(-1)]).astype(jnp.float32)

    seg = render_block(phase_field, rband, cband, zlo, zhi, lim, prm, h)

    rows_part = row_cells // groups
    parts = seg.reshape(CHANNELS + 1, groups, rows_part, col_cells)
    got = lax.all_to_all(parts, "gz", 1, 1, tiled=True)
    prefix = jnp.zeros((rows_part, col_cells), jnp.float32)
    rad = jnp.zeros((CHANNELS, rows_part, col_cells), jnp.float32)
    for g in range(groups):
        rad = rad + jnp.exp(-h * prefix)[None] * got[:CHANNELS, g]
        prefix = prefix + got[CHANNELS, g]
    alpha = 1.0 - jnp.exp(-h * prefix)
    return jnp.concatenate([rad, alpha[None]], axis=0)


def solution(mesh):
    placed = (P("gz", "gx", "gy"), P(), P(), P(), P())
    return jax.shard_map(
        shards_body, mesh=mesh, in_specs=placed, out_specs=P(None, ("gx", "gz"), "gy"), check_vma=False
    )
```

```python
import functools
import itertools

import jax
import jax.numpy as jnp
from jax import lax
from jax.experimental import pallas as pl
from jax.experimental.pallas import tpu as pltpu
from jax.sharding import PartitionSpec as P

STEPS = 4
MATERIALS = 4
CHANNELS = 3

KAPPA = 0.5
RATE_DEPTH = 0.3
RATE_PLANE = 0.09
LANES = 256


def pick(cond, a, b):
    if isinstance(cond, bool):
        return a if cond else b
    return jnp.where(cond, a, b)


def axis_moves(axis):
    n = lax.axis_size(axis)
    if n == 1:
        return []
    if n == 2:
        me = lax.axis_index(axis)
        return [([(0, 1), (1, 0)], me == 0, me == 1)]
    up = [(i, i + 1) for i in range(n - 1)]
    down = [(i + 1, i) for i in range(n - 1)]
    return [(up, True, True), (down, False, False)]


def halo_stage(x, dim_axes, width):
    dims = [d for d, _ in dim_axes]
    axes = [a for _, a in dim_axes]
    sizes = [lax.axis_size(a) for a in axes]
    options = [[None] + axis_moves(a) for a in axes]
    blocks = {}
    for combo in itertools.product(*options):
        if all(m is None for m in combo):
            continue
        piece = x
        for d, m in zip(dims, combo):
            if m is not None:
                n_d = piece.shape[d]
                lo = lax.slice_in_dim(piece, 0, width, axis=d)
                hi = lax.slice_in_dim(piece, n_d - width, n_d, axis=d)
                piece = pick(m[1], hi, lo)
        used = [(a, s, m) for a, s, m in zip(axes, sizes, combo) if m is not None]
        pairs = []
        for parts in itertools.product(*[m[0] for _, _, m in used]):
            src = dst = 0
            for (_, s, _), (p, q) in zip(used, parts):
                src, dst = src * s + p, dst * s + q
            pairs.append((src, dst))
        narrow = piece.ndim == 3 and piece.shape[2] == width and piece.shape[1] > width
        if narrow:
            piece = jnp.transpose(piece, (2, 0, 1))
        got = lax.ppermute(piece, tuple(a for a, _, _ in used), pairs)
        if narrow:
            got = jnp.transpose(got, (1, 2, 0))
        landing = [(d, m[2]) for d, m in zip(dims, combo) if m is not None]
        for sides in itertools.product(("lo", "hi"), repeat=len(landing)):
            cond = True
            for (d, land_lo), side in zip(landing, sides):
                this = land_lo if side == "lo" else (not land_lo if isinstance(land_lo, bool) else ~land_lo)
                if isinstance(cond, bool) and isinstance(this, bool):
                    cond = cond and this
                elif isinstance(cond, bool):
                    cond = this if cond else False
                elif isinstance(this, bool):
                    cond = cond if this else False
                else:
                    cond = cond & this
            if cond is False:
                continue
            key = [None] * len(dims)
            for (d, _), side in zip(landing, sides):
                key[dims.index(d)] = side
            key = tuple(k or "mid" for k in key)
            val = got if cond is True else jnp.where(cond, got, 0.0)
            blocks[key] = val if key not in blocks else blocks[key] + val
    blocks[tuple("mid" for _ in dims)] = x

    def block(*key):
        if key in blocks:
            return blocks[key]
        shape = list(x.shape)
        for d, k in zip(dims, key):
            if k != "mid":
                shape[d] = width
        return jnp.zeros(shape, x.dtype)

    return block


def flux(d, rate):
    q = d * (1.0 / KAPPA)
    return rate * d / (1.0 + q * q)


def render_kernel(lim_ref, prm_ref, x_hbm, zlo_hbm, zhi_hbm, rband_hbm, cband_hbm, out_ref, a_ref, b_ref, m_ref, acc_ref, sem,
                  *, interior, h):
    depth, rows, lanes = a_ref.shape
    d_in, r_in, l_in = interior
    halo = STEPS
    copies = [
        pltpu.make_async_copy(x_hbm, b_ref.at[halo:halo + d_in, 0:r_in, 0:l_in], sem.at[0]),
        pltpu.make_async_copy(zlo_hbm, b_ref.at[0:halo, 0:r_in, 0:l_in], sem.at[1]),
        pltpu.make_async_copy(zhi_hbm, b_ref.at[halo + d_in:depth, 0:r_in, 0:l_in], sem.at[2]),
        pltpu.make_async_copy(rband_hbm, b_ref.at[:, r_in:rows, 0:l_in], sem.at[3]),
        pltpu.make_async_copy(cband_hbm, b_ref.at[:, :, l_in:lanes], sem.at[4]),
    ]
    for cp in copies:
        cp.start()

    row = lax.broadcasted_iota(jnp.int32, (rows, lanes), 0)
    lane = lax.broadcasted_iota(jnp.int32, (rows, lanes), 1)
    row_at = jnp.where(row < r_in + halo, row, row - rows)
    lane_at = jnp.where(lane < (l_in + lanes) // 2, lane, lane - lanes)
    ok = (row_at >= lim_ref[2]) & (row_at < lim_ref[3]) & (lane_at >= lim_ref[4]) & (lane_at < lim_ref[5])
    m_ref[...] = jnp.where(ok, 1.0, 0.0).astype(jnp.float32)

    cen = [prm_ref[k] for k in range(MATERIALS)]
    wid = [prm_ref[MATERIALS + k] for k in range(MATERIALS)]
    den = [prm_ref[2 * MATERIALS + k] for k in range(MATERIALS)]
    col = [[prm_ref[3 * MATERIALS + ch * MATERIALS + k] for k in range(MATERIALS)] for ch in range(CHANNELS)]
    out_ref[CHANNELS] = jnp.zeros((r_in, l_in), jnp.float32)
    for k in range(MATERIALS):
        acc_ref[k] = jnp.zeros((r_in, l_in), jnp.float32)

    for cp in copies:
        cp.wait()

    def smooth(src, dst, s):
        z0, z1 = s + 1, depth - 1 - s
        g0 = flux(src[z0] - src[z0 - 1], RATE_DEPTH)

        def body(z, g_prev):
            c = src[z]
            g = flux(src[z + 1] - c, RATE_DEPTH)
            fr = flux(pltpu.roll(c, rows - 1, 0) - c, RATE_PLANE)
            fc = flux(pltpu.roll(c, lanes - 1, 1) - c, RATE_PLANE)
            new = c + (g - g_prev) + (fr - pltpu.roll(fr, 1, 0)) + (fc - pltpu.roll(fc, 1, 1))
            inside = (z >= lim_ref[0]) & (z < lim_ref[1])
            zf = jnp.where(inside, 1.0, 0.0).astype(jnp.float32)
            dst[z] = new * (m_ref[...] * zf)
            return g

        lax.fori_loop(z0, z1, body, g0)

    smooth(b_ref, a_ref, 0)
    smooth(a_ref, b_ref, 1)
    smooth(b_ref, a_ref, 2)

    z0, z1 = halo, halo + d_in
    g0 = flux(a_ref[z0, 0:r_in, 0:l_in] - a_ref[z0 - 1, 0:r_in, 0:l_in], RATE_DEPTH)

    def final(z, g_prev):
        ci = a_ref[z, 0:r_in, 0:l_in]
        g = flux(a_ref[z + 1, 0:r_in, 0:l_in] - ci, RATE_DEPTH)
        c0 = a_ref[z, :, 0:l_in]
        fr = flux(pltpu.roll(c0, rows - 1, 0) - c0, RATE_PLANE)
        cr = a_ref[z, 0:r_in, :]
        fc = flux(pltpu.roll(cr, lanes - 1, 1) - cr, RATE_PLANE)
        v = ci + (g - g_prev) + (fr - pltpu.roll(fr, 1, 0))[0:r_in] + (fc - pltpu.roll(fc, 1, 1))[:, 0:l_in]
        bumps = [den[k] * jnp.exp(-(((v - cen[k]) / wid[k]) ** 2)) for k in range(MATERIALS)]
        ext = bumps[0] + bumps[1] + bumps[2] + bumps[3]
        run = out_ref[CHANNELS]
        through = jnp.exp(-h * run)
        for k in range(MATERIALS):
            acc_ref[k] = acc_ref[k] + through * bumps[k]
        out_ref[CHANNELS] = run + ext
        return g

    lax.fori_loop(z0, z1, final, g0)
    for ch in range(CHANNELS):
        emit = col[ch][0] * acc_ref[0] + col[ch][1] * acc_ref[1] + col[ch][2] * acc_ref[2] + col[ch][3] * acc_ref[3]
        out_ref[ch] = h * emit


def render_block(pieces, lim, prm, interior, h):
    d_in, r_in, l_in = interior
    depth, rows, lanes = d_in + 2 * STEPS, r_in + 2 * STEPS, LANES
    cells = depth * rows * lanes
    kernel = functools.partial(render_kernel, interior=interior, h=h)
    return pl.pallas_call(
        kernel,
        out_shape=jax.ShapeDtypeStruct((CHANNELS + 1, r_in, l_in), jnp.float32),
        in_specs=[pl.BlockSpec(memory_space=pltpu.SMEM)] * 2 + [pl.BlockSpec(memory_space=pl.ANY)] * 5,
        out_specs=pl.BlockSpec(memory_space=pltpu.VMEM),
        scratch_shapes=[
            pltpu.VMEM((depth, rows, lanes), jnp.float32),
            pltpu.VMEM((depth, rows, lanes), jnp.float32),
            pltpu.VMEM((rows, lanes), jnp.float32),
            pltpu.VMEM((MATERIALS, r_in, l_in), jnp.float32),
            pltpu.SemaphoreType.DMA((5,)),
        ],
        compiler_params=pltpu.CompilerParams(vmem_limit_bytes=48 * 1024 * 1024),
        cost_estimate=pl.CostEstimate(
            flops=int(cells * STEPS * 40 + d_in * r_in * l_in * 60),
            transcendentals=int(d_in * r_in * l_in * (MATERIALS + 1)),
            bytes_accessed=int(cells * 4 + (CHANNELS + 1) * r_in * l_in * 4),
        ),
    )(lim, prm, *pieces)


def shards(phase_field, centres, widths, densities, colours):
    depth_cells, row_cells, col_cells = phase_field.shape
    groups = lax.axis_size("gz")
    h = 1.0 / (depth_cells * groups)
    zblock = halo_stage(phase_field, ((0, "gz"),), STEPS)
    zlo, zhi = zblock("lo"), zblock("hi")
    deep = jnp.concatenate([zlo, phase_field, zhi], axis=0)
    plane = halo_stage(deep, ((1, "gx"), (2, "gy")), STEPS)
    rband = jnp.concatenate([plane("hi", "mid"), plane("lo", "mid")], axis=1)
    right = jnp.concatenate([plane("mid", "hi"), plane("hi", "hi"), plane("lo", "hi")], axis=1)
    left = jnp.concatenate([plane("mid", "lo"), plane("hi", "lo"), plane("lo", "lo")], axis=1)
    fill = jnp.zeros(right.shape[:2] + (LANES - col_cells - 2 * STEPS,), jnp.float32)
    cband = jnp.concatenate([right, fill, left], axis=2)

    z_lo = STEPS - lax.axis_index("gz") * depth_cells
    r_lo = -lax.axis_index("gx") * row_cells
    c_lo = -lax.axis_index("gy") * col_cells
    lim = jnp.stack(
        [
            z_lo,
            z_lo + depth_cells * groups,
            r_lo,
            r_lo + row_cells * lax.axis_size("gx"),
            c_lo,
            c_lo + col_cells * lax.axis_size("gy"),
        ]
    ).astype(jnp.int32)
    prm = jnp.concatenate([centres, widths, densities, colours.reshape(-1)]).astype(jnp.float32)

    seg = render_block((phase_field, zlo, zhi, rband, cband), lim, prm, (depth_cells, row_cells, col_cells), h)

    rows_part = row_cells // groups
    parts = seg.reshape(CHANNELS + 1, groups, rows_part, col_cells)
    got = lax.all_to_all(parts, "gz", 1, 1, tiled=True)
    prefix = jnp.zeros((rows_part, col_cells), jnp.float32)
    rad = jnp.zeros((CHANNELS, rows_part, col_cells), jnp.float32)
    for g in range(groups):
        rad = rad + jnp.exp(-h * prefix)[None] * got[:CHANNELS, g]
        prefix = prefix + got[CHANNELS, g]
    alpha = 1.0 - jnp.exp(-h * prefix)
    return jnp.concatenate([rad, alpha[None]], axis=0)


def solution(mesh):
    placed = (P("gz", "gx", "gy"), P(), P(), P(), P())
    return jax.shard_map(
        shards, mesh=mesh, in_specs=placed, out_specs=P(None, ("gx", "gz"), "gy"), check_vma=False
    )
```

```python
import functools
import itertools

import jax
import jax.numpy as jnp
from jax import lax
from jax.experimental import pallas as pl
from jax.experimental.pallas import tpu as pltpu
from jax.sharding import PartitionSpec as P

STEPS = 4
MATERIALS = 4
CHANNELS = 3

KAPPA = 0.5
RATE_DEPTH = 0.3
RATE_PLANE = 0.09
LANES = 256


def pick(cond, a, b):
    if isinstance(cond, bool):
        return a if cond else b
    return jnp.where(cond, a, b)


def axis_moves(axis):
    n = lax.axis_size(axis)
    if n == 1:
        return []
    if n == 2:
        me = lax.axis_index(axis)
        return [([(0, 1), (1, 0)], me == 0, me == 1)]
    up = [(i, i + 1) for i in range(n - 1)]
    down = [(i + 1, i) for i in range(n - 1)]
    return [(up, True, True), (down, False, False)]


def halo_stage(x, dim_axes, width):
    dims = [d for d, _ in dim_axes]
    axes = [a for _, a in dim_axes]
    sizes = [lax.axis_size(a) for a in axes]
    options = [[None] + axis_moves(a) for a in axes]
    blocks = {}
    for combo in itertools.product(*options):
        if all(m is None for m in combo):
            continue
        piece = x
        for d, m in zip(dims, combo):
            if m is not None:
                n_d = piece.shape[d]
                lo = lax.slice_in_dim(piece, 0, width, axis=d)
                hi = lax.slice_in_dim(piece, n_d - width, n_d, axis=d)
                piece = pick(m[1], hi, lo)
        used = [(a, s, m) for a, s, m in zip(axes, sizes, combo) if m is not None]
        pairs = []
        for parts in itertools.product(*[m[0] for _, _, m in used]):
            src = dst = 0
            for (_, s, _), (p, q) in zip(used, parts):
                src, dst = src * s + p, dst * s + q
            pairs.append((src, dst))
        narrow = piece.ndim == 3 and piece.shape[2] == width and piece.shape[1] > width
        if narrow:
            piece = jnp.transpose(piece, (2, 0, 1))
        got = lax.ppermute(piece, tuple(a for a, _, _ in used), pairs)
        if narrow:
            got = jnp.transpose(got, (1, 2, 0))
        landing = [(d, m[2]) for d, m in zip(dims, combo) if m is not None]
        for sides in itertools.product(("lo", "hi"), repeat=len(landing)):
            cond = True
            for (d, land_lo), side in zip(landing, sides):
                this = land_lo if side == "lo" else (not land_lo if isinstance(land_lo, bool) else ~land_lo)
                if isinstance(cond, bool) and isinstance(this, bool):
                    cond = cond and this
                elif isinstance(cond, bool):
                    cond = this if cond else False
                elif isinstance(this, bool):
                    cond = cond if this else False
                else:
                    cond = cond & this
            if cond is False:
                continue
            key = [None] * len(dims)
            for (d, _), side in zip(landing, sides):
                key[dims.index(d)] = side
            key = tuple(k or "mid" for k in key)
            val = got if cond is True else jnp.where(cond, got, 0.0)
            blocks[key] = val if key not in blocks else blocks[key] + val
    blocks[tuple("mid" for _ in dims)] = x

    def block(*key):
        if key in blocks:
            return blocks[key]
        shape = list(x.shape)
        for d, k in zip(dims, key):
            if k != "mid":
                shape[d] = width
        return jnp.zeros(shape, x.dtype)

    return block


def flux(d, rate):
    q = d * (1.0 / KAPPA)
    return rate * d / (1.0 + q * q)


def render_kernel(lim_ref, prm_ref, x_hbm, zlo_hbm, zhi_hbm, rband_hbm, cband_hbm, out_ref, a_ref, b_ref, m_ref, acc_ref, sem,
                  *, interior, h):
    depth, rows, lanes = a_ref.shape
    d_in, r_in, l_in = interior
    halo = STEPS
    copies = [
        pltpu.make_async_copy(x_hbm, b_ref.at[halo:halo + d_in, 0:r_in, 0:l_in], sem.at[0]),
        pltpu.make_async_copy(zlo_hbm, b_ref.at[0:halo, 0:r_in, 0:l_in], sem.at[1]),
        pltpu.make_async_copy(zhi_hbm, b_ref.at[halo + d_in:depth, 0:r_in, 0:l_in], sem.at[2]),
        pltpu.make_async_copy(rband_hbm, b_ref.at[:, r_in:rows, 0:l_in], sem.at[3]),
        pltpu.make_async_copy(cband_hbm, b_ref.at[:, :, l_in:lanes], sem.at[4]),
    ]
    for cp in copies:
        cp.start()

    row = lax.broadcasted_iota(jnp.int32, (rows, lanes), 0)
    lane = lax.broadcasted_iota(jnp.int32, (rows, lanes), 1)
    row_at = jnp.where(row < r_in + halo, row, row - rows)
    lane_at = jnp.where(lane < (l_in + lanes) // 2, lane, lane - lanes)
    ok = (row_at >= lim_ref[2]) & (row_at < lim_ref[3]) & (lane_at >= lim_ref[4]) & (lane_at < lim_ref[5])
    m_ref[...] = jnp.where(ok, 1.0, 0.0).astype(jnp.float32)

    cen = [prm_ref[k] for k in range(MATERIALS)]
    wid = [prm_ref[MATERIALS + k] for k in range(MATERIALS)]
    den = [prm_ref[2 * MATERIALS + k] for k in range(MATERIALS)]
    col = [[prm_ref[3 * MATERIALS + ch * MATERIALS + k] for k in range(MATERIALS)] for ch in range(CHANNELS)]
    out_ref[CHANNELS] = jnp.zeros((r_in, l_in), jnp.float32)
    for k in range(MATERIALS):
        acc_ref[k] = jnp.zeros((r_in, l_in), jnp.float32)

    for cp in copies:
        cp.wait()

    def smooth(src, dst, s):
        z0, z1 = s + 1, depth - 1 - s
        g0 = flux(src[z0] - src[z0 - 1], RATE_DEPTH)

        def body(z, g_prev):
            c = src[z]
            g = flux(src[z + 1] - c, RATE_DEPTH)
            fr = flux(pltpu.roll(c, rows - 1, 0) - c, RATE_PLANE)
            fc = flux(pltpu.roll(c, lanes - 1, 1) - c, RATE_PLANE)
            new = c + (g - g_prev) + (fr - pltpu.roll(fr, 1, 0)) + (fc - pltpu.roll(fc, 1, 1))
            inside = (z >= lim_ref[0]) & (z < lim_ref[1])
            zf = jnp.where(inside, 1.0, 0.0).astype(jnp.float32)
            dst[z] = new * (m_ref[...] * zf)
            return g

        lax.fori_loop(z0, z1, body, g0, unroll=4)

    smooth(b_ref, a_ref, 0)
    smooth(a_ref, b_ref, 1)
    smooth(b_ref, a_ref, 2)

    z0, z1 = halo, halo + d_in
    g0 = flux(a_ref[z0, 0:r_in, 0:l_in] - a_ref[z0 - 1, 0:r_in, 0:l_in], RATE_DEPTH)

    def final(z, g_prev):
        ci = a_ref[z, 0:r_in, 0:l_in]
        g = flux(a_ref[z + 1, 0:r_in, 0:l_in] - ci, RATE_DEPTH)
        c0 = a_ref[z, :, 0:l_in]
        fr = flux(pltpu.roll(c0, rows - 1, 0) - c0, RATE_PLANE)
        cr = a_ref[z, 0:r_in, :]
        fc = flux(pltpu.roll(cr, lanes - 1, 1) - cr, RATE_PLANE)
        v = ci + (g - g_prev) + (fr - pltpu.roll(fr, 1, 0))[0:r_in] + (fc - pltpu.roll(fc, 1, 1))[:, 0:l_in]
        bumps = [den[k] * jnp.exp(-(((v - cen[k]) / wid[k]) ** 2)) for k in range(MATERIALS)]
        ext = bumps[0] + bumps[1] + bumps[2] + bumps[3]
        run = out_ref[CHANNELS]
        through = jnp.exp(-h * run)
        for k in range(MATERIALS):
            acc_ref[k] = acc_ref[k] + through * bumps[k]
        out_ref[CHANNELS] = run + ext
        return g

    lax.fori_loop(z0, z1, final, g0, unroll=2)
    for ch in range(CHANNELS):
        emit = col[ch][0] * acc_ref[0] + col[ch][1] * acc_ref[1] + col[ch][2] * acc_ref[2] + col[ch][3] * acc_ref[3]
        out_ref[ch] = h * emit


def render_block(pieces, lim, prm, interior, h):
    d_in, r_in, l_in = interior
    depth, rows, lanes = d_in + 2 * STEPS, r_in + 2 * STEPS, LANES
    cells = depth * rows * lanes
    kernel = functools.partial(render_kernel, interior=interior, h=h)
    return pl.pallas_call(
        kernel,
        out_shape=jax.ShapeDtypeStruct((CHANNELS + 1, r_in, l_in), jnp.float32),
        in_specs=[pl.BlockSpec(memory_space=pltpu.SMEM)] * 2 + [pl.BlockSpec(memory_space=pl.ANY)] * 5,
        out_specs=pl.BlockSpec(memory_space=pltpu.VMEM),
        scratch_shapes=[
            pltpu.VMEM((depth, rows, lanes), jnp.float32),
            pltpu.VMEM((depth, rows, lanes), jnp.float32),
            pltpu.VMEM((rows, lanes), jnp.float32),
            pltpu.VMEM((MATERIALS, r_in, l_in), jnp.float32),
            pltpu.SemaphoreType.DMA((5,)),
        ],
        compiler_params=pltpu.CompilerParams(vmem_limit_bytes=48 * 1024 * 1024),
        cost_estimate=pl.CostEstimate(
            flops=int(cells * STEPS * 40 + d_in * r_in * l_in * 60),
            transcendentals=int(d_in * r_in * l_in * (MATERIALS + 1)),
            bytes_accessed=int(cells * 4 + (CHANNELS + 1) * r_in * l_in * 4),
        ),
    )(lim, prm, *pieces)


def shards(phase_field, centres, widths, densities, colours):
    depth_cells, row_cells, col_cells = phase_field.shape
    groups = lax.axis_size("gz")
    h = 1.0 / (depth_cells * groups)
    zblock = halo_stage(phase_field, ((0, "gz"),), STEPS)
    zlo, zhi = zblock("lo"), zblock("hi")
    deep = jnp.concatenate([zlo, phase_field, zhi], axis=0)
    plane = halo_stage(deep, ((1, "gx"), (2, "gy")), STEPS)
    rband = jnp.concatenate([plane("hi", "mid"), plane("lo", "mid")], axis=1)
    right = jnp.concatenate([plane("mid", "hi"), plane("hi", "hi"), plane("lo", "hi")], axis=1)
    left = jnp.concatenate([plane("mid", "lo"), plane("hi", "lo"), plane("lo", "lo")], axis=1)
    fill = jnp.zeros(right.shape[:2] + (LANES - col_cells - 2 * STEPS,), jnp.float32)
    cband = jnp.concatenate([right, fill, left], axis=2)

    z_lo = STEPS - lax.axis_index("gz") * depth_cells
    r_lo = -lax.axis_index("gx") * row_cells
    c_lo = -lax.axis_index("gy") * col_cells
    lim = jnp.stack(
        [
            z_lo,
            z_lo + depth_cells * groups,
            r_lo,
            r_lo + row_cells * lax.axis_size("gx"),
            c_lo,
            c_lo + col_cells * lax.axis_size("gy"),
        ]
    ).astype(jnp.int32)
    prm = jnp.concatenate([centres, widths, densities, colours.reshape(-1)]).astype(jnp.float32)

    seg = render_block((phase_field, zlo, zhi, rband, cband), lim, prm, (depth_cells, row_cells, col_cells), h)

    rows_part = row_cells // groups
    parts = seg.reshape(CHANNELS + 1, groups, rows_part, col_cells)
    got = lax.all_to_all(parts, "gz", 1, 1, tiled=True)
    prefix = jnp.zeros((rows_part, col_cells), jnp.float32)
    rad = jnp.zeros((CHANNELS, rows_part, col_cells), jnp.float32)
    for g in range(groups):
        rad = rad + jnp.exp(-h * prefix)[None] * got[:CHANNELS, g]
        prefix = prefix + got[CHANNELS, g]
    alpha = 1.0 - jnp.exp(-h * prefix)
    return jnp.concatenate([rad, alpha[None]], axis=0)


def solution(mesh):
    placed = (P("gz", "gx", "gy"), P(), P(), P(), P())
    return jax.shard_map(
        shards, mesh=mesh, in_specs=placed, out_specs=P(None, ("gx", "gz"), "gy"), check_vma=False
    )
```

```python
import functools
import itertools

import jax
import jax.numpy as jnp
from jax import lax
from jax.experimental import pallas as pl
from jax.experimental.pallas import tpu as pltpu
from jax.sharding import PartitionSpec as P

STEPS = 4
MATERIALS = 4
CHANNELS = 3

KAPPA = 0.5
RATE_DEPTH = 0.3
RATE_PLANE = 0.09
LANES = 256


def pick(cond, a, b):
    if isinstance(cond, bool):
        return a if cond else b
    return jnp.where(cond, a, b)


def axis_moves(axis):
    n = lax.axis_size(axis)
    if n == 1:
        return []
    if n == 2:
        me = lax.axis_index(axis)
        return [([(0, 1), (1, 0)], me == 0, me == 1)]
    up = [(i, i + 1) for i in range(n - 1)]
    down = [(i + 1, i) for i in range(n - 1)]
    return [(up, True, True), (down, False, False)]


def halo_stage(x, dim_axes, width):
    dims = [d for d, _ in dim_axes]
    axes = [a for _, a in dim_axes]
    sizes = [lax.axis_size(a) for a in axes]
    options = [[None] + axis_moves(a) for a in axes]
    blocks = {}
    for combo in itertools.product(*options):
        if all(m is None for m in combo):
            continue
        piece = x
        for d, m in zip(dims, combo):
            if m is not None:
                n_d = piece.shape[d]
                lo = lax.slice_in_dim(piece, 0, width, axis=d)
                hi = lax.slice_in_dim(piece, n_d - width, n_d, axis=d)
                piece = pick(m[1], hi, lo)
        used = [(a, s, m) for a, s, m in zip(axes, sizes, combo) if m is not None]
        pairs = []
        for parts in itertools.product(*[m[0] for _, _, m in used]):
            src = dst = 0
            for (_, s, _), (p, q) in zip(used, parts):
                src, dst = src * s + p, dst * s + q
            pairs.append((src, dst))
        narrow = piece.ndim == 3 and piece.shape[2] == width and piece.shape[1] > width
        if narrow:
            piece = jnp.transpose(piece, (2, 0, 1))
        got = lax.ppermute(piece, tuple(a for a, _, _ in used), pairs)
        if narrow:
            got = jnp.transpose(got, (1, 2, 0))
        landing = [(d, m[2]) for d, m in zip(dims, combo) if m is not None]
        for sides in itertools.product(("lo", "hi"), repeat=len(landing)):
            cond = True
            for (d, land_lo), side in zip(landing, sides):
                this = land_lo if side == "lo" else (not land_lo if isinstance(land_lo, bool) else ~land_lo)
                if isinstance(cond, bool) and isinstance(this, bool):
                    cond = cond and this
                elif isinstance(cond, bool):
                    cond = this if cond else False
                elif isinstance(this, bool):
                    cond = cond if this else False
                else:
                    cond = cond & this
            if cond is False:
                continue
            key = [None] * len(dims)
            for (d, _), side in zip(landing, sides):
                key[dims.index(d)] = side
            key = tuple(k or "mid" for k in key)
            val = got if cond is True else jnp.where(cond, got, 0.0)
            blocks[key] = val if key not in blocks else blocks[key] + val
    blocks[tuple("mid" for _ in dims)] = x

    def block(*key):
        if key in blocks:
            return blocks[key]
        shape = list(x.shape)
        for d, k in zip(dims, key):
            if k != "mid":
                shape[d] = width
        return jnp.zeros(shape, x.dtype)

    return block


def flux(d, rate):
    q = d * (1.0 / KAPPA)
    return rate * d / (1.0 + q * q)


def render_kernel(lim_ref, prm_ref, x_hbm, zlo_hbm, zhi_hbm, rband_hbm, cband_hbm, out_ref, a_ref, b_ref, m_ref, acc_ref, sem,
                  *, interior, h):
    depth, rows, lanes = a_ref.shape
    d_in, r_in, l_in = interior
    halo = STEPS
    copies = [
        pltpu.make_async_copy(x_hbm, b_ref.at[halo:halo + d_in, 0:r_in, 0:l_in], sem.at[0]),
        pltpu.make_async_copy(zlo_hbm, b_ref.at[0:halo, 0:r_in, 0:l_in], sem.at[1]),
        pltpu.make_async_copy(zhi_hbm, b_ref.at[halo + d_in:depth, 0:r_in, 0:l_in], sem.at[2]),
        pltpu.make_async_copy(rband_hbm, b_ref.at[:, r_in:rows, 0:l_in], sem.at[3]),
        pltpu.make_async_copy(cband_hbm, b_ref.at[:, :, l_in:lanes], sem.at[4]),
    ]
    for cp in copies:
        cp.start()

    row = lax.broadcasted_iota(jnp.int32, (rows, lanes), 0)
    lane = lax.broadcasted_iota(jnp.int32, (rows, lanes), 1)
    row_at = jnp.where(row < r_in + halo, row, row - rows)
    lane_at = jnp.where(lane < (l_in + lanes) // 2, lane, lane - lanes)
    ok = (row_at >= lim_ref[2]) & (row_at < lim_ref[3]) & (lane_at >= lim_ref[4]) & (lane_at < lim_ref[5])
    m_ref[...] = jnp.where(ok, 1.0, 0.0).astype(jnp.float32)

    cen = [prm_ref[k] for k in range(MATERIALS)]
    wid = [prm_ref[MATERIALS + k] for k in range(MATERIALS)]
    den = [prm_ref[2 * MATERIALS + k] for k in range(MATERIALS)]
    col = [[prm_ref[3 * MATERIALS + ch * MATERIALS + k] for k in range(MATERIALS)] for ch in range(CHANNELS)]
    out_ref[CHANNELS] = jnp.zeros((r_in, l_in), jnp.float32)
    for k in range(MATERIALS):
        acc_ref[k] = jnp.zeros((r_in, l_in), jnp.float32)

    for cp in copies:
        cp.wait()

    def smooth(src, dst, s):
        z0, z1 = s + 1, depth - 1 - s
        g0 = flux(src[z0] - src[z0 - 1], RATE_DEPTH)

        def body(z, g_prev):
            c = src[z]
            g = flux(src[z + 1] - c, RATE_DEPTH)
            fr = flux(pltpu.roll(c, rows - 1, 0) - c, RATE_PLANE)
            fc = flux(pltpu.roll(c, lanes - 1, 1) - c, RATE_PLANE)
            new = c + (g - g_prev) + (fr - pltpu.roll(fr, 1, 0)) + (fc - pltpu.roll(fc, 1, 1))
            inside = (z >= lim_ref[0]) & (z < lim_ref[1])
            zf = jnp.where(inside, 1.0, 0.0).astype(jnp.float32)
            dst[z] = new * (m_ref[...] * zf)
            return g

        lax.fori_loop(z0, z1, body, g0, unroll=8)

    smooth(b_ref, a_ref, 0)
    smooth(a_ref, b_ref, 1)
    smooth(b_ref, a_ref, 2)

    z0, z1 = halo, halo + d_in
    g0 = flux(a_ref[z0, 0:r_in, 0:l_in] - a_ref[z0 - 1, 0:r_in, 0:l_in], RATE_DEPTH)

    def final(z, g_prev):
        ci = a_ref[z, 0:r_in, 0:l_in]
        g = flux(a_ref[z + 1, 0:r_in, 0:l_in] - ci, RATE_DEPTH)
        c0 = a_ref[z, :, 0:l_in]
        fr = flux(pltpu.roll(c0, rows - 1, 0) - c0, RATE_PLANE)
        cr = a_ref[z, 0:r_in, :]
        fc = flux(pltpu.roll(cr, lanes - 1, 1) - cr, RATE_PLANE)
        v = ci + (g - g_prev) + (fr - pltpu.roll(fr, 1, 0))[0:r_in] + (fc - pltpu.roll(fc, 1, 1))[:, 0:l_in]
        bumps = [den[k] * jnp.exp(-(((v - cen[k]) / wid[k]) ** 2)) for k in range(MATERIALS)]
        ext = bumps[0] + bumps[1] + bumps[2] + bumps[3]
        run = out_ref[CHANNELS]
        through = jnp.exp(-h * run)
        for k in range(MATERIALS):
            acc_ref[k] = acc_ref[k] + through * bumps[k]
        out_ref[CHANNELS] = run + ext
        return g

    lax.fori_loop(z0, z1, final, g0, unroll=4)
    for ch in range(CHANNELS):
        emit = col[ch][0] * acc_ref[0] + col[ch][1] * acc_ref[1] + col[ch][2] * acc_ref[2] + col[ch][3] * acc_ref[3]
        out_ref[ch] = h * emit


def render_block(pieces, lim, prm, interior, h):
    d_in, r_in, l_in = interior
    depth, rows, lanes = d_in + 2 * STEPS, r_in + 2 * STEPS, LANES
    cells = depth * rows * lanes
    kernel = functools.partial(render_kernel, interior=interior, h=h)
    return pl.pallas_call(
        kernel,
        out_shape=jax.ShapeDtypeStruct((CHANNELS + 1, r_in, l_in), jnp.float32),
        in_specs=[pl.BlockSpec(memory_space=pltpu.SMEM)] * 2 + [pl.BlockSpec(memory_space=pl.ANY)] * 5,
        out_specs=pl.BlockSpec(memory_space=pltpu.VMEM),
        scratch_shapes=[
            pltpu.VMEM((depth, rows, lanes), jnp.float32),
            pltpu.VMEM((depth, rows, lanes), jnp.float32),
            pltpu.VMEM((rows, lanes), jnp.float32),
            pltpu.VMEM((MATERIALS, r_in, l_in), jnp.float32),
            pltpu.SemaphoreType.DMA((5,)),
        ],
        compiler_params=pltpu.CompilerParams(vmem_limit_bytes=48 * 1024 * 1024),
        cost_estimate=pl.CostEstimate(
            flops=int(cells * STEPS * 40 + d_in * r_in * l_in * 60),
            transcendentals=int(d_in * r_in * l_in * (MATERIALS + 1)),
            bytes_accessed=int(cells * 4 + (CHANNELS + 1) * r_in * l_in * 4),
        ),
    )(lim, prm, *pieces)


def shards(phase_field, centres, widths, densities, colours):
    depth_cells, row_cells, col_cells = phase_field.shape
    groups = lax.axis_size("gz")
    h = 1.0 / (depth_cells * groups)
    zblock = halo_stage(phase_field, ((0, "gz"),), STEPS)
    zlo, zhi = zblock("lo"), zblock("hi")
    deep = jnp.concatenate([zlo, phase_field, zhi], axis=0)
    plane = halo_stage(deep, ((1, "gx"), (2, "gy")), STEPS)
    rband = jnp.concatenate([plane("hi", "mid"), plane("lo", "mid")], axis=1)
    right = jnp.concatenate([plane("mid", "hi"), plane("hi", "hi"), plane("lo", "hi")], axis=1)
    left = jnp.concatenate([plane("mid", "lo"), plane("hi", "lo"), plane("lo", "lo")], axis=1)
    fill = jnp.zeros(right.shape[:2] + (LANES - col_cells - 2 * STEPS,), jnp.float32)
    cband = jnp.concatenate([right, fill, left], axis=2)

    z_lo = STEPS - lax.axis_index("gz") * depth_cells
    r_lo = -lax.axis_index("gx") * row_cells
    c_lo = -lax.axis_index("gy") * col_cells
    lim = jnp.stack(
        [
            z_lo,
            z_lo + depth_cells * groups,
            r_lo,
            r_lo + row_cells * lax.axis_size("gx"),
            c_lo,
            c_lo + col_cells * lax.axis_size("gy"),
        ]
    ).astype(jnp.int32)
    prm = jnp.concatenate([centres, widths, densities, colours.reshape(-1)]).astype(jnp.float32)

    seg = render_block((phase_field, zlo, zhi, rband, cband), lim, prm, (depth_cells, row_cells, col_cells), h)

    rows_part = row_cells // groups
    parts = seg.reshape(CHANNELS + 1, groups, rows_part, col_cells)
    got = lax.all_to_all(parts, "gz", 1, 1, tiled=True)
    prefix = jnp.zeros((rows_part, col_cells), jnp.float32)
    rad = jnp.zeros((CHANNELS, rows_part, col_cells), jnp.float32)
    for g in range(groups):
        rad = rad + jnp.exp(-h * prefix)[None] * got[:CHANNELS, g]
        prefix = prefix + got[CHANNELS, g]
    alpha = 1.0 - jnp.exp(-h * prefix)
    return jnp.concatenate([rad, alpha[None]], axis=0)


def solution(mesh):
    placed = (P("gz", "gx", "gy"), P(), P(), P(), P())
    return jax.shard_map(
        shards, mesh=mesh, in_specs=placed, out_specs=P(None, ("gx", "gz"), "gy"), check_vma=False
    )
```

```python
import functools
import itertools

import jax
import jax.numpy as jnp
from jax import lax
from jax.experimental import pallas as pl
from jax.experimental.pallas import tpu as pltpu
from jax.sharding import PartitionSpec as P

STEPS = 4
MATERIALS = 4
CHANNELS = 3

KAPPA = 0.5
RATE_DEPTH = 0.3
RATE_PLANE = 0.09
LANES = 256


def pick(cond, a, b):
    if isinstance(cond, bool):
        return a if cond else b
    return jnp.where(cond, a, b)


def axis_moves(axis):
    n = lax.axis_size(axis)
    if n == 1:
        return []
    if n == 2:
        me = lax.axis_index(axis)
        return [([(0, 1), (1, 0)], me == 0, me == 1)]
    up = [(i, i + 1) for i in range(n - 1)]
    down = [(i + 1, i) for i in range(n - 1)]
    return [(up, True, True), (down, False, False)]


def halo_stage(x, dim_axes, width):
    dims = [d for d, _ in dim_axes]
    axes = [a for _, a in dim_axes]
    sizes = [lax.axis_size(a) for a in axes]
    options = [[None] + axis_moves(a) for a in axes]
    blocks = {}
    for combo in itertools.product(*options):
        if all(m is None for m in combo):
            continue
        piece = x
        for d, m in zip(dims, combo):
            if m is not None:
                n_d = piece.shape[d]
                lo = lax.slice_in_dim(piece, 0, width, axis=d)
                hi = lax.slice_in_dim(piece, n_d - width, n_d, axis=d)
                piece = pick(m[1], hi, lo)
        used = [(a, s, m) for a, s, m in zip(axes, sizes, combo) if m is not None]
        pairs = []
        for parts in itertools.product(*[m[0] for _, _, m in used]):
            src = dst = 0
            for (_, s, _), (p, q) in zip(used, parts):
                src, dst = src * s + p, dst * s + q
            pairs.append((src, dst))
        narrow = piece.ndim == 3 and piece.shape[2] == width and piece.shape[1] > width
        if narrow:
            piece = jnp.transpose(piece, (2, 0, 1))
        got = lax.ppermute(piece, tuple(a for a, _, _ in used), pairs)
        if narrow:
            got = jnp.transpose(got, (1, 2, 0))
        landing = [(d, m[2]) for d, m in zip(dims, combo) if m is not None]
        for sides in itertools.product(("lo", "hi"), repeat=len(landing)):
            cond = True
            for (d, land_lo), side in zip(landing, sides):
                this = land_lo if side == "lo" else (not land_lo if isinstance(land_lo, bool) else ~land_lo)
                if isinstance(cond, bool) and isinstance(this, bool):
                    cond = cond and this
                elif isinstance(cond, bool):
                    cond = this if cond else False
                elif isinstance(this, bool):
                    cond = cond if this else False
                else:
                    cond = cond & this
            if cond is False:
                continue
            key = [None] * len(dims)
            for (d, _), side in zip(landing, sides):
                key[dims.index(d)] = side
            key = tuple(k or "mid" for k in key)
            val = got if cond is True else jnp.where(cond, got, 0.0)
            blocks[key] = val if key not in blocks else blocks[key] + val
    blocks[tuple("mid" for _ in dims)] = x

    def block(*key):
        if key in blocks:
            return blocks[key]
        shape = list(x.shape)
        for d, k in zip(dims, key):
            if k != "mid":
                shape[d] = width
        return jnp.zeros(shape, x.dtype)

    return block


def flux(d):
    q = d * (1.0 / KAPPA)
    return d / (1.0 + q * q)


def render_kernel(lim_ref, prm_ref, x_hbm, zlo_hbm, zhi_hbm, rband_hbm, cband_hbm, out_ref, a_ref, b_ref, m_ref, acc_ref, sem,
                  *, interior, h):
    depth, rows, lanes = a_ref.shape
    d_in, r_in, l_in = interior
    halo = STEPS
    copies = [
        pltpu.make_async_copy(x_hbm, b_ref.at[halo:halo + d_in, 0:r_in, 0:l_in], sem.at[0]),
        pltpu.make_async_copy(zlo_hbm, b_ref.at[0:halo, 0:r_in, 0:l_in], sem.at[1]),
        pltpu.make_async_copy(zhi_hbm, b_ref.at[halo + d_in:depth, 0:r_in, 0:l_in], sem.at[2]),
        pltpu.make_async_copy(rband_hbm, b_ref.at[:, r_in:rows, 0:l_in], sem.at[3]),
        pltpu.make_async_copy(cband_hbm, b_ref.at[:, :, l_in:lanes], sem.at[4]),
    ]
    for cp in copies:
        cp.start()

    row = lax.broadcasted_iota(jnp.int32, (rows, lanes), 0)
    lane = lax.broadcasted_iota(jnp.int32, (rows, lanes), 1)
    row_at = jnp.where(row < r_in + halo, row, row - rows)
    lane_at = jnp.where(lane < (l_in + lanes) // 2, lane, lane - lanes)
    ok = (row_at >= lim_ref[2]) & (row_at < lim_ref[3]) & (lane_at >= lim_ref[4]) & (lane_at < lim_ref[5])
    m_ref[...] = jnp.where(ok, 1.0, 0.0).astype(jnp.float32)

    cen = [prm_ref[k] for k in range(MATERIALS)]
    wid = [prm_ref[MATERIALS + k] for k in range(MATERIALS)]
    den = [prm_ref[2 * MATERIALS + k] for k in range(MATERIALS)]
    col = [[prm_ref[3 * MATERIALS + ch * MATERIALS + k] for k in range(MATERIALS)] for ch in range(CHANNELS)]
    out_ref[CHANNELS] = jnp.zeros((r_in, l_in), jnp.float32)
    for k in range(MATERIALS):
        acc_ref[k] = jnp.zeros((r_in, l_in), jnp.float32)

    for cp in copies:
        cp.wait()

    def smooth(src, dst, s):
        z0, z1 = s + 1, depth - 1 - s
        g0 = flux(src[z0] - src[z0 - 1])

        def body(z, g_prev):
            c = src[z]
            g = flux(src[z + 1] - c)
            fr = flux(pltpu.roll(c, rows - 1, 0) - c)
            fc = flux(pltpu.roll(c, lanes - 1, 1) - c)
            plane = (fr - pltpu.roll(fr, 1, 0)) + (fc - pltpu.roll(fc, 1, 1))
            new = c + RATE_DEPTH * (g - g_prev) + RATE_PLANE * plane
            inside = (z >= lim_ref[0]) & (z < lim_ref[1])

            @pl.when(inside)
            def _():
                dst[z, 0:r_in, 0:l_in] = new[0:r_in, 0:l_in]
                dst[z, r_in:rows, :] = new[r_in:rows] * m_ref[r_in:rows, :]
                dst[z, 0:r_in, l_in:lanes] = new[0:r_in, l_in:lanes] * m_ref[0:r_in, l_in:lanes]

            @pl.when(jnp.logical_not(inside))
            def _():
                dst[z] = jnp.zeros((rows, lanes), jnp.float32)

            return g

        lax.fori_loop(z0, z1, body, g0, unroll=8)

    smooth(b_ref, a_ref, 0)
    smooth(a_ref, b_ref, 1)
    smooth(b_ref, a_ref, 2)

    z0, z1 = halo, halo + d_in
    g0 = flux(a_ref[z0, 0:r_in, 0:l_in] - a_ref[z0 - 1, 0:r_in, 0:l_in])

    def final(z, g_prev):
        ci = a_ref[z, 0:r_in, 0:l_in]
        g = flux(a_ref[z + 1, 0:r_in, 0:l_in] - ci)
        c0 = a_ref[z, :, 0:l_in]
        fr = flux(pltpu.roll(c0, rows - 1, 0) - c0)
        cr = a_ref[z, 0:r_in, :]
        fc = flux(pltpu.roll(cr, lanes - 1, 1) - cr)
        plane = (fr - pltpu.roll(fr, 1, 0))[0:r_in] + (fc - pltpu.roll(fc, 1, 1))[:, 0:l_in]
        v = ci + RATE_DEPTH * (g - g_prev) + RATE_PLANE * plane
        bumps = [den[k] * jnp.exp(-(((v - cen[k]) / wid[k]) ** 2)) for k in range(MATERIALS)]
        ext = bumps[0] + bumps[1] + bumps[2] + bumps[3]
        run = out_ref[CHANNELS]
        through = jnp.exp(-h * run)
        for k in range(MATERIALS):
            acc_ref[k] = acc_ref[k] + through * bumps[k]
        out_ref[CHANNELS] = run + ext
        return g

    lax.fori_loop(z0, z1, final, g0, unroll=4)
    for ch in range(CHANNELS):
        emit = col[ch][0] * acc_ref[0] + col[ch][1] * acc_ref[1] + col[ch][2] * acc_ref[2] + col[ch][3] * acc_ref[3]
        out_ref[ch] = h * emit


def render_block(pieces, lim, prm, interior, h):
    d_in, r_in, l_in = interior
    depth, rows, lanes = d_in + 2 * STEPS, r_in + 2 * STEPS, LANES
    cells = depth * rows * lanes
    kernel = functools.partial(render_kernel, interior=interior, h=h)
    return pl.pallas_call(
        kernel,
        out_shape=jax.ShapeDtypeStruct((CHANNELS + 1, r_in, l_in), jnp.float32),
        in_specs=[pl.BlockSpec(memory_space=pltpu.SMEM)] * 2 + [pl.BlockSpec(memory_space=pl.ANY)] * 5,
        out_specs=pl.BlockSpec(memory_space=pltpu.VMEM),
        scratch_shapes=[
            pltpu.VMEM((depth, rows, lanes), jnp.float32),
            pltpu.VMEM((depth, rows, lanes), jnp.float32),
            pltpu.VMEM((rows, lanes), jnp.float32),
            pltpu.VMEM((MATERIALS, r_in, l_in), jnp.float32),
            pltpu.SemaphoreType.DMA((5,)),
        ],
        compiler_params=pltpu.CompilerParams(vmem_limit_bytes=48 * 1024 * 1024),
        cost_estimate=pl.CostEstimate(
            flops=int(cells * STEPS * 40 + d_in * r_in * l_in * 60),
            transcendentals=int(d_in * r_in * l_in * (MATERIALS + 1)),
            bytes_accessed=int(cells * 4 + (CHANNELS + 1) * r_in * l_in * 4),
        ),
    )(lim, prm, *pieces)


def shards(phase_field, centres, widths, densities, colours):
    depth_cells, row_cells, col_cells = phase_field.shape
    groups = lax.axis_size("gz")
    h = 1.0 / (depth_cells * groups)
    zblock = halo_stage(phase_field, ((0, "gz"),), STEPS)
    zlo, zhi = zblock("lo"), zblock("hi")
    deep = jnp.concatenate([zlo, phase_field, zhi], axis=0)
    plane = halo_stage(deep, ((1, "gx"), (2, "gy")), STEPS)
    rband = jnp.concatenate([plane("hi", "mid"), plane("lo", "mid")], axis=1)
    right = jnp.concatenate([plane("mid", "hi"), plane("hi", "hi"), plane("lo", "hi")], axis=1)
    left = jnp.concatenate([plane("mid", "lo"), plane("hi", "lo"), plane("lo", "lo")], axis=1)
    fill = jnp.zeros(right.shape[:2] + (LANES - col_cells - 2 * STEPS,), jnp.float32)
    cband = jnp.concatenate([right, fill, left], axis=2)

    z_lo = STEPS - lax.axis_index("gz") * depth_cells
    r_lo = -lax.axis_index("gx") * row_cells
    c_lo = -lax.axis_index("gy") * col_cells
    lim = jnp.stack(
        [
            z_lo,
            z_lo + depth_cells * groups,
            r_lo,
            r_lo + row_cells * lax.axis_size("gx"),
            c_lo,
            c_lo + col_cells * lax.axis_size("gy"),
        ]
    ).astype(jnp.int32)
    prm = jnp.concatenate([centres, widths, densities, colours.reshape(-1)]).astype(jnp.float32)

    seg = render_block((phase_field, zlo, zhi, rband, cband), lim, prm, (depth_cells, row_cells, col_cells), h)

    rows_part = row_cells // groups
    parts = seg.reshape(CHANNELS + 1, groups, rows_part, col_cells)
    got = lax.all_to_all(parts, "gz", 1, 1, tiled=True)
    prefix = jnp.zeros((rows_part, col_cells), jnp.float32)
    rad = jnp.zeros((CHANNELS, rows_part, col_cells), jnp.float32)
    for g in range(groups):
        rad = rad + jnp.exp(-h * prefix)[None] * got[:CHANNELS, g]
        prefix = prefix + got[CHANNELS, g]
    alpha = 1.0 - jnp.exp(-h * prefix)
    return jnp.concatenate([rad, alpha[None]], axis=0)


def solution(mesh):
    placed = (P("gz", "gx", "gy"), P(), P(), P(), P())
    return jax.shard_map(
        shards, mesh=mesh, in_specs=placed, out_specs=P(None, ("gx", "gz"), "gy"), check_vma=False
    )
```

```python
import functools
import itertools

import jax
import jax.numpy as jnp
from jax import lax
from jax.experimental import pallas as pl
from jax.experimental.pallas import tpu as pltpu
from jax.sharding import PartitionSpec as P

STEPS = 4
MATERIALS = 4
CHANNELS = 3

KAPPA = 0.5
RATE_DEPTH = 0.3
RATE_PLANE = 0.09
LANES = 256


def pick(cond, a, b):
    if isinstance(cond, bool):
        return a if cond else b
    return jnp.where(cond, a, b)


def axis_moves(axis):
    n = lax.axis_size(axis)
    if n == 1:
        return []
    if n == 2:
        me = lax.axis_index(axis)
        return [([(0, 1), (1, 0)], me == 0, me == 1)]
    up = [(i, i + 1) for i in range(n - 1)]
    down = [(i + 1, i) for i in range(n - 1)]
    return [(up, True, True), (down, False, False)]


def halo_stage(x, dim_axes, width):
    dims = [d for d, _ in dim_axes]
    axes = [a for _, a in dim_axes]
    sizes = [lax.axis_size(a) for a in axes]
    options = [[None] + axis_moves(a) for a in axes]
    blocks = {}
    for combo in itertools.product(*options):
        if all(m is None for m in combo):
            continue
        piece = x
        for d, m in zip(dims, combo):
            if m is not None:
                n_d = piece.shape[d]
                lo = lax.slice_in_dim(piece, 0, width, axis=d)
                hi = lax.slice_in_dim(piece, n_d - width, n_d, axis=d)
                piece = pick(m[1], hi, lo)
        used = [(a, s, m) for a, s, m in zip(axes, sizes, combo) if m is not None]
        pairs = []
        for parts in itertools.product(*[m[0] for _, _, m in used]):
            src = dst = 0
            for (_, s, _), (p, q) in zip(used, parts):
                src, dst = src * s + p, dst * s + q
            pairs.append((src, dst))
        narrow = piece.ndim == 3 and piece.shape[2] == width and piece.shape[1] > width
        if narrow:
            piece = jnp.transpose(piece, (2, 0, 1))
        got = lax.ppermute(piece, tuple(a for a, _, _ in used), pairs)
        if narrow:
            got = jnp.transpose(got, (1, 2, 0))
        landing = [(d, m[2]) for d, m in zip(dims, combo) if m is not None]
        for sides in itertools.product(("lo", "hi"), repeat=len(landing)):
            cond = True
            for (d, land_lo), side in zip(landing, sides):
                this = land_lo if side == "lo" else (not land_lo if isinstance(land_lo, bool) else ~land_lo)
                if isinstance(cond, bool) and isinstance(this, bool):
                    cond = cond and this
                elif isinstance(cond, bool):
                    cond = this if cond else False
                elif isinstance(this, bool):
                    cond = cond if this else False
                else:
                    cond = cond & this
            if cond is False:
                continue
            key = [None] * len(dims)
            for (d, _), side in zip(landing, sides):
                key[dims.index(d)] = side
            key = tuple(k or "mid" for k in key)
            val = got if cond is True else jnp.where(cond, got, 0.0)
            blocks[key] = val if key not in blocks else blocks[key] + val
    blocks[tuple("mid" for _ in dims)] = x

    def block(*key):
        if key in blocks:
            return blocks[key]
        shape = list(x.shape)
        for d, k in zip(dims, key):
            if k != "mid":
                shape[d] = width
        return jnp.zeros(shape, x.dtype)

    return block


def flux(d):
    q = d * (1.0 / KAPPA)
    return d / (1.0 + q * q)


def render_kernel(lim_ref, prm_ref, x_hbm, zlo_hbm, zhi_hbm, rband_hbm, cband_hbm, out_ref, a_ref, b_ref, m_ref, acc_ref, sem,
                  *, interior, h):
    depth, rows, lanes = a_ref.shape
    d_in, r_in, l_in = interior
    halo = STEPS
    copies = [
        pltpu.make_async_copy(x_hbm, b_ref.at[halo:halo + d_in, 0:r_in, 0:l_in], sem.at[0]),
        pltpu.make_async_copy(zlo_hbm, b_ref.at[0:halo, 0:r_in, 0:l_in], sem.at[1]),
        pltpu.make_async_copy(zhi_hbm, b_ref.at[halo + d_in:depth, 0:r_in, 0:l_in], sem.at[2]),
        pltpu.make_async_copy(rband_hbm, b_ref.at[:, r_in:rows, 0:l_in], sem.at[3]),
        pltpu.make_async_copy(cband_hbm, b_ref.at[:, :, l_in:lanes], sem.at[4]),
    ]
    for cp in copies:
        cp.start()

    row = lax.broadcasted_iota(jnp.int32, (rows, lanes), 0)
    lane = lax.broadcasted_iota(jnp.int32, (rows, lanes), 1)
    row_at = jnp.where(row < r_in + halo, row, row - rows)
    lane_at = jnp.where(lane < (l_in + lanes) // 2, lane, lane - lanes)
    ok = (row_at >= lim_ref[2]) & (row_at < lim_ref[3]) & (lane_at >= lim_ref[4]) & (lane_at < lim_ref[5])
    m_ref[...] = jnp.where(ok, 1.0, 0.0).astype(jnp.float32)

    cen = [prm_ref[k] for k in range(MATERIALS)]
    wid = [prm_ref[MATERIALS + k] for k in range(MATERIALS)]
    den = [prm_ref[2 * MATERIALS + k] for k in range(MATERIALS)]
    col = [[prm_ref[3 * MATERIALS + ch * MATERIALS + k] for k in range(MATERIALS)] for ch in range(CHANNELS)]
    out_ref[CHANNELS] = jnp.zeros((r_in, l_in), jnp.float32)
    for k in range(MATERIALS):
        acc_ref[k] = jnp.zeros((r_in, l_in), jnp.float32)

    for cp in copies:
        cp.wait()

    def smooth(src, dst, s):
        z0, z1 = s + 1, depth - 1 - s
        g0 = flux(src[z0] - src[z0 - 1])

        def body(z, g_prev):
            c = src[z]
            g = flux(src[z + 1] - c)
            fr = flux(pltpu.roll(c, rows - 1, 0) - c)
            fc = flux(pltpu.roll(c, lanes - 1, 1) - c)
            plane = (fr - pltpu.roll(fr, 1, 0)) + (fc - pltpu.roll(fc, 1, 1))
            new = c + RATE_DEPTH * (g - g_prev) + RATE_PLANE * plane
            inside = (z >= lim_ref[0]) & (z < lim_ref[1])
            zf = jnp.where(inside, 1.0, 0.0).astype(jnp.float32)
            dst[z] = new * (m_ref[...] * zf)
            return g

        lax.fori_loop(z0, z1, body, g0, unroll=8)

    smooth(b_ref, a_ref, 0)
    smooth(a_ref, b_ref, 1)
    smooth(b_ref, a_ref, 2)

    z0, z1 = halo, halo + d_in
    g0 = flux(a_ref[z0, 0:r_in, 0:l_in] - a_ref[z0 - 1, 0:r_in, 0:l_in])

    def final(z, g_prev):
        ci = a_ref[z, 0:r_in, 0:l_in]
        g = flux(a_ref[z + 1, 0:r_in, 0:l_in] - ci)
        c0 = a_ref[z, :, 0:l_in]
        fr = flux(pltpu.roll(c0, rows - 1, 0) - c0)
        cr = a_ref[z, 0:r_in, :]
        fc = flux(pltpu.roll(cr, lanes - 1, 1) - cr)
        plane = (fr - pltpu.roll(fr, 1, 0))[0:r_in] + (fc - pltpu.roll(fc, 1, 1))[:, 0:l_in]
        v = ci + RATE_DEPTH * (g - g_prev) + RATE_PLANE * plane
        bumps = [den[k] * jnp.exp(-(((v - cen[k]) / wid[k]) ** 2)) for k in range(MATERIALS)]
        ext = bumps[0] + bumps[1] + bumps[2] + bumps[3]
        run = out_ref[CHANNELS]
        through = jnp.exp(-h * run)
        for k in range(MATERIALS):
            acc_ref[k] = acc_ref[k] + through * bumps[k]
        out_ref[CHANNELS] = run + ext
        return g

    lax.fori_loop(z0, z1, final, g0, unroll=4)
    for ch in range(CHANNELS):
        emit = col[ch][0] * acc_ref[0] + col[ch][1] * acc_ref[1] + col[ch][2] * acc_ref[2] + col[ch][3] * acc_ref[3]
        out_ref[ch] = h * emit


def render_block(pieces, lim, prm, interior, h):
    d_in, r_in, l_in = interior
    depth, rows, lanes = d_in + 2 * STEPS, r_in + 2 * STEPS, LANES
    cells = depth * rows * lanes
    kernel = functools.partial(render_kernel, interior=interior, h=h)
    return pl.pallas_call(
        kernel,
        out_shape=jax.ShapeDtypeStruct((CHANNELS + 1, r_in, l_in), jnp.float32),
        in_specs=[pl.BlockSpec(memory_space=pltpu.SMEM)] * 2 + [pl.BlockSpec(memory_space=pl.ANY)] * 5,
        out_specs=pl.BlockSpec(memory_space=pltpu.VMEM),
        scratch_shapes=[
            pltpu.VMEM((depth, rows, lanes), jnp.float32),
            pltpu.VMEM((depth, rows, lanes), jnp.float32),
            pltpu.VMEM((rows, lanes), jnp.float32),
            pltpu.VMEM((MATERIALS, r_in, l_in), jnp.float32),
            pltpu.SemaphoreType.DMA((5,)),
        ],
        compiler_params=pltpu.CompilerParams(vmem_limit_bytes=48 * 1024 * 1024),
        cost_estimate=pl.CostEstimate(
            flops=int(cells * STEPS * 40 + d_in * r_in * l_in * 60),
            transcendentals=int(d_in * r_in * l_in * (MATERIALS + 1)),
            bytes_accessed=int(cells * 4 + (CHANNELS + 1) * r_in * l_in * 4),
        ),
    )(lim, prm, *pieces)


def shards(phase_field, centres, widths, densities, colours):
    depth_cells, row_cells, col_cells = phase_field.shape
    groups = lax.axis_size("gz")
    h = 1.0 / (depth_cells * groups)
    zblock = halo_stage(phase_field, ((0, "gz"),), STEPS)
    zlo, zhi = zblock("lo"), zblock("hi")
    deep = jnp.concatenate([zlo, phase_field, zhi], axis=0)
    plane = halo_stage(deep, ((1, "gx"), (2, "gy")), STEPS)
    rband = jnp.concatenate([plane("hi", "mid"), plane("lo", "mid")], axis=1)
    right = jnp.concatenate([plane("mid", "hi"), plane("hi", "hi"), plane("lo", "hi")], axis=1)
    left = jnp.concatenate([plane("mid", "lo"), plane("hi", "lo"), plane("lo", "lo")], axis=1)
    fill = jnp.zeros(right.shape[:2] + (LANES - col_cells - 2 * STEPS,), jnp.float32)
    cband = jnp.concatenate([right, fill, left], axis=2)

    z_lo = STEPS - lax.axis_index("gz") * depth_cells
    r_lo = -lax.axis_index("gx") * row_cells
    c_lo = -lax.axis_index("gy") * col_cells
    lim = jnp.stack(
        [
            z_lo,
            z_lo + depth_cells * groups,
            r_lo,
            r_lo + row_cells * lax.axis_size("gx"),
            c_lo,
            c_lo + col_cells * lax.axis_size("gy"),
        ]
    ).astype(jnp.int32)
    prm = jnp.concatenate([centres, widths, densities, colours.reshape(-1)]).astype(jnp.float32)

    seg = render_block((phase_field, zlo, zhi, rband, cband), lim, prm, (depth_cells, row_cells, col_cells), h)

    rows_part = row_cells // groups
    parts = seg.reshape(CHANNELS + 1, groups, rows_part, col_cells)
    got = lax.all_to_all(parts, "gz", 1, 1, tiled=True)
    prefix = jnp.zeros((rows_part, col_cells), jnp.float32)
    rad = jnp.zeros((CHANNELS, rows_part, col_cells), jnp.float32)
    for g in range(groups):
        rad = rad + jnp.exp(-h * prefix)[None] * got[:CHANNELS, g]
        prefix = prefix + got[CHANNELS, g]
    alpha = 1.0 - jnp.exp(-h * prefix)
    return jnp.concatenate([rad, alpha[None]], axis=0)


def solution(mesh):
    placed = (P("gz", "gx", "gy"), P(), P(), P(), P())
    return jax.shard_map(
        shards, mesh=mesh, in_specs=placed, out_specs=P(None, ("gx", "gz"), "gy"), check_vma=False
    )
```

```python
import functools
import itertools

import jax
import jax.numpy as jnp
from jax import lax
from jax.experimental import pallas as pl
from jax.experimental.pallas import tpu as pltpu
from jax.sharding import PartitionSpec as P

STEPS = 4
MATERIALS = 4
CHANNELS = 3

KAPPA = 0.5
RATE_DEPTH = 0.3
RATE_PLANE = 0.09
LANES = 256


def pick(cond, a, b):
    if isinstance(cond, bool):
        return a if cond else b
    return jnp.where(cond, a, b)


def axis_moves(axis):
    n = lax.axis_size(axis)
    if n == 1:
        return []
    if n == 2:
        me = lax.axis_index(axis)
        return [([(0, 1), (1, 0)], me == 0, me == 1)]
    up = [(i, i + 1) for i in range(n - 1)]
    down = [(i + 1, i) for i in range(n - 1)]
    return [(up, True, True), (down, False, False)]


def halo_stage(x, dim_axes, width):
    dims = [d for d, _ in dim_axes]
    axes = [a for _, a in dim_axes]
    sizes = [lax.axis_size(a) for a in axes]
    options = [[None] + axis_moves(a) for a in axes]
    blocks = {}
    for combo in itertools.product(*options):
        if all(m is None for m in combo):
            continue
        piece = x
        for d, m in zip(dims, combo):
            if m is not None:
                n_d = piece.shape[d]
                lo = lax.slice_in_dim(piece, 0, width, axis=d)
                hi = lax.slice_in_dim(piece, n_d - width, n_d, axis=d)
                piece = pick(m[1], hi, lo)
        used = [(a, s, m) for a, s, m in zip(axes, sizes, combo) if m is not None]
        pairs = []
        for parts in itertools.product(*[m[0] for _, _, m in used]):
            src = dst = 0
            for (_, s, _), (p, q) in zip(used, parts):
                src, dst = src * s + p, dst * s + q
            pairs.append((src, dst))
        narrow = piece.ndim == 3 and piece.shape[2] == width and piece.shape[1] > width
        if narrow:
            piece = jnp.transpose(piece, (2, 0, 1))
        got = lax.ppermute(piece, tuple(a for a, _, _ in used), pairs)
        if narrow:
            got = jnp.transpose(got, (1, 2, 0))
        landing = [(d, m[2]) for d, m in zip(dims, combo) if m is not None]
        for sides in itertools.product(("lo", "hi"), repeat=len(landing)):
            cond = True
            for (d, land_lo), side in zip(landing, sides):
                this = land_lo if side == "lo" else (not land_lo if isinstance(land_lo, bool) else ~land_lo)
                if isinstance(cond, bool) and isinstance(this, bool):
                    cond = cond and this
                elif isinstance(cond, bool):
                    cond = this if cond else False
                elif isinstance(this, bool):
                    cond = cond if this else False
                else:
                    cond = cond & this
            if cond is False:
                continue
            key = [None] * len(dims)
            for (d, _), side in zip(landing, sides):
                key[dims.index(d)] = side
            key = tuple(k or "mid" for k in key)
            val = got if cond is True else jnp.where(cond, got, 0.0)
            blocks[key] = val if key not in blocks else blocks[key] + val
    blocks[tuple("mid" for _ in dims)] = x

    def block(*key):
        if key in blocks:
            return blocks[key]
        shape = list(x.shape)
        for d, k in zip(dims, key):
            if k != "mid":
                shape[d] = width
        return jnp.zeros(shape, x.dtype)

    return block


def flux(d, rate):
    q = d * (1.0 / KAPPA)
    return rate * d / (1.0 + q * q)


def render_kernel(lim_ref, prm_ref, x_hbm, zlo_hbm, zhi_hbm, rband_hbm, cband_hbm, out_ref, a_ref, b_ref, m_ref, acc_ref, sem,
                  *, interior, h):
    depth, rows, lanes = a_ref.shape
    d_in, r_in, l_in = interior
    halo = STEPS
    copies = [
        pltpu.make_async_copy(x_hbm, b_ref.at[halo:halo + d_in, 0:r_in, 0:l_in], sem.at[0]),
        pltpu.make_async_copy(zlo_hbm, b_ref.at[0:halo, 0:r_in, 0:l_in], sem.at[1]),
        pltpu.make_async_copy(zhi_hbm, b_ref.at[halo + d_in:depth, 0:r_in, 0:l_in], sem.at[2]),
        pltpu.make_async_copy(rband_hbm, b_ref.at[:, r_in:rows, 0:l_in], sem.at[3]),
        pltpu.make_async_copy(cband_hbm, b_ref.at[:, :, l_in:lanes], sem.at[4]),
    ]
    for cp in copies:
        cp.start()

    row = lax.broadcasted_iota(jnp.int32, (rows, lanes), 0)
    lane = lax.broadcasted_iota(jnp.int32, (rows, lanes), 1)
    row_at = jnp.where(row < r_in + halo, row, row - rows)
    lane_at = jnp.where(lane < (l_in + lanes) // 2, lane, lane - lanes)
    ok = (row_at >= lim_ref[2]) & (row_at < lim_ref[3]) & (lane_at >= lim_ref[4]) & (lane_at < lim_ref[5])
    m_ref[...] = jnp.where(ok, 1.0, 0.0).astype(jnp.float32)

    cen = [prm_ref[k] for k in range(MATERIALS)]
    wid = [prm_ref[MATERIALS + k] for k in range(MATERIALS)]
    den = [prm_ref[2 * MATERIALS + k] for k in range(MATERIALS)]
    col = [[prm_ref[3 * MATERIALS + ch * MATERIALS + k] for k in range(MATERIALS)] for ch in range(CHANNELS)]
    out_ref[CHANNELS] = jnp.zeros((r_in, l_in), jnp.float32)
    for k in range(MATERIALS):
        acc_ref[k] = jnp.zeros((r_in, l_in), jnp.float32)

    for cp in copies:
        cp.wait()

    def smooth(src, dst, s):
        z0, z1 = s + 1, depth - 1 - s
        g0 = flux(src[z0] - src[z0 - 1], RATE_DEPTH)

        def body(z, g_prev):
            c = src[z]
            g = flux(src[z + 1] - c, RATE_DEPTH)
            fr = flux(pltpu.roll(c, rows - 1, 0) - c, RATE_PLANE)
            fc = flux(pltpu.roll(c, lanes - 1, 1) - c, RATE_PLANE)
            new = c + (g - g_prev) + (fr - pltpu.roll(fr, 1, 0)) + (fc - pltpu.roll(fc, 1, 1))
            inside = (z >= lim_ref[0]) & (z < lim_ref[1])
            zf = jnp.where(inside, 1.0, 0.0).astype(jnp.float32)
            dst[z] = new * (m_ref[...] * zf)
            return g

        lax.fori_loop(z0, z1, body, g0, unroll=8)

    smooth(b_ref, a_ref, 0)
    smooth(a_ref, b_ref, 1)
    smooth(b_ref, a_ref, 2)

    z0, z1 = halo, halo + d_in
    g0 = flux(a_ref[z0, 0:r_in, 0:l_in] - a_ref[z0 - 1, 0:r_in, 0:l_in], RATE_DEPTH)

    def final(z, g_prev):
        ci = a_ref[z, 0:r_in, 0:l_in]
        g = flux(a_ref[z + 1, 0:r_in, 0:l_in] - ci, RATE_DEPTH)
        c0 = a_ref[z, :, 0:l_in]
        fr = flux(pltpu.roll(c0, rows - 1, 0) - c0, RATE_PLANE)
        cr = a_ref[z, 0:r_in, :]
        fc = flux(pltpu.roll(cr, lanes - 1, 1) - cr, RATE_PLANE)
        v = ci + (g - g_prev) + (fr - pltpu.roll(fr, 1, 0))[0:r_in] + (fc - pltpu.roll(fc, 1, 1))[:, 0:l_in]
        bumps = [den[k] * jnp.exp(-(((v - cen[k]) / wid[k]) ** 2)) for k in range(MATERIALS)]
        ext = bumps[0] + bumps[1] + bumps[2] + bumps[3]
        run = out_ref[CHANNELS]
        through = jnp.exp(-h * run)
        for k in range(MATERIALS):
            acc_ref[k] = acc_ref[k] + through * bumps[k]
        out_ref[CHANNELS] = run + ext
        return g

    lax.fori_loop(z0, z1, final, g0, unroll=4)
    for ch in range(CHANNELS):
        emit = col[ch][0] * acc_ref[0] + col[ch][1] * acc_ref[1] + col[ch][2] * acc_ref[2] + col[ch][3] * acc_ref[3]
        out_ref[ch] = h * emit


def render_block(pieces, lim, prm, interior, h):
    d_in, r_in, l_in = interior
    depth, rows, lanes = d_in + 2 * STEPS, r_in + 2 * STEPS, LANES
    cells = depth * rows * lanes
    kernel = functools.partial(render_kernel, interior=interior, h=h)
    return pl.pallas_call(
        kernel,
        out_shape=jax.ShapeDtypeStruct((CHANNELS + 1, r_in, l_in), jnp.float32),
        in_specs=[pl.BlockSpec(memory_space=pltpu.SMEM)] * 2 + [pl.BlockSpec(memory_space=pl.ANY)] * 5,
        out_specs=pl.BlockSpec(memory_space=pltpu.VMEM),
        scratch_shapes=[
            pltpu.VMEM((depth, rows, lanes), jnp.float32),
            pltpu.VMEM((depth, rows, lanes), jnp.float32),
            pltpu.VMEM((rows, lanes), jnp.float32),
            pltpu.VMEM((MATERIALS, r_in, l_in), jnp.float32),
            pltpu.SemaphoreType.DMA((5,)),
        ],
        compiler_params=pltpu.CompilerParams(vmem_limit_bytes=67043328),
        cost_estimate=pl.CostEstimate(
            flops=int(cells * STEPS * 40 + d_in * r_in * l_in * 60),
            transcendentals=int(d_in * r_in * l_in * (MATERIALS + 1)),
            bytes_accessed=int(cells * 4 + (CHANNELS + 1) * r_in * l_in * 4),
        ),
    )(lim, prm, *pieces)


def shards(phase_field, centres, widths, densities, colours):
    depth_cells, row_cells, col_cells = phase_field.shape
    groups = lax.axis_size("gz")
    h = 1.0 / (depth_cells * groups)
    zblock = halo_stage(phase_field, ((0, "gz"),), STEPS)
    zlo, zhi = zblock("lo"), zblock("hi")
    deep = jnp.concatenate([zlo, phase_field, zhi], axis=0)
    plane = halo_stage(deep, ((1, "gx"), (2, "gy")), STEPS)
    rband = jnp.concatenate([plane("hi", "mid"), plane("lo", "mid")], axis=1)
    right = jnp.concatenate([plane("mid", "hi"), plane("hi", "hi"), plane("lo", "hi")], axis=1)
    left = jnp.concatenate([plane("mid", "lo"), plane("hi", "lo"), plane("lo", "lo")], axis=1)
    fill = jnp.zeros(right.shape[:2] + (LANES - col_cells - 2 * STEPS,), jnp.float32)
    cband = jnp.concatenate([right, fill, left], axis=2)

    z_lo = STEPS - lax.axis_index("gz") * depth_cells
    r_lo = -lax.axis_index("gx") * row_cells
    c_lo = -lax.axis_index("gy") * col_cells
    lim = jnp.stack(
        [
            z_lo,
            z_lo + depth_cells * groups,
            r_lo,
            r_lo + row_cells * lax.axis_size("gx"),
            c_lo,
            c_lo + col_cells * lax.axis_size("gy"),
        ]
    ).astype(jnp.int32)
    prm = jnp.concatenate([centres, widths, densities, colours.reshape(-1)]).astype(jnp.float32)

    seg = render_block((phase_field, zlo, zhi, rband, cband), lim, prm, (depth_cells, row_cells, col_cells), h)

    rows_part = row_cells // groups
    parts = seg.reshape(CHANNELS + 1, groups, rows_part, col_cells)
    got = lax.all_to_all(parts, "gz", 1, 1, tiled=True)
    prefix = jnp.zeros((rows_part, col_cells), jnp.float32)
    rad = jnp.zeros((CHANNELS, rows_part, col_cells), jnp.float32)
    for g in range(groups):
        rad = rad + jnp.exp(-h * prefix)[None] * got[:CHANNELS, g]
        prefix = prefix + got[CHANNELS, g]
    alpha = 1.0 - jnp.exp(-h * prefix)
    return jnp.concatenate([rad, alpha[None]], axis=0)


def solution(mesh):
    placed = (P("gz", "gx", "gy"), P(), P(), P(), P())
    return jax.shard_map(
        shards, mesh=mesh, in_specs=placed, out_specs=P(None, ("gx", "gz"), "gy"), check_vma=False
    )
```

```python
import functools
import itertools

import jax
import jax.numpy as jnp
from jax import lax
from jax.experimental import pallas as pl
from jax.experimental.pallas import tpu as pltpu
from jax.sharding import PartitionSpec as P

STEPS = 4
MATERIALS = 4
CHANNELS = 3

KAPPA = 0.5
RATE_DEPTH = 0.3
RATE_PLANE = 0.09
LANES = 256


def pick(cond, a, b):
    if isinstance(cond, bool):
        return a if cond else b
    return jnp.where(cond, a, b)


def axis_moves(axis):
    n = lax.axis_size(axis)
    if n == 1:
        return []
    if n == 2:
        me = lax.axis_index(axis)
        return [([(0, 1), (1, 0)], me == 0, me == 1)]
    up = [(i, i + 1) for i in range(n - 1)]
    down = [(i + 1, i) for i in range(n - 1)]
    return [(up, True, True), (down, False, False)]


def halo_stage(x, dim_axes, width):
    dims = [d for d, _ in dim_axes]
    axes = [a for _, a in dim_axes]
    sizes = [lax.axis_size(a) for a in axes]
    options = [[None] + axis_moves(a) for a in axes]
    blocks = {}
    for combo in itertools.product(*options):
        if all(m is None for m in combo):
            continue
        piece = x
        for d, m in zip(dims, combo):
            if m is not None:
                n_d = piece.shape[d]
                lo = lax.slice_in_dim(piece, 0, width, axis=d)
                hi = lax.slice_in_dim(piece, n_d - width, n_d, axis=d)
                piece = pick(m[1], hi, lo)
        used = [(a, s, m) for a, s, m in zip(axes, sizes, combo) if m is not None]
        pairs = []
        for parts in itertools.product(*[m[0] for _, _, m in used]):
            src = dst = 0
            for (_, s, _), (p, q) in zip(used, parts):
                src, dst = src * s + p, dst * s + q
            pairs.append((src, dst))
        narrow = piece.ndim == 3 and piece.shape[2] == width and piece.shape[1] > width
        if narrow:
            piece = jnp.transpose(piece, (2, 0, 1))
        got = lax.ppermute(piece, tuple(a for a, _, _ in used), pairs)
        if narrow:
            got = jnp.transpose(got, (1, 2, 0))
        landing = [(d, m[2]) for d, m in zip(dims, combo) if m is not None]
        for sides in itertools.product(("lo", "hi"), repeat=len(landing)):
            cond = True
            for (d, land_lo), side in zip(landing, sides):
                this = land_lo if side == "lo" else (not land_lo if isinstance(land_lo, bool) else ~land_lo)
                if isinstance(cond, bool) and isinstance(this, bool):
                    cond = cond and this
                elif isinstance(cond, bool):
                    cond = this if cond else False
                elif isinstance(this, bool):
                    cond = cond if this else False
                else:
                    cond = cond & this
            if cond is False:
                continue
            key = [None] * len(dims)
            for (d, _), side in zip(landing, sides):
                key[dims.index(d)] = side
            key = tuple(k or "mid" for k in key)
            val = got if cond is True else jnp.where(cond, got, 0.0)
            blocks[key] = val if key not in blocks else blocks[key] + val
    blocks[tuple("mid" for _ in dims)] = x

    def block(*key):
        if key in blocks:
            return blocks[key]
        shape = list(x.shape)
        for d, k in zip(dims, key):
            if k != "mid":
                shape[d] = width
        return jnp.zeros(shape, x.dtype)

    return block


def flux(d, rate):
    q = d * (1.0 / KAPPA)
    return rate * d / (1.0 + q * q)


def render_kernel(lim_ref, prm_ref, x_hbm, zlo_hbm, zhi_hbm, rband_hbm, cband_hbm, out_ref, a_ref, b_ref, m_ref, acc_ref, sem,
                  *, interior, h):
    depth, rows, lanes = a_ref.shape
    d_in, r_in, l_in = interior
    halo = STEPS
    copies = [
        pltpu.make_async_copy(x_hbm, b_ref.at[halo:halo + d_in, 0:r_in, 0:l_in], sem.at[0]),
        pltpu.make_async_copy(zlo_hbm, b_ref.at[0:halo, 0:r_in, 0:l_in], sem.at[1]),
        pltpu.make_async_copy(zhi_hbm, b_ref.at[halo + d_in:depth, 0:r_in, 0:l_in], sem.at[2]),
        pltpu.make_async_copy(rband_hbm, b_ref.at[:, r_in:rows, 0:l_in], sem.at[3]),
        pltpu.make_async_copy(cband_hbm, b_ref.at[:, :, l_in:lanes], sem.at[4]),
    ]
    for cp in copies:
        cp.start()

    row = lax.broadcasted_iota(jnp.int32, (rows, lanes), 0)
    lane = lax.broadcasted_iota(jnp.int32, (rows, lanes), 1)
    row_at = jnp.where(row < r_in + halo, row, row - rows)
    lane_at = jnp.where(lane < (l_in + lanes) // 2, lane, lane - lanes)
    ok = (row_at >= lim_ref[2]) & (row_at < lim_ref[3]) & (lane_at >= lim_ref[4]) & (lane_at < lim_ref[5])
    m_ref[...] = jnp.where(ok, 1.0, 0.0).astype(jnp.float32)

    cen = [prm_ref[k] for k in range(MATERIALS)]
    wid = [prm_ref[MATERIALS + k] for k in range(MATERIALS)]
    den = [prm_ref[2 * MATERIALS + k] for k in range(MATERIALS)]
    col = [[prm_ref[3 * MATERIALS + ch * MATERIALS + k] for k in range(MATERIALS)] for ch in range(CHANNELS)]
    out_ref[CHANNELS] = jnp.zeros((r_in, l_in), jnp.float32)
    for k in range(MATERIALS):
        acc_ref[k] = jnp.zeros((r_in, l_in), jnp.float32)

    for cp in copies:
        cp.wait()

    def smooth(src, dst, s):
        z0, z1 = s + 1, depth - 1 - s
        g0 = flux(src[z0] - src[z0 - 1], RATE_DEPTH)

        def body(z, g_prev):
            c = src[z]
            g = flux(src[z + 1] - c, RATE_DEPTH)
            fr = flux(pltpu.roll(c, rows - 1, 0) - c, RATE_PLANE)
            fc = flux(pltpu.roll(c, lanes - 1, 1) - c, RATE_PLANE)
            new = c + (g - g_prev) + (fr - pltpu.roll(fr, 1, 0)) + (fc - pltpu.roll(fc, 1, 1))
            inside = (z >= lim_ref[0]) & (z < lim_ref[1])
            zf = jnp.where(inside, 1.0, 0.0).astype(jnp.float32)
            dst[z] = new * (m_ref[...] * zf)
            return g

        lax.fori_loop(z0, z1, body, g0, unroll=8)

    smooth(b_ref, a_ref, 0)
    smooth(a_ref, b_ref, 1)
    smooth(b_ref, a_ref, 2)

    z0, z1 = halo, halo + d_in
    g0 = flux(a_ref[z0, 0:r_in, 0:l_in] - a_ref[z0 - 1, 0:r_in, 0:l_in], RATE_DEPTH)

    def final(z, g_prev):
        ci = a_ref[z, 0:r_in, 0:l_in]
        g = flux(a_ref[z + 1, 0:r_in, 0:l_in] - ci, RATE_DEPTH)
        c0 = a_ref[z, :, 0:l_in]
        fr = flux(pltpu.roll(c0, rows - 1, 0) - c0, RATE_PLANE)
        cr = a_ref[z, 0:r_in, :]
        fc = flux(pltpu.roll(cr, lanes - 1, 1) - cr, RATE_PLANE)
        v = ci + (g - g_prev) + (fr - pltpu.roll(fr, 1, 0))[0:r_in] + (fc - pltpu.roll(fc, 1, 1))[:, 0:l_in]
        bumps = [den[k] * jnp.exp(-(((v - cen[k]) / wid[k]) ** 2)) for k in range(MATERIALS)]
        ext = bumps[0] + bumps[1] + bumps[2] + bumps[3]
        run = out_ref[CHANNELS]
        through = jnp.exp(-h * run)
        for k in range(MATERIALS):
            acc_ref[k] = acc_ref[k] + through * bumps[k]
        out_ref[CHANNELS] = run + ext
        return g

    lax.fori_loop(z0, z1, final, g0, unroll=8)
    for ch in range(CHANNELS):
        emit = col[ch][0] * acc_ref[0] + col[ch][1] * acc_ref[1] + col[ch][2] * acc_ref[2] + col[ch][3] * acc_ref[3]
        out_ref[ch] = h * emit


def render_block(pieces, lim, prm, interior, h):
    d_in, r_in, l_in = interior
    depth, rows, lanes = d_in + 2 * STEPS, r_in + 2 * STEPS, LANES
    cells = depth * rows * lanes
    kernel = functools.partial(render_kernel, interior=interior, h=h)
    return pl.pallas_call(
        kernel,
        out_shape=jax.ShapeDtypeStruct((CHANNELS + 1, r_in, l_in), jnp.float32),
        in_specs=[pl.BlockSpec(memory_space=pltpu.SMEM)] * 2 + [pl.BlockSpec(memory_space=pl.ANY)] * 5,
        out_specs=pl.BlockSpec(memory_space=pltpu.VMEM),
        scratch_shapes=[
            pltpu.VMEM((depth, rows, lanes), jnp.float32),
            pltpu.VMEM((depth, rows, lanes), jnp.float32),
            pltpu.VMEM((rows, lanes), jnp.float32),
            pltpu.VMEM((MATERIALS, r_in, l_in), jnp.float32),
            pltpu.SemaphoreType.DMA((5,)),
        ],
        compiler_params=pltpu.CompilerParams(vmem_limit_bytes=48 * 1024 * 1024),
        cost_estimate=pl.CostEstimate(
            flops=int(cells * STEPS * 40 + d_in * r_in * l_in * 60),
            transcendentals=int(d_in * r_in * l_in * (MATERIALS + 1)),
            bytes_accessed=int(cells * 4 + (CHANNELS + 1) * r_in * l_in * 4),
        ),
    )(lim, prm, *pieces)


def shards(phase_field, centres, widths, densities, colours):
    depth_cells, row_cells, col_cells = phase_field.shape
    groups = lax.axis_size("gz")
    h = 1.0 / (depth_cells * groups)
    zblock = halo_stage(phase_field, ((0, "gz"),), STEPS)
    zlo, zhi = zblock("lo"), zblock("hi")
    deep = jnp.concatenate([zlo, phase_field, zhi], axis=0)
    plane = halo_stage(deep, ((1, "gx"), (2, "gy")), STEPS)
    rband = jnp.concatenate([plane("hi", "mid"), plane("lo", "mid")], axis=1)
    right = jnp.concatenate([plane("mid", "hi"), plane("hi", "hi"), plane("lo", "hi")], axis=1)
    left = jnp.concatenate([plane("mid", "lo"), plane("hi", "lo"), plane("lo", "lo")], axis=1)
    fill = jnp.zeros(right.shape[:2] + (LANES - col_cells - 2 * STEPS,), jnp.float32)
    cband = jnp.concatenate([right, fill, left], axis=2)

    z_lo = STEPS - lax.axis_index("gz") * depth_cells
    r_lo = -lax.axis_index("gx") * row_cells
    c_lo = -lax.axis_index("gy") * col_cells
    lim = jnp.stack(
        [
            z_lo,
            z_lo + depth_cells * groups,
            r_lo,
            r_lo + row_cells * lax.axis_size("gx"),
            c_lo,
            c_lo + col_cells * lax.axis_size("gy"),
        ]
    ).astype(jnp.int32)
    prm = jnp.concatenate([centres, widths, densities, colours.reshape(-1)]).astype(jnp.float32)

    seg = render_block((phase_field, zlo, zhi, rband, cband), lim, prm, (depth_cells, row_cells, col_cells), h)

    rows_part = row_cells // groups
    parts = seg.reshape(CHANNELS + 1, groups, rows_part, col_cells)
    got = lax.all_to_all(parts, "gz", 1, 1, tiled=True)
    prefix = jnp.zeros((rows_part, col_cells), jnp.float32)
    rad = jnp.zeros((CHANNELS, rows_part, col_cells), jnp.float32)
    for g in range(groups):
        rad = rad + jnp.exp(-h * prefix)[None] * got[:CHANNELS, g]
        prefix = prefix + got[CHANNELS, g]
    alpha = 1.0 - jnp.exp(-h * prefix)
    return jnp.concatenate([rad, alpha[None]], axis=0)


def solution(mesh):
    placed = (P("gz", "gx", "gy"), P(), P(), P(), P())
    return jax.shard_map(
        shards, mesh=mesh, in_specs=placed, out_specs=P(None, ("gx", "gz"), "gy"), check_vma=False
    )
```

```python
import functools
import itertools

import jax
import jax.numpy as jnp
from jax import lax
from jax.experimental import pallas as pl
from jax.experimental.pallas import tpu as pltpu
from jax.sharding import PartitionSpec as P

STEPS = 4
MATERIALS = 4
CHANNELS = 3

KAPPA = 0.5
RATE_DEPTH = 0.3
RATE_PLANE = 0.09
LANES = 256


def pick(cond, a, b):
    if isinstance(cond, bool):
        return a if cond else b
    return jnp.where(cond, a, b)


def axis_moves(axis):
    n = lax.axis_size(axis)
    if n == 1:
        return []
    if n == 2:
        me = lax.axis_index(axis)
        return [([(0, 1), (1, 0)], me == 0, me == 1)]
    up = [(i, i + 1) for i in range(n - 1)]
    down = [(i + 1, i) for i in range(n - 1)]
    return [(up, True, True), (down, False, False)]


def halo_stage(x, dim_axes, width):
    dims = [d for d, _ in dim_axes]
    axes = [a for _, a in dim_axes]
    sizes = [lax.axis_size(a) for a in axes]
    options = [[None] + axis_moves(a) for a in axes]
    blocks = {}
    for combo in itertools.product(*options):
        if all(m is None for m in combo):
            continue
        piece = x
        for d, m in zip(dims, combo):
            if m is not None:
                n_d = piece.shape[d]
                lo = lax.slice_in_dim(piece, 0, width, axis=d)
                hi = lax.slice_in_dim(piece, n_d - width, n_d, axis=d)
                piece = pick(m[1], hi, lo)
        used = [(a, s, m) for a, s, m in zip(axes, sizes, combo) if m is not None]
        pairs = []
        for parts in itertools.product(*[m[0] for _, _, m in used]):
            src = dst = 0
            for (_, s, _), (p, q) in zip(used, parts):
                src, dst = src * s + p, dst * s + q
            pairs.append((src, dst))
        narrow = piece.ndim == 3 and piece.shape[2] == width and piece.shape[1] > width
        if narrow:
            piece = jnp.transpose(piece, (2, 0, 1))
        got = lax.ppermute(piece, tuple(a for a, _, _ in used), pairs)
        if narrow:
            got = jnp.transpose(got, (1, 2, 0))
        landing = [(d, m[2]) for d, m in zip(dims, combo) if m is not None]
        for sides in itertools.product(("lo", "hi"), repeat=len(landing)):
            cond = True
            for (d, land_lo), side in zip(landing, sides):
                this = land_lo if side == "lo" else (not land_lo if isinstance(land_lo, bool) else ~land_lo)
                if isinstance(cond, bool) and isinstance(this, bool):
                    cond = cond and this
                elif isinstance(cond, bool):
                    cond = this if cond else False
                elif isinstance(this, bool):
                    cond = cond if this else False
                else:
                    cond = cond & this
            if cond is False:
                continue
            key = [None] * len(dims)
            for (d, _), side in zip(landing, sides):
                key[dims.index(d)] = side
            key = tuple(k or "mid" for k in key)
            val = got if cond is True else jnp.where(cond, got, 0.0)
            blocks[key] = val if key not in blocks else blocks[key] + val
    blocks[tuple("mid" for _ in dims)] = x

    def block(*key):
        if key in blocks:
            return blocks[key]
        shape = list(x.shape)
        for d, k in zip(dims, key):
            if k != "mid":
                shape[d] = width
        return jnp.zeros(shape, x.dtype)

    return block


def flux(d, rate):
    q = d * (1.0 / KAPPA)
    return rate * d / (1.0 + q * q)


def render_kernel(lim_ref, prm_ref, x_hbm, zlo_hbm, zhi_hbm, rband_hbm, cband_hbm, out_ref, a_ref, b_ref, m_ref, acc_ref, sem,
                  *, interior, h):
    depth, rows, lanes = a_ref.shape
    d_in, r_in, l_in = interior
    halo = STEPS
    copies = [
        pltpu.make_async_copy(x_hbm, b_ref.at[halo:halo + d_in, 0:r_in, 0:l_in], sem.at[0]),
        pltpu.make_async_copy(zlo_hbm, b_ref.at[0:halo, 0:r_in, 0:l_in], sem.at[1]),
        pltpu.make_async_copy(zhi_hbm, b_ref.at[halo + d_in:depth, 0:r_in, 0:l_in], sem.at[2]),
        pltpu.make_async_copy(rband_hbm, b_ref.at[:, r_in:rows, 0:l_in], sem.at[3]),
        pltpu.make_async_copy(cband_hbm, b_ref.at[:, :, l_in:lanes], sem.at[4]),
    ]
    for cp in copies:
        cp.start()

    row = lax.broadcasted_iota(jnp.int32, (rows, lanes), 0)
    lane = lax.broadcasted_iota(jnp.int32, (rows, lanes), 1)
    row_at = jnp.where(row < r_in + halo, row, row - rows)
    lane_at = jnp.where(lane < (l_in + lanes) // 2, lane, lane - lanes)
    ok = (row_at >= lim_ref[2]) & (row_at < lim_ref[3]) & (lane_at >= lim_ref[4]) & (lane_at < lim_ref[5])
    m_ref[0] = jnp.zeros((rows, lanes), jnp.float32)
    m_ref[1] = jnp.where(ok, 1.0, 0.0).astype(jnp.float32)

    cen = [prm_ref[k] for k in range(MATERIALS)]
    wid = [prm_ref[MATERIALS + k] for k in range(MATERIALS)]
    den = [prm_ref[2 * MATERIALS + k] for k in range(MATERIALS)]
    col = [[prm_ref[3 * MATERIALS + ch * MATERIALS + k] for k in range(MATERIALS)] for ch in range(CHANNELS)]
    out_ref[CHANNELS] = jnp.zeros((r_in, l_in), jnp.float32)
    for k in range(MATERIALS):
        acc_ref[k] = jnp.zeros((r_in, l_in), jnp.float32)

    for cp in copies:
        cp.wait()

    def smooth(src, dst, s):
        z0, z1 = s + 1, depth - 1 - s
        g0 = flux(src[z0] - src[z0 - 1], RATE_DEPTH)

        def body(z, g_prev):
            c = src[z]
            g = flux(src[z + 1] - c, RATE_DEPTH)
            fr = flux(pltpu.roll(c, rows - 1, 0) - c, RATE_PLANE)
            fc = flux(pltpu.roll(c, lanes - 1, 1) - c, RATE_PLANE)
            new = c + (g - g_prev) + (fr - pltpu.roll(fr, 1, 0)) + (fc - pltpu.roll(fc, 1, 1))
            inside = ((z >= lim_ref[0]) & (z < lim_ref[1])).astype(jnp.int32)
            dst[z] = new * m_ref[inside]
            return g

        lax.fori_loop(z0, z1, body, g0, unroll=8)

    smooth(b_ref, a_ref, 0)
    smooth(a_ref, b_ref, 1)
    smooth(b_ref, a_ref, 2)

    z0, z1 = halo, halo + d_in
    g0 = flux(a_ref[z0, 0:r_in, 0:l_in] - a_ref[z0 - 1, 0:r_in, 0:l_in], RATE_DEPTH)

    def final(z, g_prev):
        ci = a_ref[z, 0:r_in, 0:l_in]
        g = flux(a_ref[z + 1, 0:r_in, 0:l_in] - ci, RATE_DEPTH)
        c0 = a_ref[z, :, 0:l_in]
        fr = flux(pltpu.roll(c0, rows - 1, 0) - c0, RATE_PLANE)
        cr = a_ref[z, 0:r_in, :]
        fc = flux(pltpu.roll(cr, lanes - 1, 1) - cr, RATE_PLANE)
        v = ci + (g - g_prev) + (fr - pltpu.roll(fr, 1, 0))[0:r_in] + (fc - pltpu.roll(fc, 1, 1))[:, 0:l_in]
        bumps = [den[k] * jnp.exp(-(((v - cen[k]) / wid[k]) ** 2)) for k in range(MATERIALS)]
        ext = bumps[0] + bumps[1] + bumps[2] + bumps[3]
        run = out_ref[CHANNELS]
        through = jnp.exp(-h * run)
        for k in range(MATERIALS):
            acc_ref[k] = acc_ref[k] + through * bumps[k]
        out_ref[CHANNELS] = run + ext
        return g

    lax.fori_loop(z0, z1, final, g0, unroll=4)
    for ch in range(CHANNELS):
        emit = col[ch][0] * acc_ref[0] + col[ch][1] * acc_ref[1] + col[ch][2] * acc_ref[2] + col[ch][3] * acc_ref[3]
        out_ref[ch] = h * emit


def render_block(pieces, lim, prm, interior, h):
    d_in, r_in, l_in = interior
    depth, rows, lanes = d_in + 2 * STEPS, r_in + 2 * STEPS, LANES
    cells = depth * rows * lanes
    kernel = functools.partial(render_kernel, interior=interior, h=h)
    return pl.pallas_call(
        kernel,
        out_shape=jax.ShapeDtypeStruct((CHANNELS + 1, r_in, l_in), jnp.float32),
        in_specs=[pl.BlockSpec(memory_space=pltpu.SMEM)] * 2 + [pl.BlockSpec(memory_space=pl.ANY)] * 5,
        out_specs=pl.BlockSpec(memory_space=pltpu.VMEM),
        scratch_shapes=[
            pltpu.VMEM((depth, rows, lanes), jnp.float32),
            pltpu.VMEM((depth, rows, lanes), jnp.float32),
            pltpu.VMEM((2, rows, lanes), jnp.float32),
            pltpu.VMEM((MATERIALS, r_in, l_in), jnp.float32),
            pltpu.SemaphoreType.DMA((5,)),
        ],
        compiler_params=pltpu.CompilerParams(vmem_limit_bytes=48 * 1024 * 1024),
        cost_estimate=pl.CostEstimate(
            flops=int(cells * STEPS * 40 + d_in * r_in * l_in * 60),
            transcendentals=int(d_in * r_in * l_in * (MATERIALS + 1)),
            bytes_accessed=int(cells * 4 + (CHANNELS + 1) * r_in * l_in * 4),
        ),
    )(lim, prm, *pieces)


def shards(phase_field, centres, widths, densities, colours):
    depth_cells, row_cells, col_cells = phase_field.shape
    groups = lax.axis_size("gz")
    h = 1.0 / (depth_cells * groups)
    zblock = halo_stage(phase_field, ((0, "gz"),), STEPS)
    zlo, zhi = zblock("lo"), zblock("hi")
    deep = jnp.concatenate([zlo, phase_field, zhi], axis=0)
    plane = halo_stage(deep, ((1, "gx"), (2, "gy")), STEPS)
    rband = jnp.concatenate([plane("hi", "mid"), plane("lo", "mid")], axis=1)
    right = jnp.concatenate([plane("mid", "hi"), plane("hi", "hi"), plane("lo", "hi")], axis=1)
    left = jnp.concatenate([plane("mid", "lo"), plane("hi", "lo"), plane("lo", "lo")], axis=1)
    fill = jnp.zeros(right.shape[:2] + (LANES - col_cells - 2 * STEPS,), jnp.float32)
    cband = jnp.concatenate([right, fill, left], axis=2)

    z_lo = STEPS - lax.axis_index("gz") * depth_cells
    r_lo = -lax.axis_index("gx") * row_cells
    c_lo = -lax.axis_index("gy") * col_cells
    lim = jnp.stack(
        [
            z_lo,
            z_lo + depth_cells * groups,
            r_lo,
            r_lo + row_cells * lax.axis_size("gx"),
            c_lo,
            c_lo + col_cells * lax.axis_size("gy"),
        ]
    ).astype(jnp.int32)
    prm = jnp.concatenate([centres, widths, densities, colours.reshape(-1)]).astype(jnp.float32)

    seg = render_block((phase_field, zlo, zhi, rband, cband), lim, prm, (depth_cells, row_cells, col_cells), h)

    rows_part = row_cells // groups
    parts = seg.reshape(CHANNELS + 1, groups, rows_part, col_cells)
    got = lax.all_to_all(parts, "gz", 1, 1, tiled=True)
    prefix = jnp.zeros((rows_part, col_cells), jnp.float32)
    rad = jnp.zeros((CHANNELS, rows_part, col_cells), jnp.float32)
    for g in range(groups):
        rad = rad + jnp.exp(-h * prefix)[None] * got[:CHANNELS, g]
        prefix = prefix + got[CHANNELS, g]
    alpha = 1.0 - jnp.exp(-h * prefix)
    return jnp.concatenate([rad, alpha[None]], axis=0)


def solution(mesh):
    placed = (P("gz", "gx", "gy"), P(), P(), P(), P())
    return jax.shard_map(
        shards, mesh=mesh, in_specs=placed, out_specs=P(None, ("gx", "gz"), "gy"), check_vma=False
    )
```

```python
import functools
import itertools

import jax
import jax.numpy as jnp
from jax import lax
from jax.experimental import pallas as pl
from jax.experimental.pallas import tpu as pltpu
from jax.sharding import PartitionSpec as P

STEPS = 4
MATERIALS = 4
CHANNELS = 3

KAPPA = 0.5
RATE_DEPTH = 0.3
RATE_PLANE = 0.09
LANES = 256


def pick(cond, a, b):
    if isinstance(cond, bool):
        return a if cond else b
    return jnp.where(cond, a, b)


def axis_moves(axis):
    n = lax.axis_size(axis)
    if n == 1:
        return []
    if n == 2:
        me = lax.axis_index(axis)
        return [([(0, 1), (1, 0)], me == 0, me == 1)]
    up = [(i, i + 1) for i in range(n - 1)]
    down = [(i + 1, i) for i in range(n - 1)]
    return [(up, True, True), (down, False, False)]


def halo_stage(x, dim_axes, width):
    dims = [d for d, _ in dim_axes]
    axes = [a for _, a in dim_axes]
    sizes = [lax.axis_size(a) for a in axes]
    options = [[None] + axis_moves(a) for a in axes]
    blocks = {}
    for combo in itertools.product(*options):
        if all(m is None for m in combo):
            continue
        piece = x
        for d, m in zip(dims, combo):
            if m is not None:
                n_d = piece.shape[d]
                lo = lax.slice_in_dim(piece, 0, width, axis=d)
                hi = lax.slice_in_dim(piece, n_d - width, n_d, axis=d)
                piece = pick(m[1], hi, lo)
        used = [(a, s, m) for a, s, m in zip(axes, sizes, combo) if m is not None]
        pairs = []
        for parts in itertools.product(*[m[0] for _, _, m in used]):
            src = dst = 0
            for (_, s, _), (p, q) in zip(used, parts):
                src, dst = src * s + p, dst * s + q
            pairs.append((src, dst))
        narrow = piece.ndim == 3 and piece.shape[2] == width and piece.shape[1] > width
        if narrow:
            piece = jnp.transpose(piece, (2, 0, 1))
        got = lax.ppermute(piece, tuple(a for a, _, _ in used), pairs)
        if narrow:
            got = jnp.transpose(got, (1, 2, 0))
        landing = [(d, m[2]) for d, m in zip(dims, combo) if m is not None]
        for sides in itertools.product(("lo", "hi"), repeat=len(landing)):
            cond = True
            for (d, land_lo), side in zip(landing, sides):
                this = land_lo if side == "lo" else (not land_lo if isinstance(land_lo, bool) else ~land_lo)
                if isinstance(cond, bool) and isinstance(this, bool):
                    cond = cond and this
                elif isinstance(cond, bool):
                    cond = this if cond else False
                elif isinstance(this, bool):
                    cond = cond if this else False
                else:
                    cond = cond & this
            if cond is False:
                continue
            key = [None] * len(dims)
            for (d, _), side in zip(landing, sides):
                key[dims.index(d)] = side
            key = tuple(k or "mid" for k in key)
            val = got if cond is True else jnp.where(cond, got, 0.0)
            blocks[key] = val if key not in blocks else blocks[key] + val
    blocks[tuple("mid" for _ in dims)] = x

    def block(*key):
        if key in blocks:
            return blocks[key]
        shape = list(x.shape)
        for d, k in zip(dims, key):
            if k != "mid":
                shape[d] = width
        return jnp.zeros(shape, x.dtype)

    return block


def flux(d, rate):
    q = d * (1.0 / KAPPA)
    return rate * d / (1.0 + q * q)


def render_kernel(lim_ref, prm_ref, x_hbm, zlo_hbm, zhi_hbm, rband_hbm, cband_hbm, out_ref, a_ref, b_ref, m_ref, acc_ref, sem,
                  *, interior, h):
    depth, rows, lanes = a_ref.shape
    d_in, r_in, l_in = interior
    halo = STEPS
    copies = [
        pltpu.make_async_copy(x_hbm, b_ref.at[halo:halo + d_in, 0:r_in, 0:l_in], sem.at[0]),
        pltpu.make_async_copy(zlo_hbm, b_ref.at[0:halo, 0:r_in, 0:l_in], sem.at[1]),
        pltpu.make_async_copy(zhi_hbm, b_ref.at[halo + d_in:depth, 0:r_in, 0:l_in], sem.at[2]),
        pltpu.make_async_copy(rband_hbm, b_ref.at[:, r_in:rows, 0:l_in], sem.at[3]),
        pltpu.make_async_copy(cband_hbm, b_ref.at[:, :, l_in:lanes], sem.at[4]),
    ]
    for cp in copies:
        cp.start()

    row = lax.broadcasted_iota(jnp.int32, (rows, lanes), 0)
    lane = lax.broadcasted_iota(jnp.int32, (rows, lanes), 1)
    row_at = jnp.where(row < r_in + halo, row, row - rows)
    lane_at = jnp.where(lane < (l_in + lanes) // 2, lane, lane - lanes)
    ok = (row_at >= lim_ref[2]) & (row_at < lim_ref[3]) & (lane_at >= lim_ref[4]) & (lane_at < lim_ref[5])
    m_ref[...] = jnp.where(ok, 1.0, 0.0).astype(jnp.float32)

    cen = [prm_ref[k] for k in range(MATERIALS)]
    wid = [prm_ref[MATERIALS + k] for k in range(MATERIALS)]
    den = [prm_ref[2 * MATERIALS + k] for k in range(MATERIALS)]
    col = [[prm_ref[3 * MATERIALS + ch * MATERIALS + k] for k in range(MATERIALS)] for ch in range(CHANNELS)]
    out_ref[CHANNELS] = jnp.zeros((r_in, l_in), jnp.float32)
    for k in range(MATERIALS):
        acc_ref[k] = jnp.zeros((r_in, l_in), jnp.float32)

    for cp in copies:
        cp.wait()

    def smooth(src, dst, s):
        z0, z1 = s + 1, depth - 1 - s
        g0 = flux(src[z0] - src[z0 - 1], RATE_DEPTH)

        def body(z, g_prev):
            c = src[z]
            g = flux(src[z + 1] - c, RATE_DEPTH)
            fr = flux(pltpu.roll(c, rows - 1, 0) - c, RATE_PLANE)
            fc = flux(pltpu.roll(c, lanes - 1, 1) - c, RATE_PLANE)
            new = c + (g - g_prev) + (fr - pltpu.roll(fr, 1, 0)) + (fc - pltpu.roll(fc, 1, 1))
            inside = (z >= lim_ref[0]) & (z < lim_ref[1])
            zf = jnp.where(inside, 1.0, 0.0).astype(jnp.float32)
            dst[z] = new * (m_ref[...] * zf)
            return g

        lax.fori_loop(z0, z1, body, g0, unroll=16)

    smooth(b_ref, a_ref, 0)
    smooth(a_ref, b_ref, 1)
    smooth(b_ref, a_ref, 2)

    z0, z1 = halo, halo + d_in
    g0 = flux(a_ref[z0, 0:r_in, 0:l_in] - a_ref[z0 - 1, 0:r_in, 0:l_in], RATE_DEPTH)

    def final(z, g_prev):
        ci = a_ref[z, 0:r_in, 0:l_in]
        g = flux(a_ref[z + 1, 0:r_in, 0:l_in] - ci, RATE_DEPTH)
        c0 = a_ref[z, :, 0:l_in]
        fr = flux(pltpu.roll(c0, rows - 1, 0) - c0, RATE_PLANE)
        cr = a_ref[z, 0:r_in, :]
        fc = flux(pltpu.roll(cr, lanes - 1, 1) - cr, RATE_PLANE)
        v = ci + (g - g_prev) + (fr - pltpu.roll(fr, 1, 0))[0:r_in] + (fc - pltpu.roll(fc, 1, 1))[:, 0:l_in]
        bumps = [den[k] * jnp.exp(-(((v - cen[k]) / wid[k]) ** 2)) for k in range(MATERIALS)]
        ext = bumps[0] + bumps[1] + bumps[2] + bumps[3]
        run = out_ref[CHANNELS]
        through = jnp.exp(-h * run)
        for k in range(MATERIALS):
            acc_ref[k] = acc_ref[k] + through * bumps[k]
        out_ref[CHANNELS] = run + ext
        return g

    lax.fori_loop(z0, z1, final, g0, unroll=4)
    for ch in range(CHANNELS):
        emit = col[ch][0] * acc_ref[0] + col[ch][1] * acc_ref[1] + col[ch][2] * acc_ref[2] + col[ch][3] * acc_ref[3]
        out_ref[ch] = h * emit


def render_block(pieces, lim, prm, interior, h):
    d_in, r_in, l_in = interior
    depth, rows, lanes = d_in + 2 * STEPS, r_in + 2 * STEPS, LANES
    cells = depth * rows * lanes
    kernel = functools.partial(render_kernel, interior=interior, h=h)
    return pl.pallas_call(
        kernel,
        out_shape=jax.ShapeDtypeStruct((CHANNELS + 1, r_in, l_in), jnp.float32),
        in_specs=[pl.BlockSpec(memory_space=pltpu.SMEM)] * 2 + [pl.BlockSpec(memory_space=pl.ANY)] * 5,
        out_specs=pl.BlockSpec(memory_space=pltpu.VMEM),
        scratch_shapes=[
            pltpu.VMEM((depth, rows, lanes), jnp.float32),
            pltpu.VMEM((depth, rows, lanes), jnp.float32),
            pltpu.VMEM((rows, lanes), jnp.float32),
            pltpu.VMEM((MATERIALS, r_in, l_in), jnp.float32),
            pltpu.SemaphoreType.DMA((5,)),
        ],
        compiler_params=pltpu.CompilerParams(vmem_limit_bytes=48 * 1024 * 1024),
        cost_estimate=pl.CostEstimate(
            flops=int(cells * STEPS * 40 + d_in * r_in * l_in * 60),
            transcendentals=int(d_in * r_in * l_in * (MATERIALS + 1)),
            bytes_accessed=int(cells * 4 + (CHANNELS + 1) * r_in * l_in * 4),
        ),
    )(lim, prm, *pieces)


def shards(phase_field, centres, widths, densities, colours):
    depth_cells, row_cells, col_cells = phase_field.shape
    groups = lax.axis_size("gz")
    h = 1.0 / (depth_cells * groups)
    zblock = halo_stage(phase_field, ((0, "gz"),), STEPS)
    zlo, zhi = zblock("lo"), zblock("hi")
    deep = jnp.concatenate([zlo, phase_field, zhi], axis=0)
    plane = halo_stage(deep, ((1, "gx"), (2, "gy")), STEPS)
    rband = jnp.concatenate([plane("hi", "mid"), plane("lo", "mid")], axis=1)
    right = jnp.concatenate([plane("mid", "hi"), plane("hi", "hi"), plane("lo", "hi")], axis=1)
    left = jnp.concatenate([plane("mid", "lo"), plane("hi", "lo"), plane("lo", "lo")], axis=1)
    fill = jnp.zeros(right.shape[:2] + (LANES - col_cells - 2 * STEPS,), jnp.float32)
    cband = jnp.concatenate([right, fill, left], axis=2)

    z_lo = STEPS - lax.axis_index("gz") * depth_cells
    r_lo = -lax.axis_index("gx") * row_cells
    c_lo = -lax.axis_index("gy") * col_cells
    lim = jnp.stack(
        [
            z_lo,
            z_lo + depth_cells * groups,
            r_lo,
            r_lo + row_cells * lax.axis_size("gx"),
            c_lo,
            c_lo + col_cells * lax.axis_size("gy"),
        ]
    ).astype(jnp.int32)
    prm = jnp.concatenate([centres, widths, densities, colours.reshape(-1)]).astype(jnp.float32)

    seg = render_block((phase_field, zlo, zhi, rband, cband), lim, prm, (depth_cells, row_cells, col_cells), h)

    rows_part = row_cells // groups
    parts = seg.reshape(CHANNELS + 1, groups, rows_part, col_cells)
    got = lax.all_to_all(parts, "gz", 1, 1, tiled=True)
    prefix = jnp.zeros((rows_part, col_cells), jnp.float32)
    rad = jnp.zeros((CHANNELS, rows_part, col_cells), jnp.float32)
    for g in range(groups):
        rad = rad + jnp.exp(-h * prefix)[None] * got[:CHANNELS, g]
        prefix = prefix + got[CHANNELS, g]
    alpha = 1.0 - jnp.exp(-h * prefix)
    return jnp.concatenate([rad, alpha[None]], axis=0)


def solution(mesh):
    placed = (P("gz", "gx", "gy"), P(), P(), P(), P())
    return jax.shard_map(
        shards, mesh=mesh, in_specs=placed, out_specs=P(None, ("gx", "gz"), "gy"), check_vma=False
    )
```
